32 devices in a mesh: pipe: 2 (over x), ctx: 8 (over z, y), tp: 2 (over core).
Axes of the slice: x: 2, y: 2, z: 4, core: 2. Of those that a mesh axis runs over, the one named last changes fastest.
Arguments:
- fwd_in: bfloat16 [2, 1024, 3, 8192], P('pipe', 'ctx', None, 'tp'), may hold values from -60 to 60
- bwd_in: bfloat16 [2, 1024, 3, 8192], P('pipe', 'ctx', None, 'tp'), may hold values from -60 to 60
- bwd_cot: bfloat16 [2, 1024, 8192], P('pipe', 'ctx', 'tp'), may hold values from -16 to 16
- filter_taps: float32 [2, 2, 4096, 1024], P('pipe', 'tp', 'ctx'), may hold values from -8 to 8
- norm_gain: float32 [2, 8192], P('pipe', 'tp'), may hold values from 0.5 to 2
Outputs:
- next_rows: bfloat16 [2, 1024, 8192], P('pipe', 'ctx', 'tp')
- prev_grads: bfloat16 [2, 1024, 3, 8192], P('pipe', 'ctx', None, 'tp')
- taps_grad: float32 [2, 2, 4096, 1024], P('pipe', 'tp', 'ctx')
The draws below stay inside these ranges and needn't reach their ends.
All inputs are finite; a program needn't handle non-finite values.
Results may differ from the reference program's by a relative error of at most 0.0058.
Values may be sent and summed in bfloat16 or wider, within the bound.
No kernel may reach another device: no remote copies, remote signals or barrier semaphores. Data moves between devices by JAX's collectives and lax.ppermute only.
A program may use at most 128 MiB of HBM per device.

```python
import math
import jax
import jax.numpy as jnp
from jax import lax

D = 8192
TOK_DEV = 128
SECTIONS = 2
TOKENS = 1024
TP_GROUPS = 2
CH_TP = 4096


def spread_rows(key, full_shape, overall, clip_at):
    subkeys = jax.random.split(key, 3)
    token_shape = full_shape[:2] + (1,) * (len(full_shape) - 2)
    channel_shape = (full_shape[0], 1) + full_shape[2:]
    noise_base = jnp.clip(jax.random.normal(subkeys[0], full_shape, jnp.float32), -5.0, 5.0)
    trend_slope = 0.5 * math.log(3.0)
    row_factor = jnp.power(10.0, jax.random.uniform(subkeys[1], token_shape, jnp.float32) - 0.5)
    col_factor = jnp.power(10.0, jax.random.uniform(subkeys[2], channel_shape, jnp.float32) - 0.5)
    position = lax.broadcasted_iota(jnp.float32, channel_shape, len(full_shape) - 1) / full_shape[-1] - 0.5
    trend_factor = jnp.exp(trend_slope * position)
    return jnp.clip(overall * noise_base * row_factor * col_factor * trend_factor, -clip_at, clip_at)


def projection_draw(key):
    full_shape = (SECTIONS, TOKENS, 3, D)
    spread = spread_rows(jax.random.fold_in(key, 1), full_shape, 1.0, 60.0)
    drawn_part = jnp.clip(jax.random.normal(jax.random.fold_in(key, 2), full_shape, jnp.float32), -5.0, 5.0)
    branch_index = lax.broadcasted_iota(jnp.int32, full_shape, 2)
    return jnp.where(branch_index == 0, spread, drawn_part).astype(jnp.bfloat16)


def draw_fwd_in(key, part):
    return projection_draw(jax.random.fold_in(key, 11))


def draw_bwd_in(key, part):
    return projection_draw(jax.random.fold_in(key, 12))


def draw_bwd_cot(key, part):
    return spread_rows(jax.random.fold_in(key, 13), (SECTIONS, TOKENS, D), 0.25, 16.0).astype(jnp.bfloat16)


def draw_filter_taps(key, part):
    full_shape = (SECTIONS, TP_GROUPS, CH_TP, TOKENS)
    subkeys = jax.random.split(jax.random.fold_in(key, 14), 2)
    low_reach = TOK_DEV / 4.0
    noise_part = jnp.clip(jax.random.normal(subkeys[1], full_shape, jnp.float32), -5.0, 5.0)
    high_reach = 4.0 * TOKENS
    reach_pick = jax.random.uniform(subkeys[0], (SECTIONS, TP_GROUPS, CH_TP, 1), jnp.float32)
    reach_length = jnp.exp(math.log(low_reach) + reach_pick * (math.log(high_reach) - math.log(low_reach)))
    lag_index = lax.broadcasted_iota(jnp.float32, full_shape, 3)
    envelope = jnp.exp(-lag_index / reach_length)
    amplitude = jnp.sqrt(2.0 / jnp.minimum(reach_length, 1.0 * TOKENS))
    return jnp.clip(amplitude * envelope * noise_part, -8.0, 8.0)


def block_levels(stream_key, extent, cuts, smallest, top_value):
    def one(dim, blocks):
        heights = jax.random.uniform(jax.random.fold_in(jax.random.fold_in(stream_key, 6), dim), (blocks,), jnp.float32, smallest / len(cuts), top_value / len(cuts))
        return jnp.repeat(jnp.exp(heights), extent[dim] // blocks).reshape((-1,) + (1,) * (len(extent) - dim - 1))

    loudness = one(*cuts[0])
    for cut in cuts[1:]:
        loudness = loudness * one(*cut)
    return loudness


def setup_inputs(seed: int = 0) -> dict:
    splits = jax.random.split(jax.random.key(seed), 6)
    fwd_in = draw_fwd_in(jax.random.fold_in(splits[5], 71), 0)
    bwd_in = draw_bwd_in(jax.random.fold_in(splits[5], 71), 0)
    bwd_cot = draw_bwd_cot(jax.random.fold_in(splits[5], 71), 0)
    filter_taps = draw_filter_taps(jax.random.fold_in(splits[5], 71), 0)
    norm_gain = jnp.clip(jnp.exp(math.log(2.0) - 1.3862944 * jax.random.uniform(splits[4], (SECTIONS, D), jnp.float32) ** block_levels(splits[4], (SECTIONS, D), ((0, 2), (1, 2)), -0.2, 0.2)), 0.5, 2.0)
    return {"fwd_in": fwd_in, "bwd_in": bwd_in, "bwd_cot": bwd_cot, "filter_taps": filter_taps, "norm_gain": norm_gain}


epsilon = 1e-06

def causal_conv(signal, filter_row):
    length_now = signal.shape[-1]
    product = jnp.fft.rfft(signal, n=2 * length_now) * jnp.fft.rfft(filter_row, n=2 * length_now)
    return jnp.fft.irfft(product, n=2 * length_now)[..., :length_now]

def correlate(leading, trailing):
    length_now = leading.shape[-1]
    product = jnp.fft.rfft(leading, n=2 * length_now) * jnp.conj(jnp.fft.rfft(trailing, n=2 * length_now))
    return jnp.fft.irfft(product, n=2 * length_now)[..., :length_now]

def blockwise(operation, first_part, second_part):
    stacked = (first_part.reshape(TP_GROUPS, CH_TP, TOKENS), second_part.reshape(TP_GROUPS, CH_TP, TOKENS))
    result = lax.map(lambda members: operation(members[0], members[1]), stacked)
    return result.reshape(D, TOKENS)

def one_section(section_args):
    fwd_rows, bwd_rows, cotangent, local_taps, gain_row = section_args
    taps_flat = local_taps.reshape(D, TOKENS)
    forward_mix = (fwd_rows[:, 1].astype(jnp.float32) * fwd_rows[:, 2].astype(jnp.float32)).astype(jnp.bfloat16)
    forward_conv = jnp.transpose(blockwise(causal_conv, jnp.transpose(forward_mix).astype(jnp.float32), taps_flat)).astype(jnp.bfloat16)
    forward_y = fwd_rows[:, 0].astype(jnp.float32) * forward_conv.astype(jnp.float32)
    forward_scale = lax.rsqrt(lax.optimization_barrier(jnp.mean(forward_y * forward_y, axis=1, keepdims=True)) + epsilon)
    forward_out = (forward_y * forward_scale * gain_row[None, :]).astype(jnp.bfloat16)
    backward_mix = (bwd_rows[:, 1].astype(jnp.float32) * bwd_rows[:, 2].astype(jnp.float32)).astype(jnp.bfloat16)
    mix_columns = jnp.transpose(backward_mix).astype(jnp.float32)
    backward_conv = jnp.transpose(blockwise(causal_conv, mix_columns, taps_flat)).astype(jnp.bfloat16)
    backward_q = bwd_rows[:, 0].astype(jnp.float32)
    conv_value = backward_conv.astype(jnp.float32)
    backward_y = backward_q * conv_value
    backward_scale = lax.rsqrt(lax.optimization_barrier(jnp.mean(backward_y * backward_y, axis=1, keepdims=True)) + epsilon)
    weighted = cotangent.astype(jnp.float32) * gain_row[None, :]
    normed = backward_y * backward_scale
    average = lax.optimization_barrier(jnp.mean(weighted * normed, axis=1, keepdims=True))
    grad_y = backward_scale * (weighted - normed * average)
    grad_z = (grad_y * backward_q).astype(jnp.bfloat16)
    grad_columns = jnp.transpose(grad_z).astype(jnp.float32)
    grad_mix = jnp.transpose(blockwise(correlate, grad_columns, taps_flat)).astype(jnp.bfloat16)
    filt_step = blockwise(correlate, grad_columns, mix_columns)
    mix_value = grad_mix.astype(jnp.float32)
    section_grads = jnp.stack([grad_y * conv_value, mix_value * bwd_rows[:, 2].astype(jnp.float32), mix_value * bwd_rows[:, 1].astype(jnp.float32)], axis=1).astype(jnp.bfloat16)
    return (forward_out, section_grads, filt_step.reshape(TP_GROUPS, CH_TP, TOKENS))

def reference(fwd_in, bwd_in, bwd_cot, filter_taps, norm_gain):
    forward_out, section_grads, taps_grad = lax.map(one_section, (fwd_in, bwd_in, bwd_cot, filter_taps, norm_gain))
    return (jnp.roll(forward_out, 1, axis=0), jnp.roll(section_grads, -1, axis=0), taps_grad)
```

```python
import math

import jax
import jax.numpy as jnp
from jax import lax
from jax.sharding import PartitionSpec as P

epsilon = 1e-06
highest = lax.Precision.HIGHEST


def from_partner(block, axis, bit):
    count = lax.axis_size(axis)
    route = []
    for low in range(count):
        high = low | 1 << bit
        if high != low and high < count:
            route += [(low, high), (high, low)]
    return lax.ppermute(block, axis, route)


def unit_table(count_out, count_in, period):
    product = lax.broadcasted_iota(jnp.int32, (count_out, count_in), 0) * lax.broadcasted_iota(
        jnp.int32, (count_out, count_in), 1
    )
    phase_angle = (product % period).astype(jnp.float32) * (-2.0 * math.pi / period)
    return (jnp.cos(phase_angle), jnp.sin(phase_angle))


def dft_tables(padded):
    blocks = padded // 128
    cos_high, sin_high = unit_table(blocks, blocks, blocks)
    cos_low, sin_low = unit_table(128, 128, 128)
    cos_twist, sin_twist = unit_table(blocks, 128, padded)
    return (cos_high, sin_high, cos_low, sin_low, cos_twist, sin_twist)


def spectrum(signal, tables):
    cos_high, sin_high, cos_low, sin_low, cos_twist, sin_twist = tables
    channels = signal.shape[0]
    half_blocks = signal.shape[1] // 128
    folded = signal.reshape(channels, half_blocks, 128)
    first_re = jnp.einsum("can,ak->ckn", folded, cos_high[:half_blocks], precision=highest)
    first_im = jnp.einsum("can,ak->ckn", folded, sin_high[:half_blocks], precision=highest)
    turned_re = first_re * cos_twist - first_im * sin_twist
    turned_im = first_re * sin_twist + first_im * cos_twist
    spec_re = jnp.einsum("ckn,nj->ckj", turned_re, cos_low, precision=highest) - jnp.einsum(
        "ckn,nj->ckj", turned_im, sin_low, precision=highest
    )
    spec_im = jnp.einsum("ckn,nj->ckj", turned_re, sin_low, precision=highest) + jnp.einsum(
        "ckn,nj->ckj", turned_im, cos_low, precision=highest
    )
    return (spec_re, spec_im)


def signal_of(spec_re, spec_im, tables):
    cos_high, sin_high, cos_low, sin_low, cos_twist, sin_twist = tables
    channels = spec_re.shape[0]
    blocks = spec_re.shape[1]
    half_blocks = blocks // 2
    mid_re = jnp.einsum("ckj,jn->ckn", spec_re, cos_low, precision=highest) + jnp.einsum(
        "ckj,jn->ckn", spec_im, sin_low, precision=highest
    )
    mid_im = jnp.einsum("ckj,jn->ckn", spec_im, cos_low, precision=highest) - jnp.einsum(
        "ckj,jn->ckn", spec_re, sin_low, precision=highest
    )
    back_re = mid_re * cos_twist + mid_im * sin_twist
    back_im = mid_im * cos_twist - mid_re * sin_twist
    values = jnp.einsum(
        "ak,ckn->can", cos_high[:half_blocks], back_re, precision=highest
    ) + jnp.einsum("ak,ckn->can", sin_high[:half_blocks], back_im, precision=highest)
    return values.reshape(channels, half_blocks * 128) / (blocks * 128)


def spec_product(a_re, a_im, b_re, b_im):
    return (a_re * b_re - a_im * b_im, a_re * b_im + a_im * b_re)


def spec_against(a_re, a_im, b_re, b_im):
    return (a_re * b_re + a_im * b_im, a_im * b_re - a_re * b_im)


def split_bf16(values):
    high = lax.reduce_precision(values, exponent_bits=8, mantissa_bits=7)
    return (high.astype(jnp.bfloat16), (values - high).astype(jnp.bfloat16))


def unit_angles(count_rows, count_cols, stride, padded):
    rows = lax.broadcasted_iota(jnp.int32, (count_rows, count_cols), 0) * stride
    cols = lax.broadcasted_iota(jnp.int32, (count_rows, count_cols), 1)
    angle = ((rows * cols) % padded).astype(jnp.float32) * (2.0 * math.pi / padded)
    return (jnp.cos(angle), jnp.sin(angle))


def real_dft_table(length):
    padded = 2 * length
    inner = 1 << (length.bit_length() // 2)
    if length % inner:
        inner = 1
    outer = length // inner
    cos_outer, sin_outer = unit_angles(outer, length, inner, padded)
    cos_inner, sin_inner = unit_angles(inner, length, 1, padded)
    cos_full = (cos_outer[:, None] * cos_inner[None] - sin_outer[:, None] * sin_inner[None]).reshape(
        length, length
    )
    sin_full = (sin_outer[:, None] * cos_inner[None] + cos_outer[:, None] * sin_inner[None]).reshape(
        length, length
    )
    rows = lax.broadcasted_iota(jnp.int32, (length, length), 0)
    cols = lax.broadcasted_iota(jnp.int32, (length, length), 1)
    alternating = jnp.where(rows % 2 == 0, 1.0, -1.0).astype(jnp.float32)
    sin_part = jnp.where(cols == 0, alternating, -sin_full)
    table = jnp.concatenate([cos_full, sin_part], axis=1)
    return split_bf16(table)


def dot_tf(table, signal):
    return lax.dot_general(
        table, signal, (((0,), (0,)), ((), ())), preferred_element_type=jnp.float32
    )


def dot_tt(table, spec):
    return lax.dot_general(
        table, spec, (((1,), (0,)), ((), ())), preferred_element_type=jnp.float32
    )


def dense_spectrum_exact(rows_bf16, table):
    table_hi, table_lo = table
    return dot_tf(table_hi, rows_bf16) + dot_tf(table_lo, rows_bf16)


def dense_signal(spec, table):
    table_hi, table_lo = table
    spec_hi, spec_lo = split_bf16(spec)
    return dot_tt(table_hi, spec_hi) + (dot_tt(table_lo, spec_hi) + dot_tt(table_hi, spec_lo))


def dense_taps_spectrum(taps, table):
    table_hi, table_lo = table
    taps_hi, taps_lo = split_bf16(taps)
    dims = (((0,), (1,)), ((), ()))
    part = lambda a, b: lax.dot_general(a, b, dims, preferred_element_type=jnp.float32)
    return part(table_hi, taps_hi) + (part(table_lo, taps_hi) + part(table_hi, taps_lo))


def spectral_weights(length):
    index = lax.broadcasted_iota(jnp.int32, (2 * length, 1), 0)
    edge = (index == 0) | (index == length)
    return jnp.where(edge, 1.0, 2.0).astype(jnp.float32) / (2 * length)


def dense_multiply(a, b, conjugate):
    length = a.shape[0] // 2
    a_re, a_im = a[:length], a[length:]
    b_re, b_im = b[:length], b[length:]
    first = lax.broadcasted_iota(jnp.int32, (length, 1), 0) == 0
    if conjugate:
        re = a_re * b_re + a_im * b_im
        im = a_im * b_re - a_re * b_im
    else:
        re = a_re * b_re - a_im * b_im
        im = a_re * b_im + a_im * b_re
    re = jnp.where(first, a_re * b_re, re)
    im = jnp.where(first, a_im * b_im, im)
    return jnp.concatenate([re, im], axis=0)


def dense_fits(length):
    return 4 * length * length * 2 <= 16 * 1024 * 1024


def on_device_factored(fwd_in, bwd_in, bwd_cot, filter_taps, norm_gain):
    model_width = norm_gain.shape[1] * lax.axis_size("tp")
    local_taps = filter_taps[0, 0]
    tables = dft_tables(2 * local_taps.shape[1])
    tap_re, tap_im = spectrum(local_taps, tables)
    gain_row = norm_gain[0]
    forward_rows = fwd_in[0]
    backward_rows = bwd_in[0]

    def featurize(proj_rows):
        return (proj_rows[:, 1].astype(jnp.float32) * proj_rows[:, 2].astype(jnp.float32)).astype(
            jnp.bfloat16
        )

    def convolve(columns):
        sig_re, sig_im = spectrum(columns.astype(jnp.float32), tables)
        prod_re, prod_im = spec_product(sig_re, sig_im, tap_re, tap_im)
        return (signal_of(prod_re, prod_im, tables).astype(jnp.bfloat16), (sig_re, sig_im))

    def relayout(mixed_rows):
        columns = lax.all_to_all(
            jnp.transpose(mixed_rows), "ctx", split_axis=0, concat_axis=1, tiled=True
        )
        result, kept_spec = convolve(columns)
        return (
            jnp.transpose(lax.all_to_all(result, "ctx", split_axis=1, concat_axis=0, tiled=True)),
            kept_spec,
        )

    def row_total(values):
        return lax.psum(jnp.sum(values, axis=1), "tp")

    forward_mix = featurize(forward_rows)
    backward_mix = featurize(backward_rows)
    forward_z = relayout(forward_mix)[0]
    backward_z, backward_spec = relayout(backward_mix)
    forward_y = forward_rows[:, 0].astype(jnp.float32) * forward_z.astype(jnp.float32)
    backward_q = backward_rows[:, 0].astype(jnp.float32)
    conv_value = backward_z.astype(jnp.float32)
    backward_y = backward_q * conv_value
    weighted = bwd_cot[0].astype(jnp.float32) * gain_row
    forward_scale = lax.rsqrt(row_total(forward_y * forward_y) / model_width + epsilon)[:, None]
    backward_scale = lax.rsqrt(row_total(backward_y * backward_y) / model_width + epsilon)[:, None]
    normed = backward_y * backward_scale
    average = (row_total(weighted * normed) / model_width)[:, None]
    forward_out = (forward_y * forward_scale * gain_row).astype(jnp.bfloat16)
    grad_y = backward_scale * (weighted - normed * average)
    grad_z = (grad_y * backward_q).astype(jnp.bfloat16)
    grad_cols = lax.all_to_all(
        jnp.transpose(grad_z), "ctx", split_axis=0, concat_axis=1, tiled=True
    )
    grad_re, grad_im = spectrum(grad_cols.astype(jnp.float32), tables)
    input_re, input_im = spec_against(grad_re, grad_im, tap_re, tap_im)
    grad_mix_cols = signal_of(input_re, input_im, tables).astype(jnp.bfloat16)
    taps_re, taps_im = spec_against(grad_re, grad_im, backward_spec[0], backward_spec[1])
    filt_step = signal_of(taps_re, taps_im, tables)
    grad_mix = jnp.transpose(
        lax.all_to_all(grad_mix_cols, "ctx", split_axis=1, concat_axis=0, tiled=True)
    ).astype(jnp.float32)
    section_grads = jnp.stack(
        [
            grad_y * conv_value,
            grad_mix * backward_rows[:, 2].astype(jnp.float32),
            grad_mix * backward_rows[:, 1].astype(jnp.float32),
        ],
        axis=1,
    ).astype(jnp.bfloat16)
    section_grads, filt_step = (section_grads, filt_step)
    sent_rows, sent_grads = from_partner((forward_out, section_grads), "pipe", 0)
    return (sent_rows[None], sent_grads[None], filt_step[None, None])


def on_device(fwd_in, bwd_in, bwd_cot, filter_taps, norm_gain):
    length = filter_taps.shape[3]
    if not dense_fits(length):
        return on_device_factored(fwd_in, bwd_in, bwd_cot, filter_taps, norm_gain)
    model_width = norm_gain.shape[1] * lax.axis_size("tp")
    table = real_dft_table(length)
    weights = spectral_weights(length)
    tap_spec = dense_taps_spectrum(filter_taps[0, 0], table)
    tap_scaled = tap_spec * weights
    gain_row = norm_gain[0]
    forward_rows = fwd_in[0]
    backward_rows = bwd_in[0]

    def featurize(proj_rows):
        return (proj_rows[:, 1].astype(jnp.float32) * proj_rows[:, 2].astype(jnp.float32)).astype(
            jnp.bfloat16
        )

    def to_columns(rows):
        return lax.all_to_all(rows, "ctx", split_axis=1, concat_axis=0, tiled=True)

    def to_rows(columns):
        return lax.all_to_all(columns, "ctx", split_axis=0, concat_axis=1, tiled=True)

    def row_total(values):
        return lax.psum(jnp.sum(values, axis=1), "tp")

    forward_cols = to_columns(featurize(forward_rows))
    backward_cols = to_columns(featurize(backward_rows))
    forward_spec = dense_spectrum_exact(forward_cols, table)
    forward_z = to_rows(
        dense_signal(dense_multiply(forward_spec, tap_scaled, False), table).astype(jnp.bfloat16)
    )
    backward_spec = dense_spectrum_exact(backward_cols, table)
    backward_z = to_rows(
        dense_signal(dense_multiply(backward_spec, tap_scaled, False), table).astype(jnp.bfloat16)
    )
    forward_y = forward_rows[:, 0].astype(jnp.float32) * forward_z.astype(jnp.float32)
    forward_scale = lax.rsqrt(row_total(forward_y * forward_y) / model_width + epsilon)[:, None]
    forward_out = (forward_y * forward_scale * gain_row).astype(jnp.bfloat16)
    sent_rows = from_partner(forward_out, "pipe", 0)
    backward_q = backward_rows[:, 0].astype(jnp.float32)
    conv_value = backward_z.astype(jnp.float32)
    backward_y = backward_q * conv_value
    weighted = bwd_cot[0].astype(jnp.float32) * gain_row
    backward_scale = lax.rsqrt(row_total(backward_y * backward_y) / model_width + epsilon)[:, None]
    normed = backward_y * backward_scale
    average = (row_total(weighted * normed) / model_width)[:, None]
    grad_y = backward_scale * (weighted - normed * average)
    grad_z = (grad_y * backward_q).astype(jnp.bfloat16)
    sent_first = from_partner((grad_y * conv_value).astype(jnp.bfloat16), "pipe", 0)
    grad_spec = dense_spectrum_exact(to_columns(grad_z), table) * weights
    grad_mix_cols = dense_signal(dense_multiply(grad_spec, tap_spec, True), table).astype(
        jnp.bfloat16
    )
    taps_prod = dense_multiply(grad_spec, backward_spec, True)
    taps_hi, taps_lo = split_bf16(taps_prod)
    table_hi, table_lo = table
    dims = (((0,), (1,)), ((), ()))
    part = lambda a, b: lax.dot_general(a, b, dims, preferred_element_type=jnp.float32)
    filt_step = part(taps_hi, table_hi) + (part(taps_hi, table_lo) + part(taps_lo, table_hi))
    grad_mix = to_rows(grad_mix_cols).astype(jnp.float32)
    rest = jnp.stack(
        [
            grad_mix * backward_rows[:, 2].astype(jnp.float32),
            grad_mix * backward_rows[:, 1].astype(jnp.float32),
        ],
        axis=1,
    ).astype(jnp.bfloat16)
    sent_rest = from_partner(rest, "pipe", 0)
    sent_grads = jnp.concatenate([sent_first[:, None], sent_rest], axis=1)
    return (sent_rows[None], sent_grads[None], filt_step[None, None])


def solution(mesh):
    return jax.shard_map(
        on_device,
        mesh=mesh,
        in_specs=(
            P("pipe", "ctx", None, "tp"),
            P("pipe", "ctx", None, "tp"),
            P("pipe", "ctx", "tp"),
            P("pipe", "tp", "ctx", None),
            P("pipe", "tp"),
        ),
        out_specs=(
            P("pipe", "ctx", "tp"),
            P("pipe", "ctx", None, "tp"),
            P("pipe", "tp", "ctx", None),
        ),
        check_vma=False,
    )
```

```python
import math

import jax
import jax.numpy as jnp
from jax import lax
from jax.sharding import PartitionSpec as P

epsilon = 1e-06
highest = lax.Precision.HIGHEST


def from_partner(block, axis, bit):
    count = lax.axis_size(axis)
    route = []
    for low in range(count):
        high = low | 1 << bit
        if high != low and high < count:
            route += [(low, high), (high, low)]
    return lax.ppermute(block, axis, route)


def unit_table(count_out, count_in, period):
    product = lax.broadcasted_iota(jnp.int32, (count_out, count_in), 0) * lax.broadcasted_iota(
        jnp.int32, (count_out, count_in), 1
    )
    phase_angle = (product % period).astype(jnp.float32) * (-2.0 * math.pi / period)
    return (jnp.cos(phase_angle), jnp.sin(phase_angle))


def dft_tables(padded):
    blocks = padded // 128
    cos_high, sin_high = unit_table(blocks, blocks, blocks)
    cos_low, sin_low = unit_table(128, 128, 128)
    cos_twist, sin_twist = unit_table(blocks, 128, padded)
    return (cos_high, sin_high, cos_low, sin_low, cos_twist, sin_twist)


def spectrum(signal, tables):
    cos_high, sin_high, cos_low, sin_low, cos_twist, sin_twist = tables
    channels = signal.shape[0]
    half_blocks = signal.shape[1] // 128
    folded = signal.reshape(channels, half_blocks, 128)
    first_re = jnp.einsum("can,ak->ckn", folded, cos_high[:half_blocks], precision=highest)
    first_im = jnp.einsum("can,ak->ckn", folded, sin_high[:half_blocks], precision=highest)
    turned_re = first_re * cos_twist - first_im * sin_twist
    turned_im = first_re * sin_twist + first_im * cos_twist
    spec_re = jnp.einsum("ckn,nj->ckj", turned_re, cos_low, precision=highest) - jnp.einsum(
        "ckn,nj->ckj", turned_im, sin_low, precision=highest
    )
    spec_im = jnp.einsum("ckn,nj->ckj", turned_re, sin_low, precision=highest) + jnp.einsum(
        "ckn,nj->ckj", turned_im, cos_low, precision=highest
    )
    return (spec_re, spec_im)


def signal_of(spec_re, spec_im, tables):
    cos_high, sin_high, cos_low, sin_low, cos_twist, sin_twist = tables
    channels = spec_re.shape[0]
    blocks = spec_re.shape[1]
    half_blocks = blocks // 2
    mid_re = jnp.einsum("ckj,jn->ckn", spec_re, cos_low, precision=highest) + jnp.einsum(
        "ckj,jn->ckn", spec_im, sin_low, precision=highest
    )
    mid_im = jnp.einsum("ckj,jn->ckn", spec_im, cos_low, precision=highest) - jnp.einsum(
        "ckj,jn->ckn", spec_re, sin_low, precision=highest
    )
    back_re = mid_re * cos_twist + mid_im * sin_twist
    back_im = mid_im * cos_twist - mid_re * sin_twist
    values = jnp.einsum(
        "ak,ckn->can", cos_high[:half_blocks], back_re, precision=highest
    ) + jnp.einsum("ak,ckn->can", sin_high[:half_blocks], back_im, precision=highest)
    return values.reshape(channels, half_blocks * 128) / (blocks * 128)


def spec_product(a_re, a_im, b_re, b_im):
    return (a_re * b_re - a_im * b_im, a_re * b_im + a_im * b_re)


def spec_against(a_re, a_im, b_re, b_im):
    return (a_re * b_re + a_im * b_im, a_im * b_re - a_re * b_im)


def split_bf16(values):
    high = lax.reduce_precision(values, exponent_bits=8, mantissa_bits=7)
    return (high.astype(jnp.bfloat16), (values - high).astype(jnp.bfloat16))


def unit_angles(count_rows, count_cols, stride, padded):
    rows = lax.broadcasted_iota(jnp.int32, (count_rows, count_cols), 0) * stride
    cols = lax.broadcasted_iota(jnp.int32, (count_rows, count_cols), 1)
    angle = ((rows * cols) % padded).astype(jnp.float32) * (2.0 * math.pi / padded)
    return (jnp.cos(angle), jnp.sin(angle))


def real_dft_table(length):
    padded = 2 * length
    inner = 1 << (length.bit_length() // 2)
    if length % inner:
        inner = 1
    outer = length // inner
    cos_outer, sin_outer = unit_angles(outer, length, inner, padded)
    cos_inner, sin_inner = unit_angles(inner, length, 1, padded)
    cos_full = (cos_outer[:, None] * cos_inner[None] - sin_outer[:, None] * sin_inner[None]).reshape(
        length, length
    )
    sin_full = (sin_outer[:, None] * cos_inner[None] + cos_outer[:, None] * sin_inner[None]).reshape(
        length, length
    )
    rows = lax.broadcasted_iota(jnp.int32, (length, length), 0)
    cols = lax.broadcasted_iota(jnp.int32, (length, length), 1)
    alternating = jnp.where(rows % 2 == 0, 1.0, -1.0).astype(jnp.float32)
    sin_part = jnp.where(cols == 0, alternating, -sin_full)
    table = jnp.concatenate([cos_full, sin_part], axis=1)
    cos_outer_t, sin_outer_t = cos_outer.T[:, :, None], sin_outer.T[:, :, None]
    cos_inner_t, sin_inner_t = cos_inner.T[:, None], sin_inner.T[:, None]
    cos_t = (cos_outer_t * cos_inner_t - sin_outer_t * sin_inner_t).reshape(length, length)
    sin_t = (sin_outer_t * cos_inner_t + cos_outer_t * sin_inner_t).reshape(length, length)
    alternating_t = jnp.where(cols % 2 == 0, 1.0, -1.0).astype(jnp.float32)
    sin_part_t = jnp.where(rows == 0, alternating_t, -sin_t)
    table_t = jnp.concatenate([cos_t, sin_part_t], axis=0)
    return split_bf16(table), split_bf16(table_t)


def dot_tf(table, signal):
    return lax.dot_general(
        table, signal, (((0,), (0,)), ((), ())), preferred_element_type=jnp.float32
    )


def dot_tt(table, spec):
    return lax.dot_general(
        table, spec, (((1,), (0,)), ((), ())), preferred_element_type=jnp.float32
    )


def dense_spectrum_exact(rows_bf16, table_t):
    table_hi, table_lo = table_t
    return dot_tt(table_hi, rows_bf16) + dot_tt(table_lo, rows_bf16)


def dense_signal(spec, table):
    table_hi, table_lo = table
    spec_hi, spec_lo = split_bf16(spec)
    return dot_tt(table_hi, spec_hi) + (dot_tt(table_lo, spec_hi) + dot_tt(table_hi, spec_lo))


def dense_taps_spectrum(taps, table_t):
    table_hi, table_lo = table_t
    taps_hi, taps_lo = split_bf16(taps)
    dims = (((1,), (1,)), ((), ()))
    part = lambda a, b: lax.dot_general(a, b, dims, preferred_element_type=jnp.float32)
    return part(table_hi, taps_hi) + (part(table_lo, taps_hi) + part(table_hi, taps_lo))


def spectral_weights(length):
    index = lax.broadcasted_iota(jnp.int32, (2 * length, 1), 0)
    edge = (index == 0) | (index == length)
    return jnp.where(edge, 1.0, 2.0).astype(jnp.float32) / (2 * length)


def dense_multiply(a, b, conjugate):
    length = a.shape[0] // 2
    a_re, a_im = a[:length], a[length:]
    b_re, b_im = b[:length], b[length:]
    first = lax.broadcasted_iota(jnp.int32, (length, 1), 0) == 0
    if conjugate:
        re = a_re * b_re + a_im * b_im
        im = a_im * b_re - a_re * b_im
    else:
        re = a_re * b_re - a_im * b_im
        im = a_re * b_im + a_im * b_re
    re = jnp.where(first, a_re * b_re, re)
    im = jnp.where(first, a_im * b_im, im)
    return jnp.concatenate([re, im], axis=0)


def dense_fits(length):
    return 4 * length * length * 2 <= 16 * 1024 * 1024


def on_device_factored(fwd_in, bwd_in, bwd_cot, filter_taps, norm_gain):
    model_width = norm_gain.shape[1] * lax.axis_size("tp")
    local_taps = filter_taps[0, 0]
    tables = dft_tables(2 * local_taps.shape[1])
    tap_re, tap_im = spectrum(local_taps, tables)
    gain_row = norm_gain[0]
    forward_rows = fwd_in[0]
    backward_rows = bwd_in[0]

    def featurize(proj_rows):
        return (proj_rows[:, 1].astype(jnp.float32) * proj_rows[:, 2].astype(jnp.float32)).astype(
            jnp.bfloat16
        )

    def convolve(columns):
        sig_re, sig_im = spectrum(columns.astype(jnp.float32), tables)
        prod_re, prod_im = spec_product(sig_re, sig_im, tap_re, tap_im)
        return (signal_of(prod_re, prod_im, tables).astype(jnp.bfloat16), (sig_re, sig_im))

    def relayout(mixed_rows):
        columns = lax.all_to_all(
            jnp.transpose(mixed_rows), "ctx", split_axis=0, concat_axis=1, tiled=True
        )
        result, kept_spec = convolve(columns)
        return (
            jnp.transpose(lax.all_to_all(result, "ctx", split_axis=1, concat_axis=0, tiled=True)),
            kept_spec,
        )

    def row_total(values):
        return lax.psum(jnp.sum(values, axis=1), "tp")

    forward_mix = featurize(forward_rows)
    backward_mix = featurize(backward_rows)
    forward_z = relayout(forward_mix)[0]
    backward_z, backward_spec = relayout(backward_mix)
    forward_y = forward_rows[:, 0].astype(jnp.float32) * forward_z.astype(jnp.float32)
    backward_q = backward_rows[:, 0].astype(jnp.float32)
    conv_value = backward_z.astype(jnp.float32)
    backward_y = backward_q * conv_value
    weighted = bwd_cot[0].astype(jnp.float32) * gain_row
    forward_scale = lax.rsqrt(row_total(forward_y * forward_y) / model_width + epsilon)[:, None]
    backward_scale = lax.rsqrt(row_total(backward_y * backward_y) / model_width + epsilon)[:, None]
    normed = backward_y * backward_scale
    average = (row_total(weighted * normed) / model_width)[:, None]
    forward_out = (forward_y * forward_scale * gain_row).astype(jnp.bfloat16)
    grad_y = backward_scale * (weighted - normed * average)
    grad_z = (grad_y * backward_q).astype(jnp.bfloat16)
    grad_cols = lax.all_to_all(
        jnp.transpose(grad_z), "ctx", split_axis=0, concat_axis=1, tiled=True
    )
    grad_re, grad_im = spectrum(grad_cols.astype(jnp.float32), tables)
    input_re, input_im = spec_against(grad_re, grad_im, tap_re, tap_im)
    grad_mix_cols = signal_of(input_re, input_im, tables).astype(jnp.bfloat16)
    taps_re, taps_im = spec_against(grad_re, grad_im, backward_spec[0], backward_spec[1])
    filt_step = signal_of(taps_re, taps_im, tables)
    grad_mix = jnp.transpose(
        lax.all_to_all(grad_mix_cols, "ctx", split_axis=1, concat_axis=0, tiled=True)
    ).astype(jnp.float32)
    section_grads = jnp.stack(
        [
            grad_y * conv_value,
            grad_mix * backward_rows[:, 2].astype(jnp.float32),
            grad_mix * backward_rows[:, 1].astype(jnp.float32),
        ],
        axis=1,
    ).astype(jnp.bfloat16)
    section_grads, filt_step = (section_grads, filt_step)
    sent_rows, sent_grads = from_partner((forward_out, section_grads), "pipe", 0)
    return (sent_rows[None], sent_grads[None], filt_step[None, None])


def on_device(fwd_in, bwd_in, bwd_cot, filter_taps, norm_gain):
    length = filter_taps.shape[3]
    if not dense_fits(length):
        return on_device_factored(fwd_in, bwd_in, bwd_cot, filter_taps, norm_gain)
    model_width = norm_gain.shape[1] * lax.axis_size("tp")
    table, table_t = real_dft_table(length)
    weights = spectral_weights(length)
    tap_spec = dense_taps_spectrum(filter_taps[0, 0], table_t)
    tap_scaled = tap_spec * weights
    gain_row = norm_gain[0]
    forward_rows = fwd_in[0]
    backward_rows = bwd_in[0]

    def featurize(proj_rows):
        return (proj_rows[:, 1].astype(jnp.float32) * proj_rows[:, 2].astype(jnp.float32)).astype(
            jnp.bfloat16
        )

    def to_columns(rows):
        return lax.all_to_all(rows, "ctx", split_axis=1, concat_axis=0, tiled=True)

    def to_rows(columns):
        return lax.all_to_all(columns, "ctx", split_axis=0, concat_axis=1, tiled=True)

    def row_total(values):
        return lax.psum(jnp.sum(values, axis=1), "tp")

    partner_kv = from_partner(backward_rows[:, 1:3], "pipe", 0)
    forward_cols = to_columns(featurize(forward_rows))
    backward_cols = to_columns(featurize(backward_rows))
    forward_spec = dense_spectrum_exact(forward_cols, table_t)
    forward_z = to_rows(
        dense_signal(dense_multiply(forward_spec, tap_scaled, False), table).astype(jnp.bfloat16)
    )
    backward_spec = dense_spectrum_exact(backward_cols, table_t)
    backward_z = to_rows(
        dense_signal(dense_multiply(backward_spec, tap_scaled, False), table).astype(jnp.bfloat16)
    )
    forward_y = forward_rows[:, 0].astype(jnp.float32) * forward_z.astype(jnp.float32)
    forward_scale = lax.rsqrt(row_total(forward_y * forward_y) / model_width + epsilon)[:, None]
    forward_out = (forward_y * forward_scale * gain_row).astype(jnp.bfloat16)
    sent_rows = from_partner(forward_out, "pipe", 0)
    backward_q = backward_rows[:, 0].astype(jnp.float32)
    conv_value = backward_z.astype(jnp.float32)
    backward_y = backward_q * conv_value
    weighted = bwd_cot[0].astype(jnp.float32) * gain_row
    backward_scale = lax.rsqrt(row_total(backward_y * backward_y) / model_width + epsilon)[:, None]
    normed = backward_y * backward_scale
    average = (row_total(weighted * normed) / model_width)[:, None]
    grad_y = backward_scale * (weighted - normed * average)
    grad_z = (grad_y * backward_q).astype(jnp.bfloat16)
    sent_first = from_partner((grad_y * conv_value).astype(jnp.bfloat16), "pipe", 0)
    grad_spec = dense_spectrum_exact(to_columns(grad_z), table_t) * weights
    grad_mix_cols = dense_signal(dense_multiply(grad_spec, tap_spec, True), table).astype(
        jnp.bfloat16
    )
    taps_prod = dense_multiply(grad_spec, backward_spec, True)
    taps_hi, taps_lo = split_bf16(taps_prod)
    table_hi, table_lo = table
    dims = (((0,), (1,)), ((), ()))
    part = lambda a, b: lax.dot_general(a, b, dims, preferred_element_type=jnp.float32)
    filt_step = part(taps_hi, table_hi) + (part(taps_hi, table_lo) + part(taps_lo, table_hi))
    sent_mix = from_partner(to_rows(grad_mix_cols), "pipe", 0).astype(jnp.float32)
    rest = jnp.stack(
        [
            sent_mix * partner_kv[:, 1].astype(jnp.float32),
            sent_mix * partner_kv[:, 0].astype(jnp.float32),
        ],
        axis=1,
    ).astype(jnp.bfloat16)
    sent_grads = jnp.concatenate([sent_first[:, None], rest], axis=1)
    return (sent_rows[None], sent_grads[None], filt_step[None, None])


def solution(mesh):
    return jax.shard_map(
        on_device,
        mesh=mesh,
        in_specs=(
            P("pipe", "ctx", None, "tp"),
            P("pipe", "ctx", None, "tp"),
            P("pipe", "ctx", "tp"),
            P("pipe", "tp", "ctx", None),
            P("pipe", "tp"),
        ),
        out_specs=(
            P("pipe", "ctx", "tp"),
            P("pipe", "ctx", None, "tp"),
            P("pipe", "tp", "ctx", None),
        ),
        check_vma=False,
    )
```

```python
import math

import jax
import jax.numpy as jnp
from jax import lax
from jax.sharding import PartitionSpec as P

epsilon = 1e-06
highest = lax.Precision.HIGHEST


def from_partner(block, axis, bit):
    count = lax.axis_size(axis)
    route = []
    for low in range(count):
        high = low | 1 << bit
        if high != low and high < count:
            route += [(low, high), (high, low)]
    return lax.ppermute(block, axis, route)


def unit_table(count_out, count_in, period):
    product = lax.broadcasted_iota(jnp.int32, (count_out, count_in), 0) * lax.broadcasted_iota(
        jnp.int32, (count_out, count_in), 1
    )
    phase_angle = (product % period).astype(jnp.float32) * (-2.0 * math.pi / period)
    return (jnp.cos(phase_angle), jnp.sin(phase_angle))


def dft_tables(padded):
    blocks = padded // 128
    cos_high, sin_high = unit_table(blocks, blocks, blocks)
    cos_low, sin_low = unit_table(128, 128, 128)
    cos_twist, sin_twist = unit_table(blocks, 128, padded)
    return (cos_high, sin_high, cos_low, sin_low, cos_twist, sin_twist)


def spectrum(signal, tables):
    cos_high, sin_high, cos_low, sin_low, cos_twist, sin_twist = tables
    channels = signal.shape[0]
    half_blocks = signal.shape[1] // 128
    folded = signal.reshape(channels, half_blocks, 128)
    first_re = jnp.einsum("can,ak->ckn", folded, cos_high[:half_blocks], precision=highest)
    first_im = jnp.einsum("can,ak->ckn", folded, sin_high[:half_blocks], precision=highest)
    turned_re = first_re * cos_twist - first_im * sin_twist
    turned_im = first_re * sin_twist + first_im * cos_twist
    spec_re = jnp.einsum("ckn,nj->ckj", turned_re, cos_low, precision=highest) - jnp.einsum(
        "ckn,nj->ckj", turned_im, sin_low, precision=highest
    )
    spec_im = jnp.einsum("ckn,nj->ckj", turned_re, sin_low, precision=highest) + jnp.einsum(
        "ckn,nj->ckj", turned_im, cos_low, precision=highest
    )
    return (spec_re, spec_im)


def signal_of(spec_re, spec_im, tables):
    cos_high, sin_high, cos_low, sin_low, cos_twist, sin_twist = tables
    channels = spec_re.shape[0]
    blocks = spec_re.shape[1]
    half_blocks = blocks // 2
    mid_re = jnp.einsum("ckj,jn->ckn", spec_re, cos_low, precision=highest) + jnp.einsum(
        "ckj,jn->ckn", spec_im, sin_low, precision=highest
    )
    mid_im = jnp.einsum("ckj,jn->ckn", spec_im, cos_low, precision=highest) - jnp.einsum(
        "ckj,jn->ckn", spec_re, sin_low, precision=highest
    )
    back_re = mid_re * cos_twist + mid_im * sin_twist
    back_im = mid_im * cos_twist - mid_re * sin_twist
    values = jnp.einsum(
        "ak,ckn->can", cos_high[:half_blocks], back_re, precision=highest
    ) + jnp.einsum("ak,ckn->can", sin_high[:half_blocks], back_im, precision=highest)
    return values.reshape(channels, half_blocks * 128) / (blocks * 128)


def spec_product(a_re, a_im, b_re, b_im):
    return (a_re * b_re - a_im * b_im, a_re * b_im + a_im * b_re)


def spec_against(a_re, a_im, b_re, b_im):
    return (a_re * b_re + a_im * b_im, a_im * b_re - a_re * b_im)


def split_bf16(values):
    high = lax.reduce_precision(values, exponent_bits=8, mantissa_bits=7)
    return (high.astype(jnp.bfloat16), (values - high).astype(jnp.bfloat16))


def unit_angles(count_rows, count_cols, stride, padded):
    rows = lax.broadcasted_iota(jnp.int32, (count_rows, count_cols), 0) * stride
    cols = lax.broadcasted_iota(jnp.int32, (count_rows, count_cols), 1)
    angle = ((rows * cols) % padded).astype(jnp.float32) * (2.0 * math.pi / padded)
    return (jnp.cos(angle), jnp.sin(angle))


def real_dft_table(length):
    padded = 2 * length
    inner = 1 << (length.bit_length() // 2)
    if length % inner:
        inner = 1
    outer = length // inner
    cos_outer, sin_outer = unit_angles(outer, length, inner, padded)
    cos_inner, sin_inner = unit_angles(inner, length, 1, padded)
    cos_full = (cos_outer[:, None] * cos_inner[None] - sin_outer[:, None] * sin_inner[None]).reshape(
        length, length
    )
    sin_full = (sin_outer[:, None] * cos_inner[None] + cos_outer[:, None] * sin_inner[None]).reshape(
        length, length
    )
    rows = lax.broadcasted_iota(jnp.int32, (length, length), 0)
    cols = lax.broadcasted_iota(jnp.int32, (length, length), 1)
    alternating = jnp.where(rows % 2 == 0, 1.0, -1.0).astype(jnp.float32)
    sin_part = jnp.where(cols == 0, alternating, -sin_full)
    table = jnp.concatenate([cos_full, sin_part], axis=1)
    return split_bf16(table)


def dot_tf(table, signal):
    return lax.dot_general(
        table, signal, (((0,), (0,)), ((), ())), preferred_element_type=jnp.float32
    )


def dot_tt(table, spec):
    return lax.dot_general(
        table, spec, (((1,), (0,)), ((), ())), preferred_element_type=jnp.float32
    )


def dense_spectrum_exact(rows_bf16, table):
    table_hi, table_lo = table
    return dot_tf(table_hi, rows_bf16) + dot_tf(table_lo, rows_bf16)


def dense_signal(spec, table):
    table_hi, table_lo = table
    spec_hi, spec_lo = split_bf16(spec)
    return dot_tt(table_hi, spec_hi) + (dot_tt(table_lo, spec_hi) + dot_tt(table_hi, spec_lo))


def dense_taps_spectrum(taps, table):
    table_hi, table_lo = table
    taps_hi, taps_lo = split_bf16(taps)
    dims = (((0,), (1,)), ((), ()))
    part = lambda a, b: lax.dot_general(a, b, dims, preferred_element_type=jnp.float32)
    return part(table_hi, taps_hi) + (part(table_lo, taps_hi) + part(table_hi, taps_lo))


def spectral_weights(length):
    index = lax.broadcasted_iota(jnp.int32, (2 * length, 1), 0)
    edge = (index == 0) | (index == length)
    return jnp.where(edge, 1.0, 2.0).astype(jnp.float32) / (2 * length)


def dense_multiply(a, b, conjugate):
    length = a.shape[0] // 2
    a_re, a_im = a[:length], a[length:]
    b_re, b_im = b[:length], b[length:]
    first = lax.broadcasted_iota(jnp.int32, (length, 1), 0) == 0
    if conjugate:
        re = a_re * b_re + a_im * b_im
        im = a_im * b_re - a_re * b_im
    else:
        re = a_re * b_re - a_im * b_im
        im = a_re * b_im + a_im * b_re
    re = jnp.where(first, a_re * b_re, re)
    im = jnp.where(first, a_im * b_im, im)
    return jnp.concatenate([re, im], axis=0)


def dense_fits(length):
    return 4 * length * length * 2 <= 16 * 1024 * 1024


def on_device_factored(fwd_in, bwd_in, bwd_cot, filter_taps, norm_gain):
    model_width = norm_gain.shape[1] * lax.axis_size("tp")
    local_taps = filter_taps[0, 0]
    tables = dft_tables(2 * local_taps.shape[1])
    tap_re, tap_im = spectrum(local_taps, tables)
    gain_row = norm_gain[0]
    forward_rows = fwd_in[0]
    backward_rows = bwd_in[0]

    def featurize(proj_rows):
        return (proj_rows[:, 1].astype(jnp.float32) * proj_rows[:, 2].astype(jnp.float32)).astype(
            jnp.bfloat16
        )

    def convolve(columns):
        sig_re, sig_im = spectrum(columns.astype(jnp.float32), tables)
        prod_re, prod_im = spec_product(sig_re, sig_im, tap_re, tap_im)
        return (signal_of(prod_re, prod_im, tables).astype(jnp.bfloat16), (sig_re, sig_im))

    def relayout(mixed_rows):
        columns = lax.all_to_all(
            jnp.transpose(mixed_rows), "ctx", split_axis=0, concat_axis=1, tiled=True
        )
        result, kept_spec = convolve(columns)
        return (
            jnp.transpose(lax.all_to_all(result, "ctx", split_axis=1, concat_axis=0, tiled=True)),
            kept_spec,
        )

    def row_total(values):
        return lax.psum(jnp.sum(values, axis=1), "tp")

    forward_mix = featurize(forward_rows)
    backward_mix = featurize(backward_rows)
    forward_z = relayout(forward_mix)[0]
    backward_z, backward_spec = relayout(backward_mix)
    forward_y = forward_rows[:, 0].astype(jnp.float32) * forward_z.astype(jnp.float32)
    backward_q = backward_rows[:, 0].astype(jnp.float32)
    conv_value = backward_z.astype(jnp.float32)
    backward_y = backward_q * conv_value
    weighted = bwd_cot[0].astype(jnp.float32) * gain_row
    forward_scale = lax.rsqrt(row_total(forward_y * forward_y) / model_width + epsilon)[:, None]
    backward_scale = lax.rsqrt(row_total(backward_y * backward_y) / model_width + epsilon)[:, None]
    normed = backward_y * backward_scale
    average = (row_total(weighted * normed) / model_width)[:, None]
    forward_out = (forward_y * forward_scale * gain_row).astype(jnp.bfloat16)
    grad_y = backward_scale * (weighted - normed * average)
    grad_z = (grad_y * backward_q).astype(jnp.bfloat16)
    grad_cols = lax.all_to_all(
        jnp.transpose(grad_z), "ctx", split_axis=0, concat_axis=1, tiled=True
    )
    grad_re, grad_im = spectrum(grad_cols.astype(jnp.float32), tables)
    input_re, input_im = spec_against(grad_re, grad_im, tap_re, tap_im)
    grad_mix_cols = signal_of(input_re, input_im, tables).astype(jnp.bfloat16)
    taps_re, taps_im = spec_against(grad_re, grad_im, backward_spec[0], backward_spec[1])
    filt_step = signal_of(taps_re, taps_im, tables)
    grad_mix = jnp.transpose(
        lax.all_to_all(grad_mix_cols, "ctx", split_axis=1, concat_axis=0, tiled=True)
    ).astype(jnp.float32)
    section_grads = jnp.stack(
        [
            grad_y * conv_value,
            grad_mix * backward_rows[:, 2].astype(jnp.float32),
            grad_mix * backward_rows[:, 1].astype(jnp.float32),
        ],
        axis=1,
    ).astype(jnp.bfloat16)
    section_grads, filt_step = (section_grads, filt_step)
    sent_rows, sent_grads = from_partner((forward_out, section_grads), "pipe", 0)
    return (sent_rows[None], sent_grads[None], filt_step[None, None])


def on_device(fwd_in, bwd_in, bwd_cot, filter_taps, norm_gain):
    length = filter_taps.shape[3]
    if not dense_fits(length):
        return on_device_factored(fwd_in, bwd_in, bwd_cot, filter_taps, norm_gain)
    model_width = norm_gain.shape[1] * lax.axis_size("tp")
    table = real_dft_table(length)
    weights = spectral_weights(length)
    tap_spec = dense_taps_spectrum(filter_taps[0, 0], table)
    tap_scaled = tap_spec * weights
    gain_row = norm_gain[0]
    forward_rows = fwd_in[0]
    backward_rows = bwd_in[0]

    def featurize(proj_rows):
        return (proj_rows[:, 1].astype(jnp.float32) * proj_rows[:, 2].astype(jnp.float32)).astype(
            jnp.bfloat16
        )

    def to_columns(rows):
        return lax.all_to_all(rows, "ctx", split_axis=1, concat_axis=0, tiled=True)

    def to_rows(columns):
        return lax.all_to_all(columns, "ctx", split_axis=0, concat_axis=1, tiled=True)

    def row_total(values):
        return lax.psum(jnp.sum(values, axis=1), "tp")

    both_cols = lax.all_to_all(
        jnp.stack([featurize(forward_rows), featurize(backward_rows)], axis=1),
        "ctx",
        split_axis=2,
        concat_axis=0,
        tiled=True,
    )
    forward_spec = dense_spectrum_exact(both_cols[:, 0], table)
    backward_spec = dense_spectrum_exact(both_cols[:, 1], table)
    forward_conv = dense_signal(dense_multiply(forward_spec, tap_scaled, False), table)
    backward_conv = dense_signal(dense_multiply(backward_spec, tap_scaled, False), table)
    both_z = lax.all_to_all(
        jnp.stack([forward_conv, backward_conv], axis=1).astype(jnp.bfloat16),
        "ctx",
        split_axis=0,
        concat_axis=2,
        tiled=True,
    )
    forward_z = both_z[:, 0]
    backward_z = both_z[:, 1]
    forward_y = forward_rows[:, 0].astype(jnp.float32) * forward_z.astype(jnp.float32)
    forward_scale = lax.rsqrt(row_total(forward_y * forward_y) / model_width + epsilon)[:, None]
    forward_out = (forward_y * forward_scale * gain_row).astype(jnp.bfloat16)
    sent_rows = from_partner(forward_out, "pipe", 0)
    backward_q = backward_rows[:, 0].astype(jnp.float32)
    conv_value = backward_z.astype(jnp.float32)
    backward_y = backward_q * conv_value
    weighted = bwd_cot[0].astype(jnp.float32) * gain_row
    backward_scale = lax.rsqrt(row_total(backward_y * backward_y) / model_width + epsilon)[:, None]
    normed = backward_y * backward_scale
    average = (row_total(weighted * normed) / model_width)[:, None]
    grad_y = backward_scale * (weighted - normed * average)
    grad_z = (grad_y * backward_q).astype(jnp.bfloat16)
    sent_first = from_partner((grad_y * conv_value).astype(jnp.bfloat16), "pipe", 0)
    grad_spec = dense_spectrum_exact(to_columns(grad_z), table) * weights
    grad_mix_cols = dense_signal(dense_multiply(grad_spec, tap_spec, True), table).astype(
        jnp.bfloat16
    )
    taps_prod = dense_multiply(grad_spec, backward_spec, True)
    taps_hi, taps_lo = split_bf16(taps_prod)
    table_hi, table_lo = table
    dims = (((0,), (1,)), ((), ()))
    part = lambda a, b: lax.dot_general(a, b, dims, preferred_element_type=jnp.float32)
    filt_step = part(taps_hi, table_hi) + (part(taps_hi, table_lo) + part(taps_lo, table_hi))
    grad_mix = to_rows(grad_mix_cols).astype(jnp.float32)
    rest = jnp.stack(
        [
            grad_mix * backward_rows[:, 2].astype(jnp.float32),
            grad_mix * backward_rows[:, 1].astype(jnp.float32),
        ],
        axis=1,
    ).astype(jnp.bfloat16)
    sent_rest = from_partner(rest, "pipe", 0)
    sent_grads = jnp.concatenate([sent_first[:, None], sent_rest], axis=1)
    return (sent_rows[None], sent_grads[None], filt_step[None, None])


def solution(mesh):
    return jax.shard_map(
        on_device,
        mesh=mesh,
        in_specs=(
            P("pipe", "ctx", None, "tp"),
            P("pipe", "ctx", None, "tp"),
            P("pipe", "ctx", "tp"),
            P("pipe", "tp", "ctx", None),
            P("pipe", "tp"),
        ),
        out_specs=(
            P("pipe", "ctx", "tp"),
            P("pipe", "ctx", None, "tp"),
            P("pipe", "tp", "ctx", None),
        ),
        check_vma=False,
    )
```

```python
import math

import jax
import jax.numpy as jnp
from jax import lax
from jax.sharding import PartitionSpec as P

epsilon = 1e-06
highest = lax.Precision.HIGHEST


def from_partner(block, axis, bit):
    count = lax.axis_size(axis)
    route = []
    for low in range(count):
        high = low | 1 << bit
        if high != low and high < count:
            route += [(low, high), (high, low)]
    return lax.ppermute(block, axis, route)


def unit_table(count_out, count_in, period):
    product = lax.broadcasted_iota(jnp.int32, (count_out, count_in), 0) * lax.broadcasted_iota(
        jnp.int32, (count_out, count_in), 1
    )
    phase_angle = (product % period).astype(jnp.float32) * (-2.0 * math.pi / period)
    return (jnp.cos(phase_angle), jnp.sin(phase_angle))


def dft_tables(padded):
    blocks = padded // 128
    cos_high, sin_high = unit_table(blocks, blocks, blocks)
    cos_low, sin_low = unit_table(128, 128, 128)
    cos_twist, sin_twist = unit_table(blocks, 128, padded)
    return (cos_high, sin_high, cos_low, sin_low, cos_twist, sin_twist)


def spectrum(signal, tables):
    cos_high, sin_high, cos_low, sin_low, cos_twist, sin_twist = tables
    channels = signal.shape[0]
    half_blocks = signal.shape[1] // 128
    folded = signal.reshape(channels, half_blocks, 128)
    first_re = jnp.einsum("can,ak->ckn", folded, cos_high[:half_blocks], precision=highest)
    first_im = jnp.einsum("can,ak->ckn", folded, sin_high[:half_blocks], precision=highest)
    turned_re = first_re * cos_twist - first_im * sin_twist
    turned_im = first_re * sin_twist + first_im * cos_twist
    spec_re = jnp.einsum("ckn,nj->ckj", turned_re, cos_low, precision=highest) - jnp.einsum(
        "ckn,nj->ckj", turned_im, sin_low, precision=highest
    )
    spec_im = jnp.einsum("ckn,nj->ckj", turned_re, sin_low, precision=highest) + jnp.einsum(
        "ckn,nj->ckj", turned_im, cos_low, precision=highest
    )
    return (spec_re, spec_im)


def signal_of(spec_re, spec_im, tables):
    cos_high, sin_high, cos_low, sin_low, cos_twist, sin_twist = tables
    channels = spec_re.shape[0]
    blocks = spec_re.shape[1]
    half_blocks = blocks // 2
    mid_re = jnp.einsum("ckj,jn->ckn", spec_re, cos_low, precision=highest) + jnp.einsum(
        "ckj,jn->ckn", spec_im, sin_low, precision=highest
    )
    mid_im = jnp.einsum("ckj,jn->ckn", spec_im, cos_low, precision=highest) - jnp.einsum(
        "ckj,jn->ckn", spec_re, sin_low, precision=highest
    )
    back_re = mid_re * cos_twist + mid_im * sin_twist
    back_im = mid_im * cos_twist - mid_re * sin_twist
    values = jnp.einsum(
        "ak,ckn->can", cos_high[:half_blocks], back_re, precision=highest
    ) + jnp.einsum("ak,ckn->can", sin_high[:half_blocks], back_im, precision=highest)
    return values.reshape(channels, half_blocks * 128) / (blocks * 128)


def spec_product(a_re, a_im, b_re, b_im):
    return (a_re * b_re - a_im * b_im, a_re * b_im + a_im * b_re)


def spec_against(a_re, a_im, b_re, b_im):
    return (a_re * b_re + a_im * b_im, a_im * b_re - a_re * b_im)


def split_bf16(values):
    high = lax.reduce_precision(values, exponent_bits=8, mantissa_bits=7)
    return (high.astype(jnp.bfloat16), (values - high).astype(jnp.bfloat16))


def unit_angles(count_rows, count_cols, stride, padded):
    rows = lax.broadcasted_iota(jnp.int32, (count_rows, count_cols), 0) * stride
    cols = lax.broadcasted_iota(jnp.int32, (count_rows, count_cols), 1)
    angle = ((rows * cols) % padded).astype(jnp.float32) * (2.0 * math.pi / padded)
    return (jnp.cos(angle), jnp.sin(angle))


def real_dft_table(length):
    padded = 2 * length
    inner = 1 << (length.bit_length() // 2)
    if length % inner:
        inner = 1
    outer = length // inner
    cos_outer, sin_outer = unit_angles(outer, length, inner, padded)
    cos_inner, sin_inner = unit_angles(inner, length, 1, padded)
    cos_full = (cos_outer[:, None] * cos_inner[None] - sin_outer[:, None] * sin_inner[None]).reshape(
        length, length
    )
    sin_full = (sin_outer[:, None] * cos_inner[None] + cos_outer[:, None] * sin_inner[None]).reshape(
        length, length
    )
    rows = lax.broadcasted_iota(jnp.int32, (length, length), 0)
    cols = lax.broadcasted_iota(jnp.int32, (length, length), 1)
    alternating = jnp.where(rows % 2 == 0, 1.0, -1.0).astype(jnp.float32)
    sin_part = jnp.where(cols == 0, alternating, -sin_full)
    table = jnp.concatenate([cos_full, sin_part], axis=1)
    return split_bf16(table)


def dot_tf(table, signal):
    return lax.dot_general(
        table, signal, (((0,), (0,)), ((), ())), preferred_element_type=jnp.float32
    )


def dot_tt(table, spec):
    return lax.dot_general(
        table, spec, (((1,), (0,)), ((), ())), preferred_element_type=jnp.float32
    )


def dense_spectrum_exact(rows_bf16, table):
    table_hi, table_lo = table
    return dot_tf(table_hi, rows_bf16) + dot_tf(table_lo, rows_bf16)


def dense_signal(spec, table):
    table_hi, table_lo = table
    spec_hi, spec_lo = split_bf16(spec)
    return dot_tt(table_hi, spec_hi) + (dot_tt(table_lo, spec_hi) + dot_tt(table_hi, spec_lo))


def dense_taps_spectrum(taps, table):
    table_hi, table_lo = table
    taps_hi, taps_lo = split_bf16(taps)
    dims = (((0,), (1,)), ((), ()))
    part = lambda a, b: lax.dot_general(a, b, dims, preferred_element_type=jnp.float32)
    return part(table_hi, taps_hi) + (part(table_lo, taps_hi) + part(table_hi, taps_lo))


def spectral_weights(length):
    index = lax.broadcasted_iota(jnp.int32, (2 * length, 1), 0)
    edge = (index == 0) | (index == length)
    return jnp.where(edge, 1.0, 2.0).astype(jnp.float32) / (2 * length)


def dense_multiply(a, b, conjugate):
    length = a.shape[0] // 2
    a_re, a_im = a[:length], a[length:]
    b_re, b_im = b[:length], b[length:]
    first = lax.broadcasted_iota(jnp.int32, (length, 1), 0) == 0
    if conjugate:
        re = a_re * b_re + a_im * b_im
        im = a_im * b_re - a_re * b_im
    else:
        re = a_re * b_re - a_im * b_im
        im = a_re * b_im + a_im * b_re
    re = jnp.where(first, a_re * b_re, re)
    im = jnp.where(first, a_im * b_im, im)
    return jnp.concatenate([re, im], axis=0)


def dense_fits(length):
    return 4 * length * length * 2 <= 16 * 1024 * 1024


def on_device_factored(fwd_in, bwd_in, bwd_cot, filter_taps, norm_gain):
    model_width = norm_gain.shape[1] * lax.axis_size("tp")
    local_taps = filter_taps[0, 0]
    tables = dft_tables(2 * local_taps.shape[1])
    tap_re, tap_im = spectrum(local_taps, tables)
    gain_row = norm_gain[0]
    forward_rows = fwd_in[0]
    backward_rows = bwd_in[0]

    def featurize(proj_rows):
        return (proj_rows[:, 1].astype(jnp.float32) * proj_rows[:, 2].astype(jnp.float32)).astype(
            jnp.bfloat16
        )

    def convolve(columns):
        sig_re, sig_im = spectrum(columns.astype(jnp.float32), tables)
        prod_re, prod_im = spec_product(sig_re, sig_im, tap_re, tap_im)
        return (signal_of(prod_re, prod_im, tables).astype(jnp.bfloat16), (sig_re, sig_im))

    def relayout(mixed_rows):
        columns = lax.all_to_all(
            jnp.transpose(mixed_rows), "ctx", split_axis=0, concat_axis=1, tiled=True
        )
        result, kept_spec = convolve(columns)
        return (
            jnp.transpose(lax.all_to_all(result, "ctx", split_axis=1, concat_axis=0, tiled=True)),
            kept_spec,
        )

    def row_total(values):
        return lax.psum(jnp.sum(values, axis=1), "tp")

    forward_mix = featurize(forward_rows)
    backward_mix = featurize(backward_rows)
    forward_z = relayout(forward_mix)[0]
    backward_z, backward_spec = relayout(backward_mix)
    forward_y = forward_rows[:, 0].astype(jnp.float32) * forward_z.astype(jnp.float32)
    backward_q = backward_rows[:, 0].astype(jnp.float32)
    conv_value = backward_z.astype(jnp.float32)
    backward_y = backward_q * conv_value
    weighted = bwd_cot[0].astype(jnp.float32) * gain_row
    forward_scale = lax.rsqrt(row_total(forward_y * forward_y) / model_width + epsilon)[:, None]
    backward_scale = lax.rsqrt(row_total(backward_y * backward_y) / model_width + epsilon)[:, None]
    normed = backward_y * backward_scale
    average = (row_total(weighted * normed) / model_width)[:, None]
    forward_out = (forward_y * forward_scale * gain_row).astype(jnp.bfloat16)
    grad_y = backward_scale * (weighted - normed * average)
    grad_z = (grad_y * backward_q).astype(jnp.bfloat16)
    grad_cols = lax.all_to_all(
        jnp.transpose(grad_z), "ctx", split_axis=0, concat_axis=1, tiled=True
    )
    grad_re, grad_im = spectrum(grad_cols.astype(jnp.float32), tables)
    input_re, input_im = spec_against(grad_re, grad_im, tap_re, tap_im)
    grad_mix_cols = signal_of(input_re, input_im, tables).astype(jnp.bfloat16)
    taps_re, taps_im = spec_against(grad_re, grad_im, backward_spec[0], backward_spec[1])
    filt_step = signal_of(taps_re, taps_im, tables)
    grad_mix = jnp.transpose(
        lax.all_to_all(grad_mix_cols, "ctx", split_axis=1, concat_axis=0, tiled=True)
    ).astype(jnp.float32)
    section_grads = jnp.stack(
        [
            grad_y * conv_value,
            grad_mix * backward_rows[:, 2].astype(jnp.float32),
            grad_mix * backward_rows[:, 1].astype(jnp.float32),
        ],
        axis=1,
    ).astype(jnp.bfloat16)
    section_grads, filt_step = (section_grads, filt_step)
    sent_rows, sent_grads = from_partner((forward_out, section_grads), "pipe", 0)
    return (sent_rows[None], sent_grads[None], filt_step[None, None])


def on_device(fwd_in, bwd_in, bwd_cot, filter_taps, norm_gain):
    length = filter_taps.shape[3]
    if not dense_fits(length):
        return on_device_factored(fwd_in, bwd_in, bwd_cot, filter_taps, norm_gain)
    model_width = norm_gain.shape[1] * lax.axis_size("tp")
    table = real_dft_table(length)
    weights = spectral_weights(length)
    tap_spec = dense_taps_spectrum(filter_taps[0, 0], table)
    tap_scaled = tap_spec * weights
    gain_row = norm_gain[0]
    forward_rows = fwd_in[0]
    backward_rows = bwd_in[0]

    def featurize(proj_rows):
        return (proj_rows[:, 1].astype(jnp.float32) * proj_rows[:, 2].astype(jnp.float32)).astype(
            jnp.bfloat16
        )

    def to_columns(rows):
        return lax.all_to_all(rows, "ctx", split_axis=1, concat_axis=0, tiled=True)

    def to_rows(columns):
        return lax.all_to_all(columns, "ctx", split_axis=0, concat_axis=1, tiled=True)

    def row_total(values):
        return lax.psum(jnp.sum(values, axis=1), "tp")

    partner_kv = from_partner(backward_rows[:, 1:3], "pipe", 0)
    forward_cols = to_columns(featurize(forward_rows))
    backward_cols = to_columns(featurize(backward_rows))
    forward_spec = dense_spectrum_exact(forward_cols, table)
    forward_z = to_rows(
        dense_signal(dense_multiply(forward_spec, tap_scaled, False), table).astype(jnp.bfloat16)
    )
    partner_kv, backward_cols = lax.optimization_barrier((partner_kv, backward_cols))
    backward_spec = dense_spectrum_exact(backward_cols, table)
    backward_z = to_rows(
        dense_signal(dense_multiply(backward_spec, tap_scaled, False), table).astype(jnp.bfloat16)
    )
    forward_y = forward_rows[:, 0].astype(jnp.float32) * forward_z.astype(jnp.float32)
    forward_scale = lax.rsqrt(row_total(forward_y * forward_y) / model_width + epsilon)[:, None]
    forward_out = (forward_y * forward_scale * gain_row).astype(jnp.bfloat16)
    sent_rows = from_partner(forward_out, "pipe", 0)
    backward_q = backward_rows[:, 0].astype(jnp.float32)
    conv_value = backward_z.astype(jnp.float32)
    backward_y = backward_q * conv_value
    weighted = bwd_cot[0].astype(jnp.float32) * gain_row
    backward_scale = lax.rsqrt(row_total(backward_y * backward_y) / model_width + epsilon)[:, None]
    normed = backward_y * backward_scale
    average = (row_total(weighted * normed) / model_width)[:, None]
    grad_y = backward_scale * (weighted - normed * average)
    grad_z = (grad_y * backward_q).astype(jnp.bfloat16)
    sent_first = from_partner((grad_y * conv_value).astype(jnp.bfloat16), "pipe", 0)
    grad_cols = to_columns(grad_z)
    sent_rows, sent_first, grad_cols = lax.optimization_barrier((sent_rows, sent_first, grad_cols))
    grad_spec = dense_spectrum_exact(grad_cols, table) * weights
    grad_mix_cols = dense_signal(dense_multiply(grad_spec, tap_spec, True), table).astype(
        jnp.bfloat16
    )
    taps_prod = dense_multiply(grad_spec, backward_spec, True)
    taps_hi, taps_lo = split_bf16(taps_prod)
    table_hi, table_lo = table
    dims = (((0,), (1,)), ((), ()))
    part = lambda a, b: lax.dot_general(a, b, dims, preferred_element_type=jnp.float32)
    filt_step = part(taps_hi, table_hi) + (part(taps_hi, table_lo) + part(taps_lo, table_hi))
    sent_mix = from_partner(to_rows(grad_mix_cols), "pipe", 0).astype(jnp.float32)
    rest = jnp.stack(
        [
            sent_mix * partner_kv[:, 1].astype(jnp.float32),
            sent_mix * partner_kv[:, 0].astype(jnp.float32),
        ],
        axis=1,
    ).astype(jnp.bfloat16)
    sent_grads = jnp.concatenate([sent_first[:, None], rest], axis=1)
    return (sent_rows[None], sent_grads[None], filt_step[None, None])


def solution(mesh):
    return jax.shard_map(
        on_device,
        mesh=mesh,
        in_specs=(
            P("pipe", "ctx", None, "tp"),
            P("pipe", "ctx", None, "tp"),
            P("pipe", "ctx", "tp"),
            P("pipe", "tp", "ctx", None),
            P("pipe", "tp"),
        ),
        out_specs=(
            P("pipe", "ctx", "tp"),
            P("pipe", "ctx", None, "tp"),
            P("pipe", "tp", "ctx", None),
        ),
        check_vma=False,
    )
```

```python
import math

import jax
import jax.numpy as jnp
from jax import lax
from jax.sharding import PartitionSpec as P

epsilon = 1e-06
highest = lax.Precision.HIGHEST


def from_partner(block, axis, bit):
    count = lax.axis_size(axis)
    route = []
    for low in range(count):
        high = low | 1 << bit
        if high != low and high < count:
            route += [(low, high), (high, low)]
    return lax.ppermute(block, axis, route)


def unit_table(count_out, count_in, period):
    product = lax.broadcasted_iota(jnp.int32, (count_out, count_in), 0) * lax.broadcasted_iota(
        jnp.int32, (count_out, count_in), 1
    )
    phase_angle = (product % period).astype(jnp.float32) * (-2.0 * math.pi / period)
    return (jnp.cos(phase_angle), jnp.sin(phase_angle))


def dft_tables(padded):
    blocks = padded // 128
    cos_high, sin_high = unit_table(blocks, blocks, blocks)
    cos_low, sin_low = unit_table(128, 128, 128)
    cos_twist, sin_twist = unit_table(blocks, 128, padded)
    return (cos_high, sin_high, cos_low, sin_low, cos_twist, sin_twist)


def spectrum(signal, tables):
    cos_high, sin_high, cos_low, sin_low, cos_twist, sin_twist = tables
    channels = signal.shape[0]
    half_blocks = signal.shape[1] // 128
    folded = signal.reshape(channels, half_blocks, 128)
    first_re = jnp.einsum("can,ak->ckn", folded, cos_high[:half_blocks], precision=highest)
    first_im = jnp.einsum("can,ak->ckn", folded, sin_high[:half_blocks], precision=highest)
    turned_re = first_re * cos_twist - first_im * sin_twist
    turned_im = first_re * sin_twist + first_im * cos_twist
    spec_re = jnp.einsum("ckn,nj->ckj", turned_re, cos_low, precision=highest) - jnp.einsum(
        "ckn,nj->ckj", turned_im, sin_low, precision=highest
    )
    spec_im = jnp.einsum("ckn,nj->ckj", turned_re, sin_low, precision=highest) + jnp.einsum(
        "ckn,nj->ckj", turned_im, cos_low, precision=highest
    )
    return (spec_re, spec_im)


def signal_of(spec_re, spec_im, tables):
    cos_high, sin_high, cos_low, sin_low, cos_twist, sin_twist = tables
    channels = spec_re.shape[0]
    blocks = spec_re.shape[1]
    half_blocks = blocks // 2
    mid_re = jnp.einsum("ckj,jn->ckn", spec_re, cos_low, precision=highest) + jnp.einsum(
        "ckj,jn->ckn", spec_im, sin_low, precision=highest
    )
    mid_im = jnp.einsum("ckj,jn->ckn", spec_im, cos_low, precision=highest) - jnp.einsum(
        "ckj,jn->ckn", spec_re, sin_low, precision=highest
    )
    back_re = mid_re * cos_twist + mid_im * sin_twist
    back_im = mid_im * cos_twist - mid_re * sin_twist
    values = jnp.einsum(
        "ak,ckn->can", cos_high[:half_blocks], back_re, precision=highest
    ) + jnp.einsum("ak,ckn->can", sin_high[:half_blocks], back_im, precision=highest)
    return values.reshape(channels, half_blocks * 128) / (blocks * 128)


def spec_product(a_re, a_im, b_re, b_im):
    return (a_re * b_re - a_im * b_im, a_re * b_im + a_im * b_re)


def spec_against(a_re, a_im, b_re, b_im):
    return (a_re * b_re + a_im * b_im, a_im * b_re - a_re * b_im)


def split_bf16(values):
    high = lax.reduce_precision(values, exponent_bits=8, mantissa_bits=7)
    return (high.astype(jnp.bfloat16), (values - high).astype(jnp.bfloat16))


def unit_angles(count_rows, count_cols, stride, padded):
    rows = lax.broadcasted_iota(jnp.int32, (count_rows, count_cols), 0) * stride
    cols = lax.broadcasted_iota(jnp.int32, (count_rows, count_cols), 1)
    angle = ((rows * cols) % padded).astype(jnp.float32) * (2.0 * math.pi / padded)
    return (jnp.cos(angle), jnp.sin(angle))


def real_dft_table(length):
    padded = 2 * length
    inner = 1 << (length.bit_length() // 2)
    if length % inner:
        inner = 1
    outer = length // inner
    cos_outer, sin_outer = unit_angles(outer, length, inner, padded)
    cos_inner, sin_inner = unit_angles(inner, length, 1, padded)
    cos_full = (cos_outer[:, None] * cos_inner[None] - sin_outer[:, None] * sin_inner[None]).reshape(
        length, length
    )
    sin_full = (sin_outer[:, None] * cos_inner[None] + cos_outer[:, None] * sin_inner[None]).reshape(
        length, length
    )
    rows = lax.broadcasted_iota(jnp.int32, (length, length), 0)
    cols = lax.broadcasted_iota(jnp.int32, (length, length), 1)
    alternating = jnp.where(rows % 2 == 0, 1.0, -1.0).astype(jnp.float32)
    sin_part = jnp.where(cols == 0, alternating, -sin_full)
    table = jnp.concatenate([cos_full, sin_part], axis=1)
    return split_bf16(table)


def dot_tf(table, signal):
    return lax.dot_general(
        table, signal, (((0,), (0,)), ((), ())), preferred_element_type=jnp.float32
    )


def dot_tt(table, spec):
    return lax.dot_general(
        table, spec, (((1,), (0,)), ((), ())), preferred_element_type=jnp.float32
    )


def dense_spectrum_exact(rows_bf16, table):
    table_hi, table_lo = table
    return dot_tf(table_hi, rows_bf16) + dot_tf(table_lo, rows_bf16)


def dense_signal(spec, table):
    table_hi, table_lo = table
    spec_hi, spec_lo = split_bf16(spec)
    return dot_tt(table_hi, spec_hi) + (dot_tt(table_lo, spec_hi) + dot_tt(table_hi, spec_lo))


def dense_taps_spectrum(taps, table):
    table_hi, table_lo = table
    taps_hi, taps_lo = split_bf16(taps)
    dims = (((0,), (1,)), ((), ()))
    part = lambda a, b: lax.dot_general(a, b, dims, preferred_element_type=jnp.float32)
    return part(table_hi, taps_hi) + (part(table_lo, taps_hi) + part(table_hi, taps_lo))


def spectral_weights(length):
    index = lax.broadcasted_iota(jnp.int32, (2 * length, 1), 0)
    edge = (index == 0) | (index == length)
    return jnp.where(edge, 1.0, 2.0).astype(jnp.float32) / (2 * length)


def dense_multiply(a, b, conjugate):
    length = a.shape[0] // 2
    a_re, a_im = a[:length], a[length:]
    b_re, b_im = b[:length], b[length:]
    first = lax.broadcasted_iota(jnp.int32, (length, 1), 0) == 0
    if conjugate:
        re = a_re * b_re + a_im * b_im
        im = a_im * b_re - a_re * b_im
    else:
        re = a_re * b_re - a_im * b_im
        im = a_re * b_im + a_im * b_re
    re = jnp.where(first, a_re * b_re, re)
    im = jnp.where(first, a_im * b_im, im)
    return jnp.concatenate([re, im], axis=0)


def dense_fits(length):
    return 4 * length * length * 2 <= 16 * 1024 * 1024


def on_device_factored(fwd_in, bwd_in, bwd_cot, filter_taps, norm_gain):
    model_width = norm_gain.shape[1] * lax.axis_size("tp")
    local_taps = filter_taps[0, 0]
    tables = dft_tables(2 * local_taps.shape[1])
    tap_re, tap_im = spectrum(local_taps, tables)
    gain_row = norm_gain[0]
    forward_rows = fwd_in[0]
    backward_rows = bwd_in[0]

    def featurize(proj_rows):
        return (proj_rows[:, 1].astype(jnp.float32) * proj_rows[:, 2].astype(jnp.float32)).astype(
            jnp.bfloat16
        )

    def convolve(columns):
        sig_re, sig_im = spectrum(columns.astype(jnp.float32), tables)
        prod_re, prod_im = spec_product(sig_re, sig_im, tap_re, tap_im)
        return (signal_of(prod_re, prod_im, tables).astype(jnp.bfloat16), (sig_re, sig_im))

    def relayout(mixed_rows):
        columns = lax.all_to_all(
            jnp.transpose(mixed_rows), "ctx", split_axis=0, concat_axis=1, tiled=True
        )
        result, kept_spec = convolve(columns)
        return (
            jnp.transpose(lax.all_to_all(result, "ctx", split_axis=1, concat_axis=0, tiled=True)),
            kept_spec,
        )

    def row_total(values):
        return lax.psum(jnp.sum(values, axis=1), "tp")

    forward_mix = featurize(forward_rows)
    backward_mix = featurize(backward_rows)
    forward_z = relayout(forward_mix)[0]
    backward_z, backward_spec = relayout(backward_mix)
    forward_y = forward_rows[:, 0].astype(jnp.float32) * forward_z.astype(jnp.float32)
    backward_q = backward_rows[:, 0].astype(jnp.float32)
    conv_value = backward_z.astype(jnp.float32)
    backward_y = backward_q * conv_value
    weighted = bwd_cot[0].astype(jnp.float32) * gain_row
    forward_scale = lax.rsqrt(row_total(forward_y * forward_y) / model_width + epsilon)[:, None]
    backward_scale = lax.rsqrt(row_total(backward_y * backward_y) / model_width + epsilon)[:, None]
    normed = backward_y * backward_scale
    average = (row_total(weighted * normed) / model_width)[:, None]
    forward_out = (forward_y * forward_scale * gain_row).astype(jnp.bfloat16)
    grad_y = backward_scale * (weighted - normed * average)
    grad_z = (grad_y * backward_q).astype(jnp.bfloat16)
    grad_cols = lax.all_to_all(
        jnp.transpose(grad_z), "ctx", split_axis=0, concat_axis=1, tiled=True
    )
    grad_re, grad_im = spectrum(grad_cols.astype(jnp.float32), tables)
    input_re, input_im = spec_against(grad_re, grad_im, tap_re, tap_im)
    grad_mix_cols = signal_of(input_re, input_im, tables).astype(jnp.bfloat16)
    taps_re, taps_im = spec_against(grad_re, grad_im, backward_spec[0], backward_spec[1])
    filt_step = signal_of(taps_re, taps_im, tables)
    grad_mix = jnp.transpose(
        lax.all_to_all(grad_mix_cols, "ctx", split_axis=1, concat_axis=0, tiled=True)
    ).astype(jnp.float32)
    section_grads = jnp.stack(
        [
            grad_y * conv_value,
            grad_mix * backward_rows[:, 2].astype(jnp.float32),
            grad_mix * backward_rows[:, 1].astype(jnp.float32),
        ],
        axis=1,
    ).astype(jnp.bfloat16)
    section_grads, filt_step = (section_grads, filt_step)
    sent_rows, sent_grads = from_partner((forward_out, section_grads), "pipe", 0)
    return (sent_rows[None], sent_grads[None], filt_step[None, None])


def on_device(fwd_in, bwd_in, bwd_cot, filter_taps, norm_gain):
    length = filter_taps.shape[3]
    if not dense_fits(length):
        return on_device_factored(fwd_in, bwd_in, bwd_cot, filter_taps, norm_gain)
    model_width = norm_gain.shape[1] * lax.axis_size("tp")
    table = real_dft_table(length)
    weights = spectral_weights(length)
    tap_spec = dense_taps_spectrum(filter_taps[0, 0], table)
    tap_scaled = tap_spec * weights
    gain_row = norm_gain[0]
    forward_rows = fwd_in[0]
    backward_rows = bwd_in[0]

    def featurize(proj_rows):
        return (proj_rows[:, 1].astype(jnp.float32) * proj_rows[:, 2].astype(jnp.float32)).astype(
            jnp.bfloat16
        )

    def to_columns(rows):
        return lax.all_to_all(rows, "ctx", split_axis=1, concat_axis=0, tiled=True)

    def to_rows(columns):
        return lax.all_to_all(columns, "ctx", split_axis=0, concat_axis=1, tiled=True)

    def row_total(values):
        return lax.psum(jnp.sum(values, axis=1), "tp")

    partner_kv = from_partner(backward_rows[:, 1:3], "pipe", 0)
    forward_cols = to_columns(featurize(forward_rows))
    backward_cols = to_columns(featurize(backward_rows))
    forward_spec = dense_spectrum_exact(forward_cols, table)
    forward_z = to_rows(
        dense_signal(dense_multiply(forward_spec, tap_scaled, False), table).astype(jnp.bfloat16)
    )
    partner_kv, backward_cols = lax.optimization_barrier((partner_kv, backward_cols))
    backward_spec = dense_spectrum_exact(backward_cols, table)
    backward_z = to_rows(
        dense_signal(dense_multiply(backward_spec, tap_scaled, False), table).astype(jnp.bfloat16)
    )
    forward_y = forward_rows[:, 0].astype(jnp.float32) * forward_z.astype(jnp.float32)
    forward_scale = lax.rsqrt(row_total(forward_y * forward_y) / model_width + epsilon)[:, None]
    forward_out = (forward_y * forward_scale * gain_row).astype(jnp.bfloat16)
    sent_rows = from_partner(forward_out, "pipe", 0)
    backward_q = backward_rows[:, 0].astype(jnp.float32)
    conv_value = backward_z.astype(jnp.float32)
    backward_y = backward_q * conv_value
    weighted = bwd_cot[0].astype(jnp.float32) * gain_row
    backward_scale = lax.rsqrt(row_total(backward_y * backward_y) / model_width + epsilon)[:, None]
    normed = backward_y * backward_scale
    average = (row_total(weighted * normed) / model_width)[:, None]
    grad_y = backward_scale * (weighted - normed * average)
    grad_z = (grad_y * backward_q).astype(jnp.bfloat16)
    sent_first = from_partner((grad_y * conv_value).astype(jnp.bfloat16), "pipe", 0)
    grad_cols = to_columns(grad_z)
    grad_spec = dense_spectrum_exact(grad_cols, table) * weights
    grad_mix_cols = dense_signal(dense_multiply(grad_spec, tap_spec, True), table).astype(
        jnp.bfloat16
    )
    sent_rows, sent_first, grad_mix_cols = lax.optimization_barrier((sent_rows, sent_first, grad_mix_cols))
    taps_prod = dense_multiply(grad_spec, backward_spec, True)
    taps_hi, taps_lo = split_bf16(taps_prod)
    table_hi, table_lo = table
    dims = (((0,), (1,)), ((), ()))
    part = lambda a, b: lax.dot_general(a, b, dims, preferred_element_type=jnp.float32)
    filt_step = part(taps_hi, table_hi) + (part(taps_hi, table_lo) + part(taps_lo, table_hi))
    sent_mix = from_partner(to_rows(grad_mix_cols), "pipe", 0).astype(jnp.float32)
    rest = jnp.stack(
        [
            sent_mix * partner_kv[:, 1].astype(jnp.float32),
            sent_mix * partner_kv[:, 0].astype(jnp.float32),
        ],
        axis=1,
    ).astype(jnp.bfloat16)
    sent_grads = jnp.concatenate([sent_first[:, None], rest], axis=1)
    return (sent_rows[None], sent_grads[None], filt_step[None, None])


def solution(mesh):
    return jax.shard_map(
        on_device,
        mesh=mesh,
        in_specs=(
            P("pipe", "ctx", None, "tp"),
            P("pipe", "ctx", None, "tp"),
            P("pipe", "ctx", "tp"),
            P("pipe", "tp", "ctx", None),
            P("pipe", "tp"),
        ),
        out_specs=(
            P("pipe", "ctx", "tp"),
            P("pipe", "ctx", None, "tp"),
            P("pipe", "tp", "ctx", None),
        ),
        check_vma=False,
    )
```

```python
import math

import jax
import jax.numpy as jnp
from jax import lax
from jax.sharding import PartitionSpec as P

epsilon = 1e-06
highest = lax.Precision.HIGHEST


def from_partner(block, axis, bit):
    count = lax.axis_size(axis)
    route = []
    for low in range(count):
        high = low | 1 << bit
        if high != low and high < count:
            route += [(low, high), (high, low)]
    return lax.ppermute(block, axis, route)


def unit_table(count_out, count_in, period):
    product = lax.broadcasted_iota(jnp.int32, (count_out, count_in), 0) * lax.broadcasted_iota(
        jnp.int32, (count_out, count_in), 1
    )
    phase_angle = (product % period).astype(jnp.float32) * (-2.0 * math.pi / period)
    return (jnp.cos(phase_angle), jnp.sin(phase_angle))


def dft_tables(padded):
    blocks = padded // 128
    cos_high, sin_high = unit_table(blocks, blocks, blocks)
    cos_low, sin_low = unit_table(128, 128, 128)
    cos_twist, sin_twist = unit_table(blocks, 128, padded)
    return (cos_high, sin_high, cos_low, sin_low, cos_twist, sin_twist)


def spectrum(signal, tables):
    cos_high, sin_high, cos_low, sin_low, cos_twist, sin_twist = tables
    channels = signal.shape[0]
    half_blocks = signal.shape[1] // 128
    folded = signal.reshape(channels, half_blocks, 128)
    first_re = jnp.einsum("can,ak->ckn", folded, cos_high[:half_blocks], precision=highest)
    first_im = jnp.einsum("can,ak->ckn", folded, sin_high[:half_blocks], precision=highest)
    turned_re = first_re * cos_twist - first_im * sin_twist
    turned_im = first_re * sin_twist + first_im * cos_twist
    spec_re = jnp.einsum("ckn,nj->ckj", turned_re, cos_low, precision=highest) - jnp.einsum(
        "ckn,nj->ckj", turned_im, sin_low, precision=highest
    )
    spec_im = jnp.einsum("ckn,nj->ckj", turned_re, sin_low, precision=highest) + jnp.einsum(
        "ckn,nj->ckj", turned_im, cos_low, precision=highest
    )
    return (spec_re, spec_im)


def signal_of(spec_re, spec_im, tables):
    cos_high, sin_high, cos_low, sin_low, cos_twist, sin_twist = tables
    channels = spec_re.shape[0]
    blocks = spec_re.shape[1]
    half_blocks = blocks // 2
    mid_re = jnp.einsum("ckj,jn->ckn", spec_re, cos_low, precision=highest) + jnp.einsum(
        "ckj,jn->ckn", spec_im, sin_low, precision=highest
    )
    mid_im = jnp.einsum("ckj,jn->ckn", spec_im, cos_low, precision=highest) - jnp.einsum(
        "ckj,jn->ckn", spec_re, sin_low, precision=highest
    )
    back_re = mid_re * cos_twist + mid_im * sin_twist
    back_im = mid_im * cos_twist - mid_re * sin_twist
    values = jnp.einsum(
        "ak,ckn->can", cos_high[:half_blocks], back_re, precision=highest
    ) + jnp.einsum("ak,ckn->can", sin_high[:half_blocks], back_im, precision=highest)
    return values.reshape(channels, half_blocks * 128) / (blocks * 128)


def spec_product(a_re, a_im, b_re, b_im):
    return (a_re * b_re - a_im * b_im, a_re * b_im + a_im * b_re)


def spec_against(a_re, a_im, b_re, b_im):
    return (a_re * b_re + a_im * b_im, a_im * b_re - a_re * b_im)


def split_bf16(values):
    high = lax.reduce_precision(values, exponent_bits=8, mantissa_bits=7)
    return (high.astype(jnp.bfloat16), (values - high).astype(jnp.bfloat16))


def unit_angles(count_rows, count_cols, stride, padded):
    rows = lax.broadcasted_iota(jnp.int32, (count_rows, count_cols), 0) * stride
    cols = lax.broadcasted_iota(jnp.int32, (count_rows, count_cols), 1)
    angle = ((rows * cols) % padded).astype(jnp.float32) * (2.0 * math.pi / padded)
    return (jnp.cos(angle), jnp.sin(angle))


def real_dft_table(length):
    padded = 2 * length
    inner = 1 << (length.bit_length() // 2)
    if length % inner:
        inner = 1
    outer = length // inner
    cos_outer, sin_outer = unit_angles(outer, length, inner, padded)
    cos_inner, sin_inner = unit_angles(inner, length, 1, padded)
    cos_full = (cos_outer[:, None] * cos_inner[None] - sin_outer[:, None] * sin_inner[None]).reshape(
        length, length
    )
    sin_full = (sin_outer[:, None] * cos_inner[None] + cos_outer[:, None] * sin_inner[None]).reshape(
        length, length
    )
    rows = lax.broadcasted_iota(jnp.int32, (length, length), 0)
    cols = lax.broadcasted_iota(jnp.int32, (length, length), 1)
    alternating = jnp.where(rows % 2 == 0, 1.0, -1.0).astype(jnp.float32)
    sin_part = jnp.where(cols == 0, alternating, -sin_full)
    table = jnp.concatenate([cos_full, sin_part], axis=1)
    return split_bf16(table)


def dot_tf(table, signal):
    return lax.dot_general(
        table, signal, (((0,), (0,)), ((), ())), preferred_element_type=jnp.float32
    )


def dot_tt(table, spec):
    return lax.dot_general(
        table, spec, (((1,), (0,)), ((), ())), preferred_element_type=jnp.float32
    )


def dense_spectrum_exact(rows_bf16, table):
    table_hi, table_lo = table
    return dot_tf(table_hi, rows_bf16) + dot_tf(table_lo, rows_bf16)


def dense_signal(spec, table):
    table_hi, table_lo = table
    spec_hi, spec_lo = split_bf16(spec)
    return dot_tt(table_hi, spec_hi) + (dot_tt(table_lo, spec_hi) + dot_tt(table_hi, spec_lo))


def dense_taps_spectrum(taps, table):
    table_hi, table_lo = table
    taps_hi, taps_lo = split_bf16(taps)
    dims = (((0,), (1,)), ((), ()))
    part = lambda a, b: lax.dot_general(a, b, dims, preferred_element_type=jnp.float32)
    return part(table_hi, taps_hi) + (part(table_lo, taps_hi) + part(table_hi, taps_lo))


def spectral_weights(length):
    index = lax.broadcasted_iota(jnp.int32, (2 * length, 1), 0)
    edge = (index == 0) | (index == length)
    return jnp.where(edge, 1.0, 2.0).astype(jnp.float32) / (2 * length)


def dense_multiply(a, b, conjugate):
    length = a.shape[0] // 2
    a_re, a_im = a[:length], a[length:]
    b_re, b_im = b[:length], b[length:]
    first = lax.broadcasted_iota(jnp.int32, (length, 1), 0) == 0
    if conjugate:
        re = a_re * b_re + a_im * b_im
        im = a_im * b_re - a_re * b_im
    else:
        re = a_re * b_re - a_im * b_im
        im = a_re * b_im + a_im * b_re
    re = jnp.where(first, a_re * b_re, re)
    im = jnp.where(first, a_im * b_im, im)
    return jnp.concatenate([re, im], axis=0)


def dense_fits(length):
    return 4 * length * length * 2 <= 16 * 1024 * 1024


def on_device_factored(fwd_in, bwd_in, bwd_cot, filter_taps, norm_gain):
    model_width = norm_gain.shape[1] * lax.axis_size("tp")
    local_taps = filter_taps[0, 0]
    tables = dft_tables(2 * local_taps.shape[1])
    tap_re, tap_im = spectrum(local_taps, tables)
    gain_row = norm_gain[0]
    forward_rows = fwd_in[0]
    backward_rows = bwd_in[0]

    def featurize(proj_rows):
        return (proj_rows[:, 1].astype(jnp.float32) * proj_rows[:, 2].astype(jnp.float32)).astype(
            jnp.bfloat16
        )

    def convolve(columns):
        sig_re, sig_im = spectrum(columns.astype(jnp.float32), tables)
        prod_re, prod_im = spec_product(sig_re, sig_im, tap_re, tap_im)
        return (signal_of(prod_re, prod_im, tables).astype(jnp.bfloat16), (sig_re, sig_im))

    def relayout(mixed_rows):
        columns = lax.all_to_all(
            jnp.transpose(mixed_rows), "ctx", split_axis=0, concat_axis=1, tiled=True
        )
        result, kept_spec = convolve(columns)
        return (
            jnp.transpose(lax.all_to_all(result, "ctx", split_axis=1, concat_axis=0, tiled=True)),
            kept_spec,
        )

    def row_total(values):
        return lax.psum(jnp.sum(values, axis=1), "tp")

    forward_mix = featurize(forward_rows)
    backward_mix = featurize(backward_rows)
    forward_z = relayout(forward_mix)[0]
    backward_z, backward_spec = relayout(backward_mix)
    forward_y = forward_rows[:, 0].astype(jnp.float32) * forward_z.astype(jnp.float32)
    backward_q = backward_rows[:, 0].astype(jnp.float32)
    conv_value = backward_z.astype(jnp.float32)
    backward_y = backward_q * conv_value
    weighted = bwd_cot[0].astype(jnp.float32) * gain_row
    forward_scale = lax.rsqrt(row_total(forward_y * forward_y) / model_width + epsilon)[:, None]
    backward_scale = lax.rsqrt(row_total(backward_y * backward_y) / model_width + epsilon)[:, None]
    normed = backward_y * backward_scale
    average = (row_total(weighted * normed) / model_width)[:, None]
    forward_out = (forward_y * forward_scale * gain_row).astype(jnp.bfloat16)
    grad_y = backward_scale * (weighted - normed * average)
    grad_z = (grad_y * backward_q).astype(jnp.bfloat16)
    grad_cols = lax.all_to_all(
        jnp.transpose(grad_z), "ctx", split_axis=0, concat_axis=1, tiled=True
    )
    grad_re, grad_im = spectrum(grad_cols.astype(jnp.float32), tables)
    input_re, input_im = spec_against(grad_re, grad_im, tap_re, tap_im)
    grad_mix_cols = signal_of(input_re, input_im, tables).astype(jnp.bfloat16)
    taps_re, taps_im = spec_against(grad_re, grad_im, backward_spec[0], backward_spec[1])
    filt_step = signal_of(taps_re, taps_im, tables)
    grad_mix = jnp.transpose(
        lax.all_to_all(grad_mix_cols, "ctx", split_axis=1, concat_axis=0, tiled=True)
    ).astype(jnp.float32)
    section_grads = jnp.stack(
        [
            grad_y * conv_value,
            grad_mix * backward_rows[:, 2].astype(jnp.float32),
            grad_mix * backward_rows[:, 1].astype(jnp.float32),
        ],
        axis=1,
    ).astype(jnp.bfloat16)
    section_grads, filt_step = (section_grads, filt_step)
    sent_rows, sent_grads = from_partner((forward_out, section_grads), "pipe", 0)
    return (sent_rows[None], sent_grads[None], filt_step[None, None])


def on_device(fwd_in, bwd_in, bwd_cot, filter_taps, norm_gain):
    length = filter_taps.shape[3]
    if not dense_fits(length):
        return on_device_factored(fwd_in, bwd_in, bwd_cot, filter_taps, norm_gain)
    model_width = norm_gain.shape[1] * lax.axis_size("tp")
    table = real_dft_table(length)
    weights = spectral_weights(length)
    tap_spec = dense_taps_spectrum(filter_taps[0, 0], table)
    tap_scaled = tap_spec * weights
    gain_row = norm_gain[0]
    forward_rows = fwd_in[0]
    backward_rows = bwd_in[0]

    def featurize(proj_rows):
        return (proj_rows[:, 1].astype(jnp.float32) * proj_rows[:, 2].astype(jnp.float32)).astype(
            jnp.bfloat16
        )

    def to_columns(rows):
        return lax.all_to_all(rows, "ctx", split_axis=1, concat_axis=0, tiled=True)

    def to_rows(columns):
        return lax.all_to_all(columns, "ctx", split_axis=0, concat_axis=1, tiled=True)

    def row_total(values):
        return lax.psum(jnp.sum(values, axis=1), "tp")

    partner_kv = from_partner(backward_rows[:, 1:3], "pipe", 0)
    forward_cols = to_columns(featurize(forward_rows))
    backward_cols = to_columns(featurize(backward_rows))
    forward_spec = dense_spectrum_exact(forward_cols, table)
    forward_z = to_rows(
        dense_signal(dense_multiply(forward_spec, tap_scaled, False), table).astype(jnp.bfloat16)
    )
    partner_kv, backward_cols = lax.optimization_barrier((partner_kv, backward_cols))
    backward_spec = dense_spectrum_exact(backward_cols, table)
    backward_z = to_rows(
        dense_signal(dense_multiply(backward_spec, tap_scaled, False), table).astype(jnp.bfloat16)
    )
    forward_y = forward_rows[:, 0].astype(jnp.float32) * forward_z.astype(jnp.float32)
    forward_scale = lax.rsqrt(row_total(forward_y * forward_y) / model_width + epsilon)[:, None]
    forward_out = (forward_y * forward_scale * gain_row).astype(jnp.bfloat16)
    sent_rows = from_partner(forward_out, "pipe", 0)
    backward_q = backward_rows[:, 0].astype(jnp.float32)
    conv_value = backward_z.astype(jnp.float32)
    backward_y = backward_q * conv_value
    weighted = bwd_cot[0].astype(jnp.float32) * gain_row
    backward_scale = lax.rsqrt(row_total(backward_y * backward_y) / model_width + epsilon)[:, None]
    normed = backward_y * backward_scale
    average = (row_total(weighted * normed) / model_width)[:, None]
    grad_y = backward_scale * (weighted - normed * average)
    grad_z = (grad_y * backward_q).astype(jnp.bfloat16)
    sent_first = from_partner((grad_y * conv_value).astype(jnp.bfloat16), "pipe", 0)
    grad_cols = to_columns(grad_z)
    grad_spec = dense_spectrum_exact(grad_cols, table) * weights
    grad_mix_cols = dense_signal(dense_multiply(grad_spec, tap_spec, True), table).astype(
        jnp.bfloat16
    )
    sent_rows, sent_first, grad_mix_cols = lax.optimization_barrier((sent_rows, sent_first, grad_mix_cols))
    taps_prod = dense_multiply(grad_spec, backward_spec, True)
    taps_hi, taps_lo = split_bf16(taps_prod)
    table_hi, table_lo = table
    dims = (((0,), (1,)), ((), ()))
    part = lambda a, b: lax.dot_general(a, b, dims, preferred_element_type=jnp.float32)
    filt_step = part(taps_hi, table_hi) + (part(taps_hi, table_lo) + part(taps_lo, table_hi))
    grad_mix_rows, filt_step = lax.optimization_barrier((to_rows(grad_mix_cols), filt_step))
    sent_mix = from_partner(grad_mix_rows, "pipe", 0).astype(jnp.float32)
    rest = jnp.stack(
        [
            sent_mix * partner_kv[:, 1].astype(jnp.float32),
            sent_mix * partner_kv[:, 0].astype(jnp.float32),
        ],
        axis=1,
    ).astype(jnp.bfloat16)
    sent_grads = jnp.concatenate([sent_first[:, None], rest], axis=1)
    return (sent_rows[None], sent_grads[None], filt_step[None, None])


def solution(mesh):
    return jax.shard_map(
        on_device,
        mesh=mesh,
        in_specs=(
            P("pipe", "ctx", None, "tp"),
            P("pipe", "ctx", None, "tp"),
            P("pipe", "ctx", "tp"),
            P("pipe", "tp", "ctx", None),
            P("pipe", "tp"),
        ),
        out_specs=(
            P("pipe", "ctx", "tp"),
            P("pipe", "ctx", None, "tp"),
            P("pipe", "tp", "ctx", None),
        ),
        check_vma=False,
    )
```

```python
import math

import jax
import jax.numpy as jnp
from jax import lax
from jax.sharding import PartitionSpec as P

epsilon = 1e-06
highest = lax.Precision.HIGHEST


def from_partner(block, axis, bit):
    count = lax.axis_size(axis)
    route = []
    for low in range(count):
        high = low | 1 << bit
        if high != low and high < count:
            route += [(low, high), (high, low)]
    return lax.ppermute(block, axis, route)


def unit_table(count_out, count_in, period):
    product = lax.broadcasted_iota(jnp.int32, (count_out, count_in), 0) * lax.broadcasted_iota(
        jnp.int32, (count_out, count_in), 1
    )
    phase_angle = (product % period).astype(jnp.float32) * (-2.0 * math.pi / period)
    return (jnp.cos(phase_angle), jnp.sin(phase_angle))


def dft_tables(padded):
    blocks = padded // 128
    cos_high, sin_high = unit_table(blocks, blocks, blocks)
    cos_low, sin_low = unit_table(128, 128, 128)
    cos_twist, sin_twist = unit_table(blocks, 128, padded)
    return (cos_high, sin_high, cos_low, sin_low, cos_twist, sin_twist)


def spectrum(signal, tables):
    cos_high, sin_high, cos_low, sin_low, cos_twist, sin_twist = tables
    channels = signal.shape[0]
    half_blocks = signal.shape[1] // 128
    folded = signal.reshape(channels, half_blocks, 128)
    first_re = jnp.einsum("can,ak->ckn", folded, cos_high[:half_blocks], precision=highest)
    first_im = jnp.einsum("can,ak->ckn", folded, sin_high[:half_blocks], precision=highest)
    turned_re = first_re * cos_twist - first_im * sin_twist
    turned_im = first_re * sin_twist + first_im * cos_twist
    spec_re = jnp.einsum("ckn,nj->ckj", turned_re, cos_low, precision=highest) - jnp.einsum(
        "ckn,nj->ckj", turned_im, sin_low, precision=highest
    )
    spec_im = jnp.einsum("ckn,nj->ckj", turned_re, sin_low, precision=highest) + jnp.einsum(
        "ckn,nj->ckj", turned_im, cos_low, precision=highest
    )
    return (spec_re, spec_im)


def signal_of(spec_re, spec_im, tables):
    cos_high, sin_high, cos_low, sin_low, cos_twist, sin_twist = tables
    channels = spec_re.shape[0]
    blocks = spec_re.shape[1]
    half_blocks = blocks // 2
    mid_re = jnp.einsum("ckj,jn->ckn", spec_re, cos_low, precision=highest) + jnp.einsum(
        "ckj,jn->ckn", spec_im, sin_low, precision=highest
    )
    mid_im = jnp.einsum("ckj,jn->ckn", spec_im, cos_low, precision=highest) - jnp.einsum(
        "ckj,jn->ckn", spec_re, sin_low, precision=highest
    )
    back_re = mid_re * cos_twist + mid_im * sin_twist
    back_im = mid_im * cos_twist - mid_re * sin_twist
    values = jnp.einsum(
        "ak,ckn->can", cos_high[:half_blocks], back_re, precision=highest
    ) + jnp.einsum("ak,ckn->can", sin_high[:half_blocks], back_im, precision=highest)
    return values.reshape(channels, half_blocks * 128) / (blocks * 128)


def spec_product(a_re, a_im, b_re, b_im):
    return (a_re * b_re - a_im * b_im, a_re * b_im + a_im * b_re)


def spec_against(a_re, a_im, b_re, b_im):
    return (a_re * b_re + a_im * b_im, a_im * b_re - a_re * b_im)


def split_bf16(values):
    high = lax.reduce_precision(values, exponent_bits=8, mantissa_bits=7)
    return (high.astype(jnp.bfloat16), (values - high).astype(jnp.bfloat16))


def unit_angles(count_rows, count_cols, stride, padded):
    rows = lax.broadcasted_iota(jnp.int32, (count_rows, count_cols), 0) * stride
    cols = lax.broadcasted_iota(jnp.int32, (count_rows, count_cols), 1)
    angle = ((rows * cols) % padded).astype(jnp.float32) * (2.0 * math.pi / padded)
    return (jnp.cos(angle), jnp.sin(angle))


def real_dft_table(length):
    padded = 2 * length
    inner = 1 << (length.bit_length() // 2)
    if length % inner:
        inner = 1
    outer = length // inner
    cos_outer, sin_outer = unit_angles(outer, length, inner, padded)
    cos_inner, sin_inner = unit_angles(inner, length, 1, padded)
    cos_full = (cos_outer[:, None] * cos_inner[None] - sin_outer[:, None] * sin_inner[None]).reshape(
        length, length
    )
    sin_full = (sin_outer[:, None] * cos_inner[None] + cos_outer[:, None] * sin_inner[None]).reshape(
        length, length
    )
    rows = lax.broadcasted_iota(jnp.int32, (length, length), 0)
    cols = lax.broadcasted_iota(jnp.int32, (length, length), 1)
    alternating = jnp.where(rows % 2 == 0, 1.0, -1.0).astype(jnp.float32)
    sin_part = jnp.where(cols == 0, alternating, -sin_full)
    table = jnp.concatenate([cos_full, sin_part], axis=1)
    return split_bf16(table)


def dot_tf(table, signal):
    return lax.dot_general(
        table, signal, (((0,), (0,)), ((), ())), preferred_element_type=jnp.float32
    )


def dot_tt(table, spec):
    return lax.dot_general(
        table, spec, (((1,), (0,)), ((), ())), preferred_element_type=jnp.float32
    )


def dense_spectrum_exact(rows_bf16, table):
    table_hi, table_lo = table
    return dot_tf(table_hi, rows_bf16) + dot_tf(table_lo, rows_bf16)


def dense_signal(spec, table):
    table_hi, table_lo = table
    spec_hi, spec_lo = split_bf16(spec)
    return dot_tt(table_hi, spec_hi) + (dot_tt(table_lo, spec_hi) + dot_tt(table_hi, spec_lo))


def dense_taps_spectrum(taps, table):
    table_hi, table_lo = table
    taps_hi, taps_lo = split_bf16(taps)
    dims = (((0,), (1,)), ((), ()))
    part = lambda a, b: lax.dot_general(a, b, dims, preferred_element_type=jnp.float32)
    return part(table_hi, taps_hi) + (part(table_lo, taps_hi) + part(table_hi, taps_lo))


def spectral_weights(length):
    index = lax.broadcasted_iota(jnp.int32, (2 * length, 1), 0)
    edge = (index == 0) | (index == length)
    return jnp.where(edge, 1.0, 2.0).astype(jnp.float32) / (2 * length)


def dense_multiply(a, b, conjugate):
    length = a.shape[0] // 2
    a_re, a_im = a[:length], a[length:]
    b_re, b_im = b[:length], b[length:]
    first = lax.broadcasted_iota(jnp.int32, (length, 1), 0) == 0
    if conjugate:
        re = a_re * b_re + a_im * b_im
        im = a_im * b_re - a_re * b_im
    else:
        re = a_re * b_re - a_im * b_im
        im = a_re * b_im + a_im * b_re
    re = jnp.where(first, a_re * b_re, re)
    im = jnp.where(first, a_im * b_im, im)
    return jnp.concatenate([re, im], axis=0)


def dense_fits(length):
    return 4 * length * length * 2 <= 16 * 1024 * 1024


def on_device_factored(fwd_in, bwd_in, bwd_cot, filter_taps, norm_gain):
    model_width = norm_gain.shape[1] * lax.axis_size("tp")
    local_taps = filter_taps[0, 0]
    tables = dft_tables(2 * local_taps.shape[1])
    tap_re, tap_im = spectrum(local_taps, tables)
    gain_row = norm_gain[0]
    forward_rows = fwd_in[0]
    backward_rows = bwd_in[0]

    def featurize(proj_rows):
        return (proj_rows[:, 1].astype(jnp.float32) * proj_rows[:, 2].astype(jnp.float32)).astype(
            jnp.bfloat16
        )

    def convolve(columns):
        sig_re, sig_im = spectrum(columns.astype(jnp.float32), tables)
        prod_re, prod_im = spec_product(sig_re, sig_im, tap_re, tap_im)
        return (signal_of(prod_re, prod_im, tables).astype(jnp.bfloat16), (sig_re, sig_im))

    def relayout(mixed_rows):
        columns = lax.all_to_all(
            jnp.transpose(mixed_rows), "ctx", split_axis=0, concat_axis=1, tiled=True
        )
        result, kept_spec = convolve(columns)
        return (
            jnp.transpose(lax.all_to_all(result, "ctx", split_axis=1, concat_axis=0, tiled=True)),
            kept_spec,
        )

    def row_total(values):
        return lax.psum(jnp.sum(values, axis=1), "tp")

    forward_mix = featurize(forward_rows)
    backward_mix = featurize(backward_rows)
    forward_z = relayout(forward_mix)[0]
    backward_z, backward_spec = relayout(backward_mix)
    forward_y = forward_rows[:, 0].astype(jnp.float32) * forward_z.astype(jnp.float32)
    backward_q = backward_rows[:, 0].astype(jnp.float32)
    conv_value = backward_z.astype(jnp.float32)
    backward_y = backward_q * conv_value
    weighted = bwd_cot[0].astype(jnp.float32) * gain_row
    forward_scale = lax.rsqrt(row_total(forward_y * forward_y) / model_width + epsilon)[:, None]
    backward_scale = lax.rsqrt(row_total(backward_y * backward_y) / model_width + epsilon)[:, None]
    normed = backward_y * backward_scale
    average = (row_total(weighted * normed) / model_width)[:, None]
    forward_out = (forward_y * forward_scale * gain_row).astype(jnp.bfloat16)
    grad_y = backward_scale * (weighted - normed * average)
    grad_z = (grad_y * backward_q).astype(jnp.bfloat16)
    grad_cols = lax.all_to_all(
        jnp.transpose(grad_z), "ctx", split_axis=0, concat_axis=1, tiled=True
    )
    grad_re, grad_im = spectrum(grad_cols.astype(jnp.float32), tables)
    input_re, input_im = spec_against(grad_re, grad_im, tap_re, tap_im)
    grad_mix_cols = signal_of(input_re, input_im, tables).astype(jnp.bfloat16)
    taps_re, taps_im = spec_against(grad_re, grad_im, backward_spec[0], backward_spec[1])
    filt_step = signal_of(taps_re, taps_im, tables)
    grad_mix = jnp.transpose(
        lax.all_to_all(grad_mix_cols, "ctx", split_axis=1, concat_axis=0, tiled=True)
    ).astype(jnp.float32)
    section_grads = jnp.stack(
        [
            grad_y * conv_value,
            grad_mix * backward_rows[:, 2].astype(jnp.float32),
            grad_mix * backward_rows[:, 1].astype(jnp.float32),
        ],
        axis=1,
    ).astype(jnp.bfloat16)
    section_grads, filt_step = (section_grads, filt_step)
    sent_rows, sent_grads = from_partner((forward_out, section_grads), "pipe", 0)
    return (sent_rows[None], sent_grads[None], filt_step[None, None])


def on_device(fwd_in, bwd_in, bwd_cot, filter_taps, norm_gain):
    length = filter_taps.shape[3]
    if not dense_fits(length):
        return on_device_factored(fwd_in, bwd_in, bwd_cot, filter_taps, norm_gain)
    model_width = norm_gain.shape[1] * lax.axis_size("tp")
    table = real_dft_table(length)
    weights = spectral_weights(length)
    tap_spec = dense_taps_spectrum(filter_taps[0, 0], table)
    tap_scaled = tap_spec * weights
    gain_row = norm_gain[0]
    forward_rows = fwd_in[0]
    backward_rows = bwd_in[0]

    def featurize(proj_rows):
        return (proj_rows[:, 1].astype(jnp.float32) * proj_rows[:, 2].astype(jnp.float32)).astype(
            jnp.bfloat16
        )

    def to_columns(rows):
        return lax.all_to_all(rows, "ctx", split_axis=1, concat_axis=0, tiled=True)

    def to_rows(columns):
        return lax.all_to_all(columns, "ctx", split_axis=0, concat_axis=1, tiled=True)

    def row_total(values):
        return lax.psum(jnp.sum(values, axis=1), "tp")

    partner_kv = from_partner(backward_rows[:, 1:3], "pipe", 0)
    forward_cols = to_columns(featurize(forward_rows))
    backward_cols = to_columns(featurize(backward_rows))
    forward_spec = dense_spectrum_exact(forward_cols, table)
    forward_z = to_rows(
        dense_signal(dense_multiply(forward_spec, tap_scaled, False), table).astype(jnp.bfloat16)
    )
    partner_kv, backward_cols = lax.optimization_barrier((partner_kv, backward_cols))
    backward_spec = dense_spectrum_exact(backward_cols, table)
    backward_z = to_rows(
        dense_signal(dense_multiply(backward_spec, tap_scaled, False), table).astype(jnp.bfloat16)
    )
    forward_y = forward_rows[:, 0].astype(jnp.float32) * forward_z.astype(jnp.float32)
    forward_scale = lax.rsqrt(row_total(forward_y * forward_y) / model_width + epsilon)[:, None]
    forward_out = (forward_y * forward_scale * gain_row).astype(jnp.bfloat16)
    sent_rows = from_partner(forward_out, "pipe", 0)
    backward_q = backward_rows[:, 0].astype(jnp.float32)
    conv_value = backward_z.astype(jnp.float32)
    backward_y = backward_q * conv_value
    weighted = bwd_cot[0].astype(jnp.float32) * gain_row
    backward_scale = lax.rsqrt(row_total(backward_y * backward_y) / model_width + epsilon)[:, None]
    normed = backward_y * backward_scale
    average = (row_total(weighted * normed) / model_width)[:, None]
    grad_y = backward_scale * (weighted - normed * average)
    grad_z = (grad_y * backward_q).astype(jnp.bfloat16)
    sent_first = from_partner((grad_y * conv_value).astype(jnp.bfloat16), "pipe", 0)
    grad_cols = to_columns(grad_z)
    grad_spec = dense_spectrum_exact(grad_cols, table) * weights
    mix_prod = dense_multiply(grad_spec, tap_spec, True)
    width = mix_prod.shape[1] // 2 if mix_prod.shape[1] % 256 == 0 else mix_prod.shape[1]
    pieces = mix_prod.shape[1] // width
    first_cols = dense_signal(mix_prod[:, :width], table).astype(jnp.bfloat16)
    sent_rows, sent_first, first_cols = lax.optimization_barrier((sent_rows, sent_first, first_cols))
    sent_parts = [from_partner(to_rows(first_cols), "pipe", 0)]
    for piece in range(1, pieces):
        piece_cols = dense_signal(mix_prod[:, piece * width : (piece + 1) * width], table)
        sent_parts.append(from_partner(to_rows(piece_cols.astype(jnp.bfloat16)), "pipe", 0))
    taps_prod = dense_multiply(grad_spec, backward_spec, True)
    taps_hi, taps_lo = split_bf16(taps_prod)
    table_hi, table_lo = table
    dims = (((0,), (1,)), ((), ()))
    part = lambda a, b: lax.dot_general(a, b, dims, preferred_element_type=jnp.float32)
    filt_step = part(taps_hi, table_hi) + (part(taps_hi, table_lo) + part(taps_lo, table_hi))
    token_rows = sent_parts[0].shape[0]
    ctx_count = lax.axis_size("ctx")
    sent_mix = jnp.stack(
        [p.reshape(token_rows, ctx_count, width) for p in sent_parts], axis=2
    ).reshape(token_rows, -1).astype(jnp.float32)
    rest = jnp.stack(
        [
            sent_mix * partner_kv[:, 1].astype(jnp.float32),
            sent_mix * partner_kv[:, 0].astype(jnp.float32),
        ],
        axis=1,
    ).astype(jnp.bfloat16)
    sent_grads = jnp.concatenate([sent_first[:, None], rest], axis=1)
    return (sent_rows[None], sent_grads[None], filt_step[None, None])


def solution(mesh):
    return jax.shard_map(
        on_device,
        mesh=mesh,
        in_specs=(
            P("pipe", "ctx", None, "tp"),
            P("pipe", "ctx", None, "tp"),
            P("pipe", "ctx", "tp"),
            P("pipe", "tp", "ctx", None),
            P("pipe", "tp"),
        ),
        out_specs=(
            P("pipe", "ctx", "tp"),
            P("pipe", "ctx", None, "tp"),
            P("pipe", "tp", "ctx", None),
        ),
        check_vma=False,
    )
```

```python
import math

import jax
import jax.numpy as jnp
from jax import lax
from jax.sharding import PartitionSpec as P

epsilon = 1e-06
highest = lax.Precision.HIGHEST


def from_partner(block, axis, bit):
    count = lax.axis_size(axis)
    route = []
    for low in range(count):
        high = low | 1 << bit
        if high != low and high < count:
            route += [(low, high), (high, low)]
    return lax.ppermute(block, axis, route)


def unit_table(count_out, count_in, period):
    product = lax.broadcasted_iota(jnp.int32, (count_out, count_in), 0) * lax.broadcasted_iota(
        jnp.int32, (count_out, count_in), 1
    )
    phase_angle = (product % period).astype(jnp.float32) * (-2.0 * math.pi / period)
    return (jnp.cos(phase_angle), jnp.sin(phase_angle))


def dft_tables(padded):
    blocks = padded // 128
    cos_high, sin_high = unit_table(blocks, blocks, blocks)
    cos_low, sin_low = unit_table(128, 128, 128)
    cos_twist, sin_twist = unit_table(blocks, 128, padded)
    return (cos_high, sin_high, cos_low, sin_low, cos_twist, sin_twist)


def spectrum(signal, tables):
    cos_high, sin_high, cos_low, sin_low, cos_twist, sin_twist = tables
    channels = signal.shape[0]
    half_blocks = signal.shape[1] // 128
    folded = signal.reshape(channels, half_blocks, 128)
    first_re = jnp.einsum("can,ak->ckn", folded, cos_high[:half_blocks], precision=highest)
    first_im = jnp.einsum("can,ak->ckn", folded, sin_high[:half_blocks], precision=highest)
    turned_re = first_re * cos_twist - first_im * sin_twist
    turned_im = first_re * sin_twist + first_im * cos_twist
    spec_re = jnp.einsum("ckn,nj->ckj", turned_re, cos_low, precision=highest) - jnp.einsum(
        "ckn,nj->ckj", turned_im, sin_low, precision=highest
    )
    spec_im = jnp.einsum("ckn,nj->ckj", turned_re, sin_low, precision=highest) + jnp.einsum(
        "ckn,nj->ckj", turned_im, cos_low, precision=highest
    )
    return (spec_re, spec_im)


def signal_of(spec_re, spec_im, tables):
    cos_high, sin_high, cos_low, sin_low, cos_twist, sin_twist = tables
    channels = spec_re.shape[0]
    blocks = spec_re.shape[1]
    half_blocks = blocks // 2
    mid_re = jnp.einsum("ckj,jn->ckn", spec_re, cos_low, precision=highest) + jnp.einsum(
        "ckj,jn->ckn", spec_im, sin_low, precision=highest
    )
    mid_im = jnp.einsum("ckj,jn->ckn", spec_im, cos_low, precision=highest) - jnp.einsum(
        "ckj,jn->ckn", spec_re, sin_low, precision=highest
    )
    back_re = mid_re * cos_twist + mid_im * sin_twist
    back_im = mid_im * cos_twist - mid_re * sin_twist
    values = jnp.einsum(
        "ak,ckn->can", cos_high[:half_blocks], back_re, precision=highest
    ) + jnp.einsum("ak,ckn->can", sin_high[:half_blocks], back_im, precision=highest)
    return values.reshape(channels, half_blocks * 128) / (blocks * 128)


def spec_product(a_re, a_im, b_re, b_im):
    return (a_re * b_re - a_im * b_im, a_re * b_im + a_im * b_re)


def spec_against(a_re, a_im, b_re, b_im):
    return (a_re * b_re + a_im * b_im, a_im * b_re - a_re * b_im)


def split_bf16(values):
    high = lax.reduce_precision(values, exponent_bits=8, mantissa_bits=7)
    return (high.astype(jnp.bfloat16), (values - high).astype(jnp.bfloat16))


def unit_angles(count_rows, count_cols, stride, padded):
    rows = lax.broadcasted_iota(jnp.int32, (count_rows, count_cols), 0) * stride
    cols = lax.broadcasted_iota(jnp.int32, (count_rows, count_cols), 1)
    angle = ((rows * cols) % padded).astype(jnp.float32) * (2.0 * math.pi / padded)
    return (jnp.cos(angle), jnp.sin(angle))


def real_dft_table(length):
    padded = 2 * length
    inner = 1 << (length.bit_length() // 2)
    if length % inner:
        inner = 1
    outer = length // inner
    cos_outer, sin_outer = unit_angles(outer, length, inner, padded)
    cos_inner, sin_inner = unit_angles(inner, length, 1, padded)
    cos_full = (cos_outer[:, None] * cos_inner[None] - sin_outer[:, None] * sin_inner[None]).reshape(
        length, length
    )
    sin_full = (sin_outer[:, None] * cos_inner[None] + cos_outer[:, None] * sin_inner[None]).reshape(
        length, length
    )
    rows = lax.broadcasted_iota(jnp.int32, (length, length), 0)
    cols = lax.broadcasted_iota(jnp.int32, (length, length), 1)
    alternating = jnp.where(rows % 2 == 0, 1.0, -1.0).astype(jnp.float32)
    sin_part = jnp.where(cols == 0, alternating, -sin_full)
    table = jnp.concatenate([cos_full, sin_part], axis=1)
    return split_bf16(table)


def dot_tf(table, signal):
    return lax.dot_general(
        table, signal, (((0,), (0,)), ((), ())), preferred_element_type=jnp.float32
    )


def dot_tt(table, spec):
    return lax.dot_general(
        table, spec, (((1,), (0,)), ((), ())), preferred_element_type=jnp.float32
    )


def dense_spectrum_exact(rows_bf16, table):
    table_hi, table_lo = table
    return dot_tf(table_hi, rows_bf16) + dot_tf(table_lo, rows_bf16)


def dense_signal(spec, table):
    table_hi, table_lo = table
    spec_hi, spec_lo = split_bf16(spec)
    return dot_tt(table_hi, spec_hi) + (dot_tt(table_lo, spec_hi) + dot_tt(table_hi, spec_lo))


def dense_taps_spectrum(taps, table):
    table_hi, table_lo = table
    taps_hi, taps_lo = split_bf16(taps)
    dims = (((0,), (1,)), ((), ()))
    part = lambda a, b: lax.dot_general(a, b, dims, preferred_element_type=jnp.float32)
    return part(table_hi, taps_hi) + (part(table_lo, taps_hi) + part(table_hi, taps_lo))


def spectral_weights(length):
    index = lax.broadcasted_iota(jnp.int32, (2 * length, 1), 0)
    edge = (index == 0) | (index == length)
    return jnp.where(edge, 1.0, 2.0).astype(jnp.float32) / (2 * length)


def dense_multiply(a, b, conjugate):
    length = a.shape[0] // 2
    a_re, a_im = a[:length], a[length:]
    b_re, b_im = b[:length], b[length:]
    first = lax.broadcasted_iota(jnp.int32, (length, 1), 0) == 0
    if conjugate:
        re = a_re * b_re + a_im * b_im
        im = a_im * b_re - a_re * b_im
    else:
        re = a_re * b_re - a_im * b_im
        im = a_re * b_im + a_im * b_re
    re = jnp.where(first, a_re * b_re, re)
    im = jnp.where(first, a_im * b_im, im)
    return jnp.concatenate([re, im], axis=0)


def dense_fits(length):
    return 4 * length * length * 2 <= 16 * 1024 * 1024


def on_device_factored(fwd_in, bwd_in, bwd_cot, filter_taps, norm_gain):
    model_width = norm_gain.shape[1] * lax.axis_size("tp")
    local_taps = filter_taps[0, 0]
    tables = dft_tables(2 * local_taps.shape[1])
    tap_re, tap_im = spectrum(local_taps, tables)
    gain_row = norm_gain[0]
    forward_rows = fwd_in[0]
    backward_rows = bwd_in[0]

    def featurize(proj_rows):
        return (proj_rows[:, 1].astype(jnp.float32) * proj_rows[:, 2].astype(jnp.float32)).astype(
            jnp.bfloat16
        )

    def convolve(columns):
        sig_re, sig_im = spectrum(columns.astype(jnp.float32), tables)
        prod_re, prod_im = spec_product(sig_re, sig_im, tap_re, tap_im)
        return (signal_of(prod_re, prod_im, tables).astype(jnp.bfloat16), (sig_re, sig_im))

    def relayout(mixed_rows):
        columns = lax.all_to_all(
            jnp.transpose(mixed_rows), "ctx", split_axis=0, concat_axis=1, tiled=True
        )
        result, kept_spec = convolve(columns)
        return (
            jnp.transpose(lax.all_to_all(result, "ctx", split_axis=1, concat_axis=0, tiled=True)),
            kept_spec,
        )

    def row_total(values):
        return lax.psum(jnp.sum(values, axis=1), "tp")

    forward_mix = featurize(forward_rows)
    backward_mix = featurize(backward_rows)
    forward_z = relayout(forward_mix)[0]
    backward_z, backward_spec = relayout(backward_mix)
    forward_y = forward_rows[:, 0].astype(jnp.float32) * forward_z.astype(jnp.float32)
    backward_q = backward_rows[:, 0].astype(jnp.float32)
    conv_value = backward_z.astype(jnp.float32)
    backward_y = backward_q * conv_value
    weighted = bwd_cot[0].astype(jnp.float32) * gain_row
    forward_scale = lax.rsqrt(row_total(forward_y * forward_y) / model_width + epsilon)[:, None]
    backward_scale = lax.rsqrt(row_total(backward_y * backward_y) / model_width + epsilon)[:, None]
    normed = backward_y * backward_scale
    average = (row_total(weighted * normed) / model_width)[:, None]
    forward_out = (forward_y * forward_scale * gain_row).astype(jnp.bfloat16)
    grad_y = backward_scale * (weighted - normed * average)
    grad_z = (grad_y * backward_q).astype(jnp.bfloat16)
    grad_cols = lax.all_to_all(
        jnp.transpose(grad_z), "ctx", split_axis=0, concat_axis=1, tiled=True
    )
    grad_re, grad_im = spectrum(grad_cols.astype(jnp.float32), tables)
    input_re, input_im = spec_against(grad_re, grad_im, tap_re, tap_im)
    grad_mix_cols = signal_of(input_re, input_im, tables).astype(jnp.bfloat16)
    taps_re, taps_im = spec_against(grad_re, grad_im, backward_spec[0], backward_spec[1])
    filt_step = signal_of(taps_re, taps_im, tables)
    grad_mix = jnp.transpose(
        lax.all_to_all(grad_mix_cols, "ctx", split_axis=1, concat_axis=0, tiled=True)
    ).astype(jnp.float32)
    section_grads = jnp.stack(
        [
            grad_y * conv_value,
            grad_mix * backward_rows[:, 2].astype(jnp.float32),
            grad_mix * backward_rows[:, 1].astype(jnp.float32),
        ],
        axis=1,
    ).astype(jnp.bfloat16)
    section_grads, filt_step = (section_grads, filt_step)
    sent_rows, sent_grads = from_partner((forward_out, section_grads), "pipe", 0)
    return (sent_rows[None], sent_grads[None], filt_step[None, None])


def on_device(fwd_in, bwd_in, bwd_cot, filter_taps, norm_gain):
    length = filter_taps.shape[3]
    if not dense_fits(length):
        return on_device_factored(fwd_in, bwd_in, bwd_cot, filter_taps, norm_gain)
    model_width = norm_gain.shape[1] * lax.axis_size("tp")
    table = real_dft_table(length)
    weights = spectral_weights(length)
    tap_spec = dense_taps_spectrum(filter_taps[0, 0], table)
    tap_scaled = tap_spec * weights
    gain_row = norm_gain[0]
    forward_rows = fwd_in[0]
    backward_rows = bwd_in[0]

    def featurize(proj_rows):
        return (proj_rows[:, 1].astype(jnp.float32) * proj_rows[:, 2].astype(jnp.float32)).astype(
            jnp.bfloat16
        )

    def to_columns(rows):
        return lax.all_to_all(rows, "ctx", split_axis=1, concat_axis=0, tiled=True)

    def to_rows(columns):
        return lax.all_to_all(columns, "ctx", split_axis=0, concat_axis=1, tiled=True)

    def row_total(values):
        return lax.psum(jnp.sum(values, axis=1), "tp")

    partner_kv = from_partner(backward_rows[:, 1:3], "pipe", 0)
    forward_cols = to_columns(featurize(forward_rows))
    backward_cols = to_columns(featurize(backward_rows))
    partner_kv, backward_cols = lax.optimization_barrier((partner_kv, backward_cols))
    backward_spec = dense_spectrum_exact(backward_cols, table)
    backward_z = to_rows(
        dense_signal(dense_multiply(backward_spec, tap_scaled, False), table).astype(jnp.bfloat16)
    )
    backward_q = backward_rows[:, 0].astype(jnp.float32)
    conv_value = backward_z.astype(jnp.float32)
    backward_y = backward_q * conv_value
    weighted = bwd_cot[0].astype(jnp.float32) * gain_row
    backward_scale = lax.rsqrt(row_total(backward_y * backward_y) / model_width + epsilon)[:, None]
    normed = backward_y * backward_scale
    average = (row_total(weighted * normed) / model_width)[:, None]
    grad_y = backward_scale * (weighted - normed * average)
    grad_z = (grad_y * backward_q).astype(jnp.bfloat16)
    sent_first = from_partner((grad_y * conv_value).astype(jnp.bfloat16), "pipe", 0)
    grad_cols = to_columns(grad_z)
    forward_cols, grad_z = lax.optimization_barrier((forward_cols, grad_z))
    forward_spec = dense_spectrum_exact(forward_cols, table)
    forward_z = to_rows(
        dense_signal(dense_multiply(forward_spec, tap_scaled, False), table).astype(jnp.bfloat16)
    )
    forward_y = forward_rows[:, 0].astype(jnp.float32) * forward_z.astype(jnp.float32)
    forward_scale = lax.rsqrt(row_total(forward_y * forward_y) / model_width + epsilon)[:, None]
    forward_out = (forward_y * forward_scale * gain_row).astype(jnp.bfloat16)
    sent_rows = from_partner(forward_out, "pipe", 0)
    grad_spec = dense_spectrum_exact(grad_cols, table) * weights
    mix_prod = dense_multiply(grad_spec, tap_spec, True)
    width = mix_prod.shape[1] // 2 if mix_prod.shape[1] % 256 == 0 else mix_prod.shape[1]
    pieces = mix_prod.shape[1] // width
    first_cols = dense_signal(mix_prod[:, :width], table).astype(jnp.bfloat16)
    sent_first, first_cols = lax.optimization_barrier((sent_first, first_cols))
    sent_parts = [from_partner(to_rows(first_cols), "pipe", 0)]
    for piece in range(1, pieces):
        piece_cols = dense_signal(mix_prod[:, piece * width : (piece + 1) * width], table)
        piece_rows = to_rows(piece_cols.astype(jnp.bfloat16))
        sent_rows, piece_rows = lax.optimization_barrier((sent_rows, piece_rows))
        sent_parts.append(from_partner(piece_rows, "pipe", 0))
    taps_prod = dense_multiply(grad_spec, backward_spec, True)
    taps_hi, taps_lo = split_bf16(taps_prod)
    table_hi, table_lo = table
    dims = (((0,), (1,)), ((), ()))
    part = lambda a, b: lax.dot_general(a, b, dims, preferred_element_type=jnp.float32)
    filt_step = part(taps_hi, table_hi) + (part(taps_hi, table_lo) + part(taps_lo, table_hi))
    token_rows = sent_parts[0].shape[0]
    ctx_count = lax.axis_size("ctx")
    sent_mix = jnp.stack(
        [p.reshape(token_rows, ctx_count, width) for p in sent_parts], axis=2
    ).reshape(token_rows, -1).astype(jnp.float32)
    rest = jnp.stack(
        [
            sent_mix * partner_kv[:, 1].astype(jnp.float32),
            sent_mix * partner_kv[:, 0].astype(jnp.float32),
        ],
        axis=1,
    ).astype(jnp.bfloat16)
    sent_grads = jnp.concatenate([sent_first[:, None], rest], axis=1)
    return (sent_rows[None], sent_grads[None], filt_step[None, None])


def solution(mesh):
    return jax.shard_map(
        on_device,
        mesh=mesh,
        in_specs=(
            P("pipe", "ctx", None, "tp"),
            P("pipe", "ctx", None, "tp"),
            P("pipe", "ctx", "tp"),
            P("pipe", "tp", "ctx", None),
            P("pipe", "tp"),
        ),
        out_specs=(
            P("pipe", "ctx", "tp"),
            P("pipe", "ctx", None, "tp"),
            P("pipe", "tp", "ctx", None),
        ),
        check_vma=False,
    )
```

```python
import math

import jax
import ml_dtypes
import numpy as np
import jax.numpy as jnp
from jax import lax
from jax.sharding import PartitionSpec as P

epsilon = 1e-06
highest = lax.Precision.HIGHEST


def from_partner(block, axis, bit):
    count = lax.axis_size(axis)
    route = []
    for low in range(count):
        high = low | 1 << bit
        if high != low and high < count:
            route += [(low, high), (high, low)]
    return lax.ppermute(block, axis, route)


def unit_table(count_out, count_in, period):
    product = lax.broadcasted_iota(jnp.int32, (count_out, count_in), 0) * lax.broadcasted_iota(
        jnp.int32, (count_out, count_in), 1
    )
    phase_angle = (product % period).astype(jnp.float32) * (-2.0 * math.pi / period)
    return (jnp.cos(phase_angle), jnp.sin(phase_angle))


def dft_tables(padded):
    blocks = padded // 128
    cos_high, sin_high = unit_table(blocks, blocks, blocks)
    cos_low, sin_low = unit_table(128, 128, 128)
    cos_twist, sin_twist = unit_table(blocks, 128, padded)
    return (cos_high, sin_high, cos_low, sin_low, cos_twist, sin_twist)


def spectrum(signal, tables):
    cos_high, sin_high, cos_low, sin_low, cos_twist, sin_twist = tables
    channels = signal.shape[0]
    half_blocks = signal.shape[1] // 128
    folded = signal.reshape(channels, half_blocks, 128)
    first_re = jnp.einsum("can,ak->ckn", folded, cos_high[:half_blocks], precision=highest)
    first_im = jnp.einsum("can,ak->ckn", folded, sin_high[:half_blocks], precision=highest)
    turned_re = first_re * cos_twist - first_im * sin_twist
    turned_im = first_re * sin_twist + first_im * cos_twist
    spec_re = jnp.einsum("ckn,nj->ckj", turned_re, cos_low, precision=highest) - jnp.einsum(
        "ckn,nj->ckj", turned_im, sin_low, precision=highest
    )
    spec_im = jnp.einsum("ckn,nj->ckj", turned_re, sin_low, precision=highest) + jnp.einsum(
        "ckn,nj->ckj", turned_im, cos_low, precision=highest
    )
    return (spec_re, spec_im)


def signal_of(spec_re, spec_im, tables):
    cos_high, sin_high, cos_low, sin_low, cos_twist, sin_twist = tables
    channels = spec_re.shape[0]
    blocks = spec_re.shape[1]
    half_blocks = blocks // 2
    mid_re = jnp.einsum("ckj,jn->ckn", spec_re, cos_low, precision=highest) + jnp.einsum(
        "ckj,jn->ckn", spec_im, sin_low, precision=highest
    )
    mid_im = jnp.einsum("ckj,jn->ckn", spec_im, cos_low, precision=highest) - jnp.einsum(
        "ckj,jn->ckn", spec_re, sin_low, precision=highest
    )
    back_re = mid_re * cos_twist + mid_im * sin_twist
    back_im = mid_im * cos_twist - mid_re * sin_twist
    values = jnp.einsum(
        "ak,ckn->can", cos_high[:half_blocks], back_re, precision=highest
    ) + jnp.einsum("ak,ckn->can", sin_high[:half_blocks], back_im, precision=highest)
    return values.reshape(channels, half_blocks * 128) / (blocks * 128)


def spec_product(a_re, a_im, b_re, b_im):
    return (a_re * b_re - a_im * b_im, a_re * b_im + a_im * b_re)


def spec_against(a_re, a_im, b_re, b_im):
    return (a_re * b_re + a_im * b_im, a_im * b_re - a_re * b_im)


def split_bf16(values):
    high = lax.reduce_precision(values, exponent_bits=8, mantissa_bits=7)
    return (high.astype(jnp.bfloat16), (values - high).astype(jnp.bfloat16))


def unit_angles(count_rows, count_cols, stride, padded):
    rows = lax.broadcasted_iota(jnp.int32, (count_rows, count_cols), 0) * stride
    cols = lax.broadcasted_iota(jnp.int32, (count_rows, count_cols), 1)
    angle = ((rows * cols) % padded).astype(jnp.float32) * (2.0 * math.pi / padded)
    return (jnp.cos(angle), jnp.sin(angle))


def real_dft_table(length):
    padded = 2 * length
    inner = 1 << (length.bit_length() // 2)
    if length % inner:
        inner = 1
    outer = length // inner
    cos_outer, sin_outer = unit_angles(outer, length, inner, padded)
    cos_inner, sin_inner = unit_angles(inner, length, 1, padded)
    cos_full = (cos_outer[:, None] * cos_inner[None] - sin_outer[:, None] * sin_inner[None]).reshape(
        length, length
    )
    sin_full = (sin_outer[:, None] * cos_inner[None] + cos_outer[:, None] * sin_inner[None]).reshape(
        length, length
    )
    rows = lax.broadcasted_iota(jnp.int32, (length, length), 0)
    cols = lax.broadcasted_iota(jnp.int32, (length, length), 1)
    alternating = jnp.where(rows % 2 == 0, 1.0, -1.0).astype(jnp.float32)
    sin_part = jnp.where(cols == 0, alternating, -sin_full)
    table = jnp.concatenate([cos_full, sin_part], axis=1)
    return split_bf16(table)


def constant_dft_table(length):
    padded = 2 * length
    rows = np.arange(length, dtype=np.int64)[:, None]
    cols = np.arange(length, dtype=np.int64)[None, :]
    angle = ((rows * cols) % padded).astype(np.float64) * (2.0 * np.pi / padded)
    alternating = np.where(rows % 2 == 0, 1.0, -1.0)
    sin_part = np.where(cols == 0, alternating, -np.sin(angle))
    table = np.concatenate([np.cos(angle), sin_part], axis=1).astype(np.float32)
    high = table.astype(ml_dtypes.bfloat16)
    low = (table - high.astype(np.float32)).astype(ml_dtypes.bfloat16)
    return (jnp.asarray(high), jnp.asarray(low))


def dot_tf(table, signal):
    return lax.dot_general(
        table, signal, (((0,), (0,)), ((), ())), preferred_element_type=jnp.float32
    )


def dot_tt(table, spec):
    return lax.dot_general(
        table, spec, (((1,), (0,)), ((), ())), preferred_element_type=jnp.float32
    )


def dense_spectrum_exact(rows_bf16, table):
    table_hi, table_lo = table
    return dot_tf(table_hi, rows_bf16) + dot_tf(table_lo, rows_bf16)


def dense_signal(spec, table):
    table_hi, table_lo = table
    spec_hi, spec_lo = split_bf16(spec)
    return dot_tt(table_hi, spec_hi) + (dot_tt(table_lo, spec_hi) + dot_tt(table_hi, spec_lo))


def dense_taps_spectrum(taps, table):
    table_hi, table_lo = table
    taps_hi, taps_lo = split_bf16(taps)
    dims = (((0,), (1,)), ((), ()))
    part = lambda a, b: lax.dot_general(a, b, dims, preferred_element_type=jnp.float32)
    return part(table_hi, taps_hi) + (part(table_lo, taps_hi) + part(table_hi, taps_lo))


def spectral_weights(length):
    index = lax.broadcasted_iota(jnp.int32, (2 * length, 1), 0)
    edge = (index == 0) | (index == length)
    return jnp.where(edge, 1.0, 2.0).astype(jnp.float32) / (2 * length)


def dense_multiply(a, b, conjugate):
    length = a.shape[0] // 2
    a_re, a_im = a[:length], a[length:]
    b_re, b_im = b[:length], b[length:]
    first = lax.broadcasted_iota(jnp.int32, (length, 1), 0) == 0
    if conjugate:
        re = a_re * b_re + a_im * b_im
        im = a_im * b_re - a_re * b_im
    else:
        re = a_re * b_re - a_im * b_im
        im = a_re * b_im + a_im * b_re
    re = jnp.where(first, a_re * b_re, re)
    im = jnp.where(first, a_im * b_im, im)
    return jnp.concatenate([re, im], axis=0)


def dense_fits(length):
    return 4 * length * length * 2 <= 16 * 1024 * 1024


def on_device_factored(fwd_in, bwd_in, bwd_cot, filter_taps, norm_gain):
    model_width = norm_gain.shape[1] * lax.axis_size("tp")
    local_taps = filter_taps[0, 0]
    tables = dft_tables(2 * local_taps.shape[1])
    tap_re, tap_im = spectrum(local_taps, tables)
    gain_row = norm_gain[0]
    forward_rows = fwd_in[0]
    backward_rows = bwd_in[0]

    def featurize(proj_rows):
        return (proj_rows[:, 1].astype(jnp.float32) * proj_rows[:, 2].astype(jnp.float32)).astype(
            jnp.bfloat16
        )

    def convolve(columns):
        sig_re, sig_im = spectrum(columns.astype(jnp.float32), tables)
        prod_re, prod_im = spec_product(sig_re, sig_im, tap_re, tap_im)
        return (signal_of(prod_re, prod_im, tables).astype(jnp.bfloat16), (sig_re, sig_im))

    def relayout(mixed_rows):
        columns = lax.all_to_all(
            jnp.transpose(mixed_rows), "ctx", split_axis=0, concat_axis=1, tiled=True
        )
        result, kept_spec = convolve(columns)
        return (
            jnp.transpose(lax.all_to_all(result, "ctx", split_axis=1, concat_axis=0, tiled=True)),
            kept_spec,
        )

    def row_total(values):
        return lax.psum(jnp.sum(values, axis=1), "tp")

    forward_mix = featurize(forward_rows)
    backward_mix = featurize(backward_rows)
    forward_z = relayout(forward_mix)[0]
    backward_z, backward_spec = relayout(backward_mix)
    forward_y = forward_rows[:, 0].astype(jnp.float32) * forward_z.astype(jnp.float32)
    backward_q = backward_rows[:, 0].astype(jnp.float32)
    conv_value = backward_z.astype(jnp.float32)
    backward_y = backward_q * conv_value
    weighted = bwd_cot[0].astype(jnp.float32) * gain_row
    forward_scale = lax.rsqrt(row_total(forward_y * forward_y) / model_width + epsilon)[:, None]
    backward_scale = lax.rsqrt(row_total(backward_y * backward_y) / model_width + epsilon)[:, None]
    normed = backward_y * backward_scale
    average = (row_total(weighted * normed) / model_width)[:, None]
    forward_out = (forward_y * forward_scale * gain_row).astype(jnp.bfloat16)
    grad_y = backward_scale * (weighted - normed * average)
    grad_z = (grad_y * backward_q).astype(jnp.bfloat16)
    grad_cols = lax.all_to_all(
        jnp.transpose(grad_z), "ctx", split_axis=0, concat_axis=1, tiled=True
    )
    grad_re, grad_im = spectrum(grad_cols.astype(jnp.float32), tables)
    input_re, input_im = spec_against(grad_re, grad_im, tap_re, tap_im)
    grad_mix_cols = signal_of(input_re, input_im, tables).astype(jnp.bfloat16)
    taps_re, taps_im = spec_against(grad_re, grad_im, backward_spec[0], backward_spec[1])
    filt_step = signal_of(taps_re, taps_im, tables)
    grad_mix = jnp.transpose(
        lax.all_to_all(grad_mix_cols, "ctx", split_axis=1, concat_axis=0, tiled=True)
    ).astype(jnp.float32)
    section_grads = jnp.stack(
        [
            grad_y * conv_value,
            grad_mix * backward_rows[:, 2].astype(jnp.float32),
            grad_mix * backward_rows[:, 1].astype(jnp.float32),
        ],
        axis=1,
    ).astype(jnp.bfloat16)
    section_grads, filt_step = (section_grads, filt_step)
    sent_rows, sent_grads = from_partner((forward_out, section_grads), "pipe", 0)
    return (sent_rows[None], sent_grads[None], filt_step[None, None])


def on_device(fwd_in, bwd_in, bwd_cot, filter_taps, norm_gain):
    length = filter_taps.shape[3]
    if not dense_fits(length):
        return on_device_factored(fwd_in, bwd_in, bwd_cot, filter_taps, norm_gain)
    model_width = norm_gain.shape[1] * lax.axis_size("tp")
    table = constant_dft_table(length)
    weights = spectral_weights(length)
    tap_spec = dense_taps_spectrum(filter_taps[0, 0], table)
    tap_scaled = tap_spec * weights
    gain_row = norm_gain[0]
    forward_rows = fwd_in[0]
    backward_rows = bwd_in[0]

    def featurize(proj_rows):
        return (proj_rows[:, 1].astype(jnp.float32) * proj_rows[:, 2].astype(jnp.float32)).astype(
            jnp.bfloat16
        )

    def to_columns(rows):
        return lax.all_to_all(rows, "ctx", split_axis=1, concat_axis=0, tiled=True)

    def to_rows(columns):
        return lax.all_to_all(columns, "ctx", split_axis=0, concat_axis=1, tiled=True)

    def row_total(values):
        return lax.psum(jnp.sum(values, axis=1), "tp")

    partner_kv = from_partner(backward_rows[:, 1:3], "pipe", 0)
    forward_cols = to_columns(featurize(forward_rows))
    backward_cols = to_columns(featurize(backward_rows))
    forward_spec = dense_spectrum_exact(forward_cols, table)
    forward_z = to_rows(
        dense_signal(dense_multiply(forward_spec, tap_scaled, False), table).astype(jnp.bfloat16)
    )
    partner_kv, backward_cols = lax.optimization_barrier((partner_kv, backward_cols))
    backward_spec = dense_spectrum_exact(backward_cols, table)
    backward_z = to_rows(
        dense_signal(dense_multiply(backward_spec, tap_scaled, False), table).astype(jnp.bfloat16)
    )
    forward_y = forward_rows[:, 0].astype(jnp.float32) * forward_z.astype(jnp.float32)
    forward_scale = lax.rsqrt(row_total(forward_y * forward_y) / model_width + epsilon)[:, None]
    forward_out = (forward_y * forward_scale * gain_row).astype(jnp.bfloat16)
    sent_rows = from_partner(forward_out, "pipe", 0)
    backward_q = backward_rows[:, 0].astype(jnp.float32)
    conv_value = backward_z.astype(jnp.float32)
    backward_y = backward_q * conv_value
    weighted = bwd_cot[0].astype(jnp.float32) * gain_row
    backward_scale = lax.rsqrt(row_total(backward_y * backward_y) / model_width + epsilon)[:, None]
    normed = backward_y * backward_scale
    average = (row_total(weighted * normed) / model_width)[:, None]
    grad_y = backward_scale * (weighted - normed * average)
    grad_z = (grad_y * backward_q).astype(jnp.bfloat16)
    sent_first = from_partner((grad_y * conv_value).astype(jnp.bfloat16), "pipe", 0)
    grad_cols = to_columns(grad_z)
    grad_spec = dense_spectrum_exact(grad_cols, table) * weights
    mix_prod = dense_multiply(grad_spec, tap_spec, True)
    width = mix_prod.shape[1] // 2 if mix_prod.shape[1] % 256 == 0 else mix_prod.shape[1]
    pieces = mix_prod.shape[1] // width
    first_cols = dense_signal(mix_prod[:, :width], table).astype(jnp.bfloat16)
    sent_rows, sent_first, first_cols = lax.optimization_barrier((sent_rows, sent_first, first_cols))
    sent_parts = [from_partner(to_rows(first_cols), "pipe", 0)]
    for piece in range(1, pieces):
        piece_cols = dense_signal(mix_prod[:, piece * width : (piece + 1) * width], table)
        sent_parts.append(from_partner(to_rows(piece_cols.astype(jnp.bfloat16)), "pipe", 0))
    taps_prod = dense_multiply(grad_spec, backward_spec, True)
    taps_hi, taps_lo = split_bf16(taps_prod)
    table_hi, table_lo = table
    dims = (((0,), (1,)), ((), ()))
    part = lambda a, b: lax.dot_general(a, b, dims, preferred_element_type=jnp.float32)
    filt_step = part(taps_hi, table_hi) + (part(taps_hi, table_lo) + part(taps_lo, table_hi))
    token_rows = sent_parts[0].shape[0]
    ctx_count = lax.axis_size("ctx")
    sent_mix = jnp.stack(
        [p.reshape(token_rows, ctx_count, width) for p in sent_parts], axis=2
    ).reshape(token_rows, -1).astype(jnp.float32)
    rest = jnp.stack(
        [
            sent_mix * partner_kv[:, 1].astype(jnp.float32),
            sent_mix * partner_kv[:, 0].astype(jnp.float32),
        ],
        axis=1,
    ).astype(jnp.bfloat16)
    sent_grads = jnp.concatenate([sent_first[:, None], rest], axis=1)
    return (sent_rows[None], sent_grads[None], filt_step[None, None])


def solution(mesh):
    return jax.shard_map(
        on_device,
        mesh=mesh,
        in_specs=(
            P("pipe", "ctx", None, "tp"),
            P("pipe", "ctx", None, "tp"),
            P("pipe", "ctx", "tp"),
            P("pipe", "tp", "ctx", None),
            P("pipe", "tp"),
        ),
        out_specs=(
            P("pipe", "ctx", "tp"),
            P("pipe", "ctx", None, "tp"),
            P("pipe", "tp", "ctx", None),
        ),
        check_vma=False,
    )
```

```python
import math

import jax
import ml_dtypes
import numpy as np
import jax.numpy as jnp
from jax import lax
from jax.sharding import PartitionSpec as P

epsilon = 1e-06
highest = lax.Precision.HIGHEST


def from_partner(block, axis, bit):
    count = lax.axis_size(axis)
    route = []
    for low in range(count):
        high = low | 1 << bit
        if high != low and high < count:
            route += [(low, high), (high, low)]
    return lax.ppermute(block, axis, route)


def unit_table(count_out, count_in, period):
    product = lax.broadcasted_iota(jnp.int32, (count_out, count_in), 0) * lax.broadcasted_iota(
        jnp.int32, (count_out, count_in), 1
    )
    phase_angle = (product % period).astype(jnp.float32) * (-2.0 * math.pi / period)
    return (jnp.cos(phase_angle), jnp.sin(phase_angle))


def dft_tables(padded):
    blocks = padded // 128
    cos_high, sin_high = unit_table(blocks, blocks, blocks)
    cos_low, sin_low = unit_table(128, 128, 128)
    cos_twist, sin_twist = unit_table(blocks, 128, padded)
    return (cos_high, sin_high, cos_low, sin_low, cos_twist, sin_twist)


def spectrum(signal, tables):
    cos_high, sin_high, cos_low, sin_low, cos_twist, sin_twist = tables
    channels = signal.shape[0]
    half_blocks = signal.shape[1] // 128
    folded = signal.reshape(channels, half_blocks, 128)
    first_re = jnp.einsum("can,ak->ckn", folded, cos_high[:half_blocks], precision=highest)
    first_im = jnp.einsum("can,ak->ckn", folded, sin_high[:half_blocks], precision=highest)
    turned_re = first_re * cos_twist - first_im * sin_twist
    turned_im = first_re * sin_twist + first_im * cos_twist
    spec_re = jnp.einsum("ckn,nj->ckj", turned_re, cos_low, precision=highest) - jnp.einsum(
        "ckn,nj->ckj", turned_im, sin_low, precision=highest
    )
    spec_im = jnp.einsum("ckn,nj->ckj", turned_re, sin_low, precision=highest) + jnp.einsum(
        "ckn,nj->ckj", turned_im, cos_low, precision=highest
    )
    return (spec_re, spec_im)


def signal_of(spec_re, spec_im, tables):
    cos_high, sin_high, cos_low, sin_low, cos_twist, sin_twist = tables
    channels = spec_re.shape[0]
    blocks = spec_re.shape[1]
    half_blocks = blocks // 2
    mid_re = jnp.einsum("ckj,jn->ckn", spec_re, cos_low, precision=highest) + jnp.einsum(
        "ckj,jn->ckn", spec_im, sin_low, precision=highest
    )
    mid_im = jnp.einsum("ckj,jn->ckn", spec_im, cos_low, precision=highest) - jnp.einsum(
        "ckj,jn->ckn", spec_re, sin_low, precision=highest
    )
    back_re = mid_re * cos_twist + mid_im * sin_twist
    back_im = mid_im * cos_twist - mid_re * sin_twist
    values = jnp.einsum(
        "ak,ckn->can", cos_high[:half_blocks], back_re, precision=highest
    ) + jnp.einsum("ak,ckn->can", sin_high[:half_blocks], back_im, precision=highest)
    return values.reshape(channels, half_blocks * 128) / (blocks * 128)


def spec_product(a_re, a_im, b_re, b_im):
    return (a_re * b_re - a_im * b_im, a_re * b_im + a_im * b_re)


def spec_against(a_re, a_im, b_re, b_im):
    return (a_re * b_re + a_im * b_im, a_im * b_re - a_re * b_im)


def split_bf16(values):
    high = lax.reduce_precision(values, exponent_bits=8, mantissa_bits=7)
    return (high.astype(jnp.bfloat16), (values - high).astype(jnp.bfloat16))


def unit_angles(count_rows, count_cols, stride, padded):
    rows = lax.broadcasted_iota(jnp.int32, (count_rows, count_cols), 0) * stride
    cols = lax.broadcasted_iota(jnp.int32, (count_rows, count_cols), 1)
    angle = ((rows * cols) % padded).astype(jnp.float32) * (2.0 * math.pi / padded)
    return (jnp.cos(angle), jnp.sin(angle))


def real_dft_table(length):
    padded = 2 * length
    inner = 1 << (length.bit_length() // 2)
    if length % inner:
        inner = 1
    outer = length // inner
    cos_outer, sin_outer = unit_angles(outer, length, inner, padded)
    cos_inner, sin_inner = unit_angles(inner, length, 1, padded)
    cos_full = (cos_outer[:, None] * cos_inner[None] - sin_outer[:, None] * sin_inner[None]).reshape(
        length, length
    )
    sin_full = (sin_outer[:, None] * cos_inner[None] + cos_outer[:, None] * sin_inner[None]).reshape(
        length, length
    )
    rows = lax.broadcasted_iota(jnp.int32, (length, length), 0)
    cols = lax.broadcasted_iota(jnp.int32, (length, length), 1)
    alternating = jnp.where(rows % 2 == 0, 1.0, -1.0).astype(jnp.float32)
    sin_part = jnp.where(cols == 0, alternating, -sin_full)
    table = jnp.concatenate([cos_full, sin_part], axis=1)
    return split_bf16(table)


def constant_dft_table(length):
    padded = 2 * length
    rows = np.arange(length, dtype=np.int64)[:, None]
    cols = np.arange(length, dtype=np.int64)[None, :]
    angle = ((rows * cols) % padded).astype(np.float64) * (2.0 * np.pi / padded)
    alternating = np.where(rows % 2 == 0, 1.0, -1.0)
    sin_part = np.where(cols == 0, alternating, -np.sin(angle))
    table = np.concatenate([np.cos(angle), sin_part], axis=1).astype(np.float32)
    high = table.astype(ml_dtypes.bfloat16)
    low = (table - high.astype(np.float32)).astype(ml_dtypes.bfloat16)
    return (jnp.asarray(high), jnp.asarray(low))


def dot_tf(table, signal):
    return lax.dot_general(
        table, signal, (((0,), (0,)), ((), ())), preferred_element_type=jnp.float32
    )


def dot_tt(table, spec):
    return lax.dot_general(
        table, spec, (((1,), (0,)), ((), ())), preferred_element_type=jnp.float32
    )


def dense_spectrum_exact(rows_bf16, table):
    table_hi, table_lo = table
    return dot_tf(table_hi, rows_bf16) + dot_tf(table_lo, rows_bf16)


def dense_signal(spec, table):
    table_hi, table_lo = table
    spec_hi, spec_lo = split_bf16(spec)
    return dot_tt(table_hi, spec_hi) + (dot_tt(table_lo, spec_hi) + dot_tt(table_hi, spec_lo))


def dense_taps_spectrum(taps, table):
    table_hi, table_lo = table
    taps_hi, taps_lo = split_bf16(taps)
    dims = (((0,), (1,)), ((), ()))
    part = lambda a, b: lax.dot_general(a, b, dims, preferred_element_type=jnp.float32)
    return part(table_hi, taps_hi) + (part(table_lo, taps_hi) + part(table_hi, taps_lo))


def spectral_weights(length):
    index = lax.broadcasted_iota(jnp.int32, (2 * length, 1), 0)
    edge = (index == 0) | (index == length)
    return jnp.where(edge, 1.0, 2.0).astype(jnp.float32) / (2 * length)


def dense_multiply(a, b, conjugate):
    length = a.shape[0] // 2
    a_re, a_im = a[:length], a[length:]
    b_re, b_im = b[:length], b[length:]
    first = lax.broadcasted_iota(jnp.int32, (length, 1), 0) == 0
    if conjugate:
        re = a_re * b_re + a_im * b_im
        im = a_im * b_re - a_re * b_im
    else:
        re = a_re * b_re - a_im * b_im
        im = a_re * b_im + a_im * b_re
    re = jnp.where(first, a_re * b_re, re)
    im = jnp.where(first, a_im * b_im, im)
    return jnp.concatenate([re, im], axis=0)


def dense_fits(length):
    return 4 * length * length * 2 <= 16 * 1024 * 1024


def on_device_factored(fwd_in, bwd_in, bwd_cot, filter_taps, norm_gain):
    model_width = norm_gain.shape[1] * lax.axis_size("tp")
    local_taps = filter_taps[0, 0]
    tables = dft_tables(2 * local_taps.shape[1])
    tap_re, tap_im = spectrum(local_taps, tables)
    gain_row = norm_gain[0]
    forward_rows = fwd_in[0]
    backward_rows = bwd_in[0]

    def featurize(proj_rows):
        return (proj_rows[:, 1].astype(jnp.float32) * proj_rows[:, 2].astype(jnp.float32)).astype(
            jnp.bfloat16
        )

    def convolve(columns):
        sig_re, sig_im = spectrum(columns.astype(jnp.float32), tables)
        prod_re, prod_im = spec_product(sig_re, sig_im, tap_re, tap_im)
        return (signal_of(prod_re, prod_im, tables).astype(jnp.bfloat16), (sig_re, sig_im))

    def relayout(mixed_rows):
        columns = lax.all_to_all(
            jnp.transpose(mixed_rows), "ctx", split_axis=0, concat_axis=1, tiled=True
        )
        result, kept_spec = convolve(columns)
        return (
            jnp.transpose(lax.all_to_all(result, "ctx", split_axis=1, concat_axis=0, tiled=True)),
            kept_spec,
        )

    def row_total(values):
        return lax.psum(jnp.sum(values, axis=1), "tp")

    forward_mix = featurize(forward_rows)
    backward_mix = featurize(backward_rows)
    forward_z = relayout(forward_mix)[0]
    backward_z, backward_spec = relayout(backward_mix)
    forward_y = forward_rows[:, 0].astype(jnp.float32) * forward_z.astype(jnp.float32)
    backward_q = backward_rows[:, 0].astype(jnp.float32)
    conv_value = backward_z.astype(jnp.float32)
    backward_y = backward_q * conv_value
    weighted = bwd_cot[0].astype(jnp.float32) * gain_row
    forward_scale = lax.rsqrt(row_total(forward_y * forward_y) / model_width + epsilon)[:, None]
    backward_scale = lax.rsqrt(row_total(backward_y * backward_y) / model_width + epsilon)[:, None]
    normed = backward_y * backward_scale
    average = (row_total(weighted * normed) / model_width)[:, None]
    forward_out = (forward_y * forward_scale * gain_row).astype(jnp.bfloat16)
    grad_y = backward_scale * (weighted - normed * average)
    grad_z = (grad_y * backward_q).astype(jnp.bfloat16)
    grad_cols = lax.all_to_all(
        jnp.transpose(grad_z), "ctx", split_axis=0, concat_axis=1, tiled=True
    )
    grad_re, grad_im = spectrum(grad_cols.astype(jnp.float32), tables)
    input_re, input_im = spec_against(grad_re, grad_im, tap_re, tap_im)
    grad_mix_cols = signal_of(input_re, input_im, tables).astype(jnp.bfloat16)
    taps_re, taps_im = spec_against(grad_re, grad_im, backward_spec[0], backward_spec[1])
    filt_step = signal_of(taps_re, taps_im, tables)
    grad_mix = jnp.transpose(
        lax.all_to_all(grad_mix_cols, "ctx", split_axis=1, concat_axis=0, tiled=True)
    ).astype(jnp.float32)
    section_grads = jnp.stack(
        [
            grad_y * conv_value,
            grad_mix * backward_rows[:, 2].astype(jnp.float32),
            grad_mix * backward_rows[:, 1].astype(jnp.float32),
        ],
        axis=1,
    ).astype(jnp.bfloat16)
    section_grads, filt_step = (section_grads, filt_step)
    sent_rows, sent_grads = from_partner((forward_out, section_grads), "pipe", 0)
    return (sent_rows[None], sent_grads[None], filt_step[None, None])


def on_device(fwd_in, bwd_in, bwd_cot, filter_taps, norm_gain):
    length = filter_taps.shape[3]
    if not dense_fits(length):
        return on_device_factored(fwd_in, bwd_in, bwd_cot, filter_taps, norm_gain)
    model_width = norm_gain.shape[1] * lax.axis_size("tp")
    table = constant_dft_table(length)
    weights = spectral_weights(length)
    gain_row = norm_gain[0]
    forward_rows = fwd_in[0]
    backward_rows = bwd_in[0]

    def featurize(proj_rows):
        return (proj_rows[:, 1].astype(jnp.float32) * proj_rows[:, 2].astype(jnp.float32)).astype(
            jnp.bfloat16
        )

    def to_columns(rows):
        return lax.all_to_all(rows, "ctx", split_axis=1, concat_axis=0, tiled=True)

    def to_rows(columns):
        return lax.all_to_all(columns, "ctx", split_axis=0, concat_axis=1, tiled=True)

    def row_total(values):
        return lax.psum(jnp.sum(values, axis=1), "tp")

    partner_kv = from_partner(backward_rows[:, 1:3], "pipe", 0)
    local_taps, forward_mix_rows = lax.optimization_barrier((filter_taps[0, 0], featurize(forward_rows)))
    forward_cols = to_columns(forward_mix_rows)
    tap_spec = dense_taps_spectrum(local_taps, table)
    tap_scaled = tap_spec * weights
    backward_cols = to_columns(featurize(backward_rows))
    forward_spec = dense_spectrum_exact(forward_cols, table)
    forward_z = to_rows(
        dense_signal(dense_multiply(forward_spec, tap_scaled, False), table).astype(jnp.bfloat16)
    )
    partner_kv, backward_cols = lax.optimization_barrier((partner_kv, backward_cols))
    backward_spec = dense_spectrum_exact(backward_cols, table)
    backward_z = to_rows(
        dense_signal(dense_multiply(backward_spec, tap_scaled, False), table).astype(jnp.bfloat16)
    )
    forward_y = forward_rows[:, 0].astype(jnp.float32) * forward_z.astype(jnp.float32)
    forward_scale = lax.rsqrt(row_total(forward_y * forward_y) / model_width + epsilon)[:, None]
    forward_out = (forward_y * forward_scale * gain_row).astype(jnp.bfloat16)
    sent_rows = from_partner(forward_out, "pipe", 0)
    backward_q = backward_rows[:, 0].astype(jnp.float32)
    conv_value = backward_z.astype(jnp.float32)
    backward_y = backward_q * conv_value
    weighted = bwd_cot[0].astype(jnp.float32) * gain_row
    backward_scale = lax.rsqrt(row_total(backward_y * backward_y) / model_width + epsilon)[:, None]
    normed = backward_y * backward_scale
    average = (row_total(weighted * normed) / model_width)[:, None]
    grad_y = backward_scale * (weighted - normed * average)
    grad_z = (grad_y * backward_q).astype(jnp.bfloat16)
    sent_first = from_partner((grad_y * conv_value).astype(jnp.bfloat16), "pipe", 0)
    grad_cols = to_columns(grad_z)
    grad_spec = dense_spectrum_exact(grad_cols, table) * weights
    mix_prod = dense_multiply(grad_spec, tap_spec, True)
    width = mix_prod.shape[1] // 2 if mix_prod.shape[1] % 256 == 0 else mix_prod.shape[1]
    pieces = mix_prod.shape[1] // width
    first_cols = dense_signal(mix_prod[:, :width], table).astype(jnp.bfloat16)
    sent_rows, sent_first, first_cols = lax.optimization_barrier((sent_rows, sent_first, first_cols))
    sent_parts = [from_partner(to_rows(first_cols), "pipe", 0)]
    for piece in range(1, pieces):
        piece_cols = dense_signal(mix_prod[:, piece * width : (piece + 1) * width], table)
        sent_parts.append(from_partner(to_rows(piece_cols.astype(jnp.bfloat16)), "pipe", 0))
    taps_prod = dense_multiply(grad_spec, backward_spec, True)
    taps_hi, taps_lo = split_bf16(taps_prod)
    table_hi, table_lo = table
    dims = (((0,), (1,)), ((), ()))
    part = lambda a, b: lax.dot_general(a, b, dims, preferred_element_type=jnp.float32)
    filt_step = part(taps_hi, table_hi) + (part(taps_hi, table_lo) + part(taps_lo, table_hi))
    token_rows = sent_parts[0].shape[0]
    ctx_count = lax.axis_size("ctx")
    sent_mix = jnp.stack(
        [p.reshape(token_rows, ctx_count, width) for p in sent_parts], axis=2
    ).reshape(token_rows, -1).astype(jnp.float32)
    rest = jnp.stack(
        [
            sent_mix * partner_kv[:, 1].astype(jnp.float32),
            sent_mix * partner_kv[:, 0].astype(jnp.float32),
        ],
        axis=1,
    ).astype(jnp.bfloat16)
    sent_grads = jnp.concatenate([sent_first[:, None], rest], axis=1)
    return (sent_rows[None], sent_grads[None], filt_step[None, None])


def solution(mesh):
    return jax.shard_map(
        on_device,
        mesh=mesh,
        in_specs=(
            P("pipe", "ctx", None, "tp"),
            P("pipe", "ctx", None, "tp"),
            P("pipe", "ctx", "tp"),
            P("pipe", "tp", "ctx", None),
            P("pipe", "tp"),
        ),
        out_specs=(
            P("pipe", "ctx", "tp"),
            P("pipe", "ctx", None, "tp"),
            P("pipe", "tp", "ctx", None),
        ),
        check_vma=False,
    )
```

```python
import math

import jax
import ml_dtypes
import numpy as np
import jax.numpy as jnp
from jax import lax
from jax.sharding import PartitionSpec as P

epsilon = 1e-06
highest = lax.Precision.HIGHEST


def from_partner(block, axis, bit):
    count = lax.axis_size(axis)
    route = []
    for low in range(count):
        high = low | 1 << bit
        if high != low and high < count:
            route += [(low, high), (high, low)]
    return lax.ppermute(block, axis, route)


def unit_table(count_out, count_in, period):
    product = lax.broadcasted_iota(jnp.int32, (count_out, count_in), 0) * lax.broadcasted_iota(
        jnp.int32, (count_out, count_in), 1
    )
    phase_angle = (product % period).astype(jnp.float32) * (-2.0 * math.pi / period)
    return (jnp.cos(phase_angle), jnp.sin(phase_angle))


def dft_tables(padded):
    blocks = padded // 128
    cos_high, sin_high = unit_table(blocks, blocks, blocks)
    cos_low, sin_low = unit_table(128, 128, 128)
    cos_twist, sin_twist = unit_table(blocks, 128, padded)
    return (cos_high, sin_high, cos_low, sin_low, cos_twist, sin_twist)


def spectrum(signal, tables):
    cos_high, sin_high, cos_low, sin_low, cos_twist, sin_twist = tables
    channels = signal.shape[0]
    half_blocks = signal.shape[1] // 128
    folded = signal.reshape(channels, half_blocks, 128)
    first_re = jnp.einsum("can,ak->ckn", folded, cos_high[:half_blocks], precision=highest)
    first_im = jnp.einsum("can,ak->ckn", folded, sin_high[:half_blocks], precision=highest)
    turned_re = first_re * cos_twist - first_im * sin_twist
    turned_im = first_re * sin_twist + first_im * cos_twist
    spec_re = jnp.einsum("ckn,nj->ckj", turned_re, cos_low, precision=highest) - jnp.einsum(
        "ckn,nj->ckj", turned_im, sin_low, precision=highest
    )
    spec_im = jnp.einsum("ckn,nj->ckj", turned_re, sin_low, precision=highest) + jnp.einsum(
        "ckn,nj->ckj", turned_im, cos_low, precision=highest
    )
    return (spec_re, spec_im)


def signal_of(spec_re, spec_im, tables):
    cos_high, sin_high, cos_low, sin_low, cos_twist, sin_twist = tables
    channels = spec_re.shape[0]
    blocks = spec_re.shape[1]
    half_blocks = blocks // 2
    mid_re = jnp.einsum("ckj,jn->ckn", spec_re, cos_low, precision=highest) + jnp.einsum(
        "ckj,jn->ckn", spec_im, sin_low, precision=highest
    )
    mid_im = jnp.einsum("ckj,jn->ckn", spec_im, cos_low, precision=highest) - jnp.einsum(
        "ckj,jn->ckn", spec_re, sin_low, precision=highest
    )
    back_re = mid_re * cos_twist + mid_im * sin_twist
    back_im = mid_im * cos_twist - mid_re * sin_twist
    values = jnp.einsum(
        "ak,ckn->can", cos_high[:half_blocks], back_re, precision=highest
    ) + jnp.einsum("ak,ckn->can", sin_high[:half_blocks], back_im, precision=highest)
    return values.reshape(channels, half_blocks * 128) / (blocks * 128)


def spec_product(a_re, a_im, b_re, b_im):
    return (a_re * b_re - a_im * b_im, a_re * b_im + a_im * b_re)


def spec_against(a_re, a_im, b_re, b_im):
    return (a_re * b_re + a_im * b_im, a_im * b_re - a_re * b_im)


def split_bf16(values):
    high = lax.reduce_precision(values, exponent_bits=8, mantissa_bits=7)
    return (high.astype(jnp.bfloat16), (values - high).astype(jnp.bfloat16))


def unit_angles(count_rows, count_cols, stride, padded):
    rows = lax.broadcasted_iota(jnp.int32, (count_rows, count_cols), 0) * stride
    cols = lax.broadcasted_iota(jnp.int32, (count_rows, count_cols), 1)
    angle = ((rows * cols) % padded).astype(jnp.float32) * (2.0 * math.pi / padded)
    return (jnp.cos(angle), jnp.sin(angle))


def real_dft_table(length):
    padded = 2 * length
    inner = 1 << (length.bit_length() // 2)
    if length % inner:
        inner = 1
    outer = length // inner
    cos_outer, sin_outer = unit_angles(outer, length, inner, padded)
    cos_inner, sin_inner = unit_angles(inner, length, 1, padded)
    cos_full = (cos_outer[:, None] * cos_inner[None] - sin_outer[:, None] * sin_inner[None]).reshape(
        length, length
    )
    sin_full = (sin_outer[:, None] * cos_inner[None] + cos_outer[:, None] * sin_inner[None]).reshape(
        length, length
    )
    rows = lax.broadcasted_iota(jnp.int32, (length, length), 0)
    cols = lax.broadcasted_iota(jnp.int32, (length, length), 1)
    alternating = jnp.where(rows % 2 == 0, 1.0, -1.0).astype(jnp.float32)
    sin_part = jnp.where(cols == 0, alternating, -sin_full)
    table = jnp.concatenate([cos_full, sin_part], axis=1)
    return split_bf16(table)


def constant_dft_table(length):
    padded = 2 * length
    rows = np.arange(length, dtype=np.int64)[:, None]
    cols = np.arange(length, dtype=np.int64)[None, :]
    angle = ((rows * cols) % padded).astype(np.float64) * (2.0 * np.pi / padded)
    alternating = np.where(rows % 2 == 0, 1.0, -1.0)
    sin_part = np.where(cols == 0, alternating, -np.sin(angle))
    table = np.concatenate([np.cos(angle), sin_part], axis=1).astype(np.float32)
    high = table.astype(ml_dtypes.bfloat16)
    low = (table - high.astype(np.float32)).astype(ml_dtypes.bfloat16)
    return (jnp.asarray(high), jnp.asarray(low))


def dot_tf(table, signal):
    return lax.dot_general(
        table, signal, (((0,), (0,)), ((), ())), preferred_element_type=jnp.float32
    )


def dot_tt(table, spec):
    return lax.dot_general(
        table, spec, (((1,), (0,)), ((), ())), preferred_element_type=jnp.float32
    )


def dense_spectrum_exact(rows_bf16, table):
    table_hi, table_lo = table
    return dot_tf(table_hi, rows_bf16) + dot_tf(table_lo, rows_bf16)


def dense_signal(spec, table):
    table_hi, table_lo = table
    spec_hi, spec_lo = split_bf16(spec)
    return dot_tt(table_hi, spec_hi) + (dot_tt(table_lo, spec_hi) + dot_tt(table_hi, spec_lo))


def dense_taps_spectrum(taps, table):
    table_hi, table_lo = table
    taps_hi, taps_lo = split_bf16(taps)
    dims = (((0,), (1,)), ((), ()))
    part = lambda a, b: lax.dot_general(a, b, dims, preferred_element_type=jnp.float32)
    return part(table_hi, taps_hi) + (part(table_lo, taps_hi) + part(table_hi, taps_lo))


def spectral_weights(length):
    index = lax.broadcasted_iota(jnp.int32, (2 * length, 1), 0)
    edge = (index == 0) | (index == length)
    return jnp.where(edge, 1.0, 2.0).astype(jnp.float32) / (2 * length)


def dense_multiply(a, b, conjugate):
    length = a.shape[0] // 2
    a_re, a_im = a[:length], a[length:]
    b_re, b_im = b[:length], b[length:]
    first = lax.broadcasted_iota(jnp.int32, (length, 1), 0) == 0
    if conjugate:
        re = a_re * b_re + a_im * b_im
        im = a_im * b_re - a_re * b_im
    else:
        re = a_re * b_re - a_im * b_im
        im = a_re * b_im + a_im * b_re
    re = jnp.where(first, a_re * b_re, re)
    im = jnp.where(first, a_im * b_im, im)
    return jnp.concatenate([re, im], axis=0)


def dense_fits(length):
    return 4 * length * length * 2 <= 16 * 1024 * 1024


def on_device_factored(fwd_in, bwd_in, bwd_cot, filter_taps, norm_gain):
    model_width = norm_gain.shape[1] * lax.axis_size("tp")
    local_taps = filter_taps[0, 0]
    tables = dft_tables(2 * local_taps.shape[1])
    tap_re, tap_im = spectrum(local_taps, tables)
    gain_row = norm_gain[0]
    forward_rows = fwd_in[0]
    backward_rows = bwd_in[0]

    def featurize(proj_rows):
        return (proj_rows[:, 1].astype(jnp.float32) * proj_rows[:, 2].astype(jnp.float32)).astype(
            jnp.bfloat16
        )

    def convolve(columns):
        sig_re, sig_im = spectrum(columns.astype(jnp.float32), tables)
        prod_re, prod_im = spec_product(sig_re, sig_im, tap_re, tap_im)
        return (signal_of(prod_re, prod_im, tables).astype(jnp.bfloat16), (sig_re, sig_im))

    def relayout(mixed_rows):
        columns = lax.all_to_all(
            jnp.transpose(mixed_rows), "ctx", split_axis=0, concat_axis=1, tiled=True
        )
        result, kept_spec = convolve(columns)
        return (
            jnp.transpose(lax.all_to_all(result, "ctx", split_axis=1, concat_axis=0, tiled=True)),
            kept_spec,
        )

    def row_total(values):
        return lax.psum(jnp.sum(values, axis=1), "tp")

    forward_mix = featurize(forward_rows)
    backward_mix = featurize(backward_rows)
    forward_z = relayout(forward_mix)[0]
    backward_z, backward_spec = relayout(backward_mix)
    forward_y = forward_rows[:, 0].astype(jnp.float32) * forward_z.astype(jnp.float32)
    backward_q = backward_rows[:, 0].astype(jnp.float32)
    conv_value = backward_z.astype(jnp.float32)
    backward_y = backward_q * conv_value
    weighted = bwd_cot[0].astype(jnp.float32) * gain_row
    forward_scale = lax.rsqrt(row_total(forward_y * forward_y) / model_width + epsilon)[:, None]
    backward_scale = lax.rsqrt(row_total(backward_y * backward_y) / model_width + epsilon)[:, None]
    normed = backward_y * backward_scale
    average = (row_total(weighted * normed) / model_width)[:, None]
    forward_out = (forward_y * forward_scale * gain_row).astype(jnp.bfloat16)
    grad_y = backward_scale * (weighted - normed * average)
    grad_z = (grad_y * backward_q).astype(jnp.bfloat16)
    grad_cols = lax.all_to_all(
        jnp.transpose(grad_z), "ctx", split_axis=0, concat_axis=1, tiled=True
    )
    grad_re, grad_im = spectrum(grad_cols.astype(jnp.float32), tables)
    input_re, input_im = spec_against(grad_re, grad_im, tap_re, tap_im)
    grad_mix_cols = signal_of(input_re, input_im, tables).astype(jnp.bfloat16)
    taps_re, taps_im = spec_against(grad_re, grad_im, backward_spec[0], backward_spec[1])
    filt_step = signal_of(taps_re, taps_im, tables)
    grad_mix = jnp.transpose(
        lax.all_to_all(grad_mix_cols, "ctx", split_axis=1, concat_axis=0, tiled=True)
    ).astype(jnp.float32)
    section_grads = jnp.stack(
        [
            grad_y * conv_value,
            grad_mix * backward_rows[:, 2].astype(jnp.float32),
            grad_mix * backward_rows[:, 1].astype(jnp.float32),
        ],
        axis=1,
    ).astype(jnp.bfloat16)
    section_grads, filt_step = (section_grads, filt_step)
    sent_rows, sent_grads = from_partner((forward_out, section_grads), "pipe", 0)
    return (sent_rows[None], sent_grads[None], filt_step[None, None])


def on_device(fwd_in, bwd_in, bwd_cot, filter_taps, norm_gain):
    length = filter_taps.shape[3]
    if not dense_fits(length):
        return on_device_factored(fwd_in, bwd_in, bwd_cot, filter_taps, norm_gain)
    model_width = norm_gain.shape[1] * lax.axis_size("tp")
    table = constant_dft_table(length)
    weights = spectral_weights(length)
    tap_spec = dense_taps_spectrum(filter_taps[0, 0], table)
    tap_scaled = tap_spec * weights
    gain_row = norm_gain[0]
    forward_rows = fwd_in[0]
    backward_rows = bwd_in[0]

    def featurize(proj_rows):
        return (proj_rows[:, 1].astype(jnp.float32) * proj_rows[:, 2].astype(jnp.float32)).astype(
            jnp.bfloat16
        )

    def to_columns(rows):
        return lax.all_to_all(rows, "ctx", split_axis=1, concat_axis=0, tiled=True)

    def to_rows(columns):
        return lax.all_to_all(columns, "ctx", split_axis=0, concat_axis=1, tiled=True)

    def row_total(values):
        return lax.psum(jnp.sum(values, axis=1), "tp")

    partner_kv = from_partner(backward_rows[:, 1:3], "pipe", 0)
    forward_cols = to_columns(featurize(forward_rows))
    backward_cols = to_columns(featurize(backward_rows))
    forward_spec = dense_spectrum_exact(forward_cols, table)
    forward_z = to_rows(
        dense_signal(dense_multiply(forward_spec, tap_scaled, False), table).astype(jnp.bfloat16)
    )
    partner_kv, backward_cols = lax.optimization_barrier((partner_kv, backward_cols))
    backward_spec = dense_spectrum_exact(backward_cols, table)
    backward_z = to_rows(
        dense_signal(dense_multiply(backward_spec, tap_scaled, False), table).astype(jnp.bfloat16)
    )
    forward_y = forward_rows[:, 0].astype(jnp.float32) * forward_z.astype(jnp.float32)
    forward_scale = lax.rsqrt(row_total(forward_y * forward_y) / model_width + epsilon)[:, None]
    forward_out = (forward_y * forward_scale * gain_row).astype(jnp.bfloat16)
    sent_rows = from_partner(forward_out, "pipe", 0)
    backward_q = backward_rows[:, 0].astype(jnp.float32)
    conv_value = backward_z.astype(jnp.float32)
    backward_y = backward_q * conv_value
    weighted = bwd_cot[0].astype(jnp.float32) * gain_row
    backward_scale = lax.rsqrt(row_total(backward_y * backward_y) / model_width + epsilon)[:, None]
    normed = backward_y * backward_scale
    average = (row_total(weighted * normed) / model_width)[:, None]
    grad_y = backward_scale * (weighted - normed * average)
    grad_z = (grad_y * backward_q).astype(jnp.bfloat16)
    sent_first = from_partner((grad_y * conv_value).astype(jnp.bfloat16), "pipe", 0)
    token_rows = grad_z.shape[0]
    ctx_count = lax.axis_size("ctx")
    total_cols = tap_spec.shape[1]
    width = total_cols // 2 if total_cols % 256 == 0 else total_cols
    pieces = total_cols // width
    grad_pieces = grad_z.reshape(token_rows, ctx_count, pieces, width)
    grad_specs = []
    for piece in range(pieces):
        piece_rows = grad_pieces[:, :, piece].reshape(token_rows, ctx_count * width)
        grad_specs.append(dense_spectrum_exact(to_columns(piece_rows), table) * weights)
    piece_of = lambda values, piece: values[:, piece * width : (piece + 1) * width]
    first_cols = dense_signal(
        dense_multiply(grad_specs[0], piece_of(tap_spec, 0), True), table
    ).astype(jnp.bfloat16)
    sent_rows, sent_first, first_cols = lax.optimization_barrier((sent_rows, sent_first, first_cols))
    sent_parts = [from_partner(to_rows(first_cols), "pipe", 0)]
    for piece in range(1, pieces):
        piece_cols = dense_signal(
            dense_multiply(grad_specs[piece], piece_of(tap_spec, piece), True), table
        )
        sent_parts.append(from_partner(to_rows(piece_cols.astype(jnp.bfloat16)), "pipe", 0))
    table_hi, table_lo = table
    dims = (((0,), (1,)), ((), ()))
    part = lambda a, b: lax.dot_general(a, b, dims, preferred_element_type=jnp.float32)
    filt_parts = []
    for piece in range(pieces):
        taps_prod = dense_multiply(grad_specs[piece], piece_of(backward_spec, piece), True)
        taps_hi, taps_lo = split_bf16(taps_prod)
        filt_parts.append(
            part(taps_hi, table_hi) + (part(taps_hi, table_lo) + part(taps_lo, table_hi))
        )
    filt_step = jnp.concatenate(filt_parts, axis=0)
    sent_mix = jnp.stack(
        [p.reshape(token_rows, ctx_count, width) for p in sent_parts], axis=2
    ).reshape(token_rows, -1).astype(jnp.float32)
    rest = jnp.stack(
        [
            sent_mix * partner_kv[:, 1].astype(jnp.float32),
            sent_mix * partner_kv[:, 0].astype(jnp.float32),
        ],
        axis=1,
    ).astype(jnp.bfloat16)
    sent_grads = jnp.concatenate([sent_first[:, None], rest], axis=1)
    return (sent_rows[None], sent_grads[None], filt_step[None, None])


def solution(mesh):
    return jax.shard_map(
        on_device,
        mesh=mesh,
        in_specs=(
            P("pipe", "ctx", None, "tp"),
            P("pipe", "ctx", None, "tp"),
            P("pipe", "ctx", "tp"),
            P("pipe", "tp", "ctx", None),
            P("pipe", "tp"),
        ),
        out_specs=(
            P("pipe", "ctx", "tp"),
            P("pipe", "ctx", None, "tp"),
            P("pipe", "tp", "ctx", None),
        ),
        check_vma=False,
    )
```

```python
import math

import jax
import ml_dtypes
import numpy as np
import jax.numpy as jnp
from jax import lax
from jax.sharding import PartitionSpec as P

epsilon = 1e-06
highest = lax.Precision.HIGHEST


def from_partner(block, axis, bit):
    count = lax.axis_size(axis)
    route = []
    for low in range(count):
        high = low | 1 << bit
        if high != low and high < count:
            route += [(low, high), (high, low)]
    return lax.ppermute(block, axis, route)


def unit_table(count_out, count_in, period):
    product = lax.broadcasted_iota(jnp.int32, (count_out, count_in), 0) * lax.broadcasted_iota(
        jnp.int32, (count_out, count_in), 1
    )
    phase_angle = (product % period).astype(jnp.float32) * (-2.0 * math.pi / period)
    return (jnp.cos(phase_angle), jnp.sin(phase_angle))


def dft_tables(padded):
    blocks = padded // 128
    cos_high, sin_high = unit_table(blocks, blocks, blocks)
    cos_low, sin_low = unit_table(128, 128, 128)
    cos_twist, sin_twist = unit_table(blocks, 128, padded)
    return (cos_high, sin_high, cos_low, sin_low, cos_twist, sin_twist)


def spectrum(signal, tables):
    cos_high, sin_high, cos_low, sin_low, cos_twist, sin_twist = tables
    channels = signal.shape[0]
    half_blocks = signal.shape[1] // 128
    folded = signal.reshape(channels, half_blocks, 128)
    first_re = jnp.einsum("can,ak->ckn", folded, cos_high[:half_blocks], precision=highest)
    first_im = jnp.einsum("can,ak->ckn", folded, sin_high[:half_blocks], precision=highest)
    turned_re = first_re * cos_twist - first_im * sin_twist
    turned_im = first_re * sin_twist + first_im * cos_twist
    spec_re = jnp.einsum("ckn,nj->ckj", turned_re, cos_low, precision=highest) - jnp.einsum(
        "ckn,nj->ckj", turned_im, sin_low, precision=highest
    )
    spec_im = jnp.einsum("ckn,nj->ckj", turned_re, sin_low, precision=highest) + jnp.einsum(
        "ckn,nj->ckj", turned_im, cos_low, precision=highest
    )
    return (spec_re, spec_im)


def signal_of(spec_re, spec_im, tables):
    cos_high, sin_high, cos_low, sin_low, cos_twist, sin_twist = tables
    channels = spec_re.shape[0]
    blocks = spec_re.shape[1]
    half_blocks = blocks // 2
    mid_re = jnp.einsum("ckj,jn->ckn", spec_re, cos_low, precision=highest) + jnp.einsum(
        "ckj,jn->ckn", spec_im, sin_low, precision=highest
    )
    mid_im = jnp.einsum("ckj,jn->ckn", spec_im, cos_low, precision=highest) - jnp.einsum(
        "ckj,jn->ckn", spec_re, sin_low, precision=highest
    )
    back_re = mid_re * cos_twist + mid_im * sin_twist
    back_im = mid_im * cos_twist - mid_re * sin_twist
    values = jnp.einsum(
        "ak,ckn->can", cos_high[:half_blocks], back_re, precision=highest
    ) + jnp.einsum("ak,ckn->can", sin_high[:half_blocks], back_im, precision=highest)
    return values.reshape(channels, half_blocks * 128) / (blocks * 128)


def spec_product(a_re, a_im, b_re, b_im):
    return (a_re * b_re - a_im * b_im, a_re * b_im + a_im * b_re)


def spec_against(a_re, a_im, b_re, b_im):
    return (a_re * b_re + a_im * b_im, a_im * b_re - a_re * b_im)


def split_bf16(values):
    high = lax.reduce_precision(values, exponent_bits=8, mantissa_bits=7)
    return (high.astype(jnp.bfloat16), (values - high).astype(jnp.bfloat16))


def unit_angles(count_rows, count_cols, stride, padded):
    rows = lax.broadcasted_iota(jnp.int32, (count_rows, count_cols), 0) * stride
    cols = lax.broadcasted_iota(jnp.int32, (count_rows, count_cols), 1)
    angle = ((rows * cols) % padded).astype(jnp.float32) * (2.0 * math.pi / padded)
    return (jnp.cos(angle), jnp.sin(angle))


def real_dft_table(length):
    padded = 2 * length
    inner = 1 << (length.bit_length() // 2)
    if length % inner:
        inner = 1
    outer = length // inner
    cos_outer, sin_outer = unit_angles(outer, length, inner, padded)
    cos_inner, sin_inner = unit_angles(inner, length, 1, padded)
    cos_full = (cos_outer[:, None] * cos_inner[None] - sin_outer[:, None] * sin_inner[None]).reshape(
        length, length
    )
    sin_full = (sin_outer[:, None] * cos_inner[None] + cos_outer[:, None] * sin_inner[None]).reshape(
        length, length
    )
    rows = lax.broadcasted_iota(jnp.int32, (length, length), 0)
    cols = lax.broadcasted_iota(jnp.int32, (length, length), 1)
    alternating = jnp.where(rows % 2 == 0, 1.0, -1.0).astype(jnp.float32)
    sin_part = jnp.where(cols == 0, alternating, -sin_full)
    table = jnp.concatenate([cos_full, sin_part], axis=1)
    return split_bf16(table)


def constant_dft_table(length):
    padded = 2 * length
    rows = np.arange(length, dtype=np.int64)[:, None]
    cols = np.arange(length, dtype=np.int64)[None, :]
    angle = ((rows * cols) % padded).astype(np.float64) * (2.0 * np.pi / padded)
    alternating = np.where(rows % 2 == 0, 1.0, -1.0)
    sin_part = np.where(cols == 0, alternating, -np.sin(angle))
    table = np.concatenate([np.cos(angle), sin_part], axis=1).astype(np.float32)
    high = table.astype(ml_dtypes.bfloat16)
    low = (table - high.astype(np.float32)).astype(ml_dtypes.bfloat16)
    return (jnp.asarray(high), jnp.asarray(low))


def dot_tf(table, signal):
    return lax.dot_general(
        table, signal, (((0,), (0,)), ((), ())), preferred_element_type=jnp.float32
    )


def dot_tt(table, spec):
    return lax.dot_general(
        table, spec, (((1,), (0,)), ((), ())), preferred_element_type=jnp.float32
    )


def dense_spectrum_exact(rows_bf16, table):
    table_hi, table_lo = table
    return dot_tf(table_hi, rows_bf16) + dot_tf(table_lo, rows_bf16)


def dense_signal(spec, table):
    table_hi, table_lo = table
    spec_hi, spec_lo = split_bf16(spec)
    return dot_tt(table_hi, spec_hi) + (dot_tt(table_lo, spec_hi) + dot_tt(table_hi, spec_lo))


def dense_taps_spectrum(taps, table):
    table_hi, table_lo = table
    taps_hi, taps_lo = split_bf16(taps)
    dims = (((0,), (1,)), ((), ()))
    part = lambda a, b: lax.dot_general(a, b, dims, preferred_element_type=jnp.float32)
    return part(table_hi, taps_hi) + (part(table_lo, taps_hi) + part(table_hi, taps_lo))


def spectral_weights(length):
    index = lax.broadcasted_iota(jnp.int32, (2 * length, 1), 0)
    edge = (index == 0) | (index == length)
    return jnp.where(edge, 1.0, 2.0).astype(jnp.float32) / (2 * length)


def dense_multiply(a, b, conjugate):
    length = a.shape[0] // 2
    a_re, a_im = a[:length], a[length:]
    b_re, b_im = b[:length], b[length:]
    first = lax.broadcasted_iota(jnp.int32, (length, 1), 0) == 0
    if conjugate:
        re = a_re * b_re + a_im * b_im
        im = a_im * b_re - a_re * b_im
    else:
        re = a_re * b_re - a_im * b_im
        im = a_re * b_im + a_im * b_re
    re = jnp.where(first, a_re * b_re, re)
    im = jnp.where(first, a_im * b_im, im)
    return jnp.concatenate([re, im], axis=0)


def dense_fits(length):
    return 4 * length * length * 2 <= 16 * 1024 * 1024


def on_device_factored(fwd_in, bwd_in, bwd_cot, filter_taps, norm_gain):
    model_width = norm_gain.shape[1] * lax.axis_size("tp")
    local_taps = filter_taps[0, 0]
    tables = dft_tables(2 * local_taps.shape[1])
    tap_re, tap_im = spectrum(local_taps, tables)
    gain_row = norm_gain[0]
    forward_rows = fwd_in[0]
    backward_rows = bwd_in[0]

    def featurize(proj_rows):
        return (proj_rows[:, 1].astype(jnp.float32) * proj_rows[:, 2].astype(jnp.float32)).astype(
            jnp.bfloat16
        )

    def convolve(columns):
        sig_re, sig_im = spectrum(columns.astype(jnp.float32), tables)
        prod_re, prod_im = spec_product(sig_re, sig_im, tap_re, tap_im)
        return (signal_of(prod_re, prod_im, tables).astype(jnp.bfloat16), (sig_re, sig_im))

    def relayout(mixed_rows):
        columns = lax.all_to_all(
            jnp.transpose(mixed_rows), "ctx", split_axis=0, concat_axis=1, tiled=True
        )
        result, kept_spec = convolve(columns)
        return (
            jnp.transpose(lax.all_to_all(result, "ctx", split_axis=1, concat_axis=0, tiled=True)),
            kept_spec,
        )

    def row_total(values):
        return lax.psum(jnp.sum(values, axis=1), "tp")

    forward_mix = featurize(forward_rows)
    backward_mix = featurize(backward_rows)
    forward_z = relayout(forward_mix)[0]
    backward_z, backward_spec = relayout(backward_mix)
    forward_y = forward_rows[:, 0].astype(jnp.float32) * forward_z.astype(jnp.float32)
    backward_q = backward_rows[:, 0].astype(jnp.float32)
    conv_value = backward_z.astype(jnp.float32)
    backward_y = backward_q * conv_value
    weighted = bwd_cot[0].astype(jnp.float32) * gain_row
    forward_scale = lax.rsqrt(row_total(forward_y * forward_y) / model_width + epsilon)[:, None]
    backward_scale = lax.rsqrt(row_total(backward_y * backward_y) / model_width + epsilon)[:, None]
    normed = backward_y * backward_scale
    average = (row_total(weighted * normed) / model_width)[:, None]
    forward_out = (forward_y * forward_scale * gain_row).astype(jnp.bfloat16)
    grad_y = backward_scale * (weighted - normed * average)
    grad_z = (grad_y * backward_q).astype(jnp.bfloat16)
    grad_cols = lax.all_to_all(
        jnp.transpose(grad_z), "ctx", split_axis=0, concat_axis=1, tiled=True
    )
    grad_re, grad_im = spectrum(grad_cols.astype(jnp.float32), tables)
    input_re, input_im = spec_against(grad_re, grad_im, tap_re, tap_im)
    grad_mix_cols = signal_of(input_re, input_im, tables).astype(jnp.bfloat16)
    taps_re, taps_im = spec_against(grad_re, grad_im, backward_spec[0], backward_spec[1])
    filt_step = signal_of(taps_re, taps_im, tables)
    grad_mix = jnp.transpose(
        lax.all_to_all(grad_mix_cols, "ctx", split_axis=1, concat_axis=0, tiled=True)
    ).astype(jnp.float32)
    section_grads = jnp.stack(
        [
            grad_y * conv_value,
            grad_mix * backward_rows[:, 2].astype(jnp.float32),
            grad_mix * backward_rows[:, 1].astype(jnp.float32),
        ],
        axis=1,
    ).astype(jnp.bfloat16)
    section_grads, filt_step = (section_grads, filt_step)
    sent_rows, sent_grads = from_partner((forward_out, section_grads), "pipe", 0)
    return (sent_rows[None], sent_grads[None], filt_step[None, None])


def on_device(fwd_in, bwd_in, bwd_cot, filter_taps, norm_gain):
    length = filter_taps.shape[3]
    if not dense_fits(length):
        return on_device_factored(fwd_in, bwd_in, bwd_cot, filter_taps, norm_gain)
    model_width = norm_gain.shape[1] * lax.axis_size("tp")
    table = constant_dft_table(length)
    weights = spectral_weights(length)
    tap_spec = dense_taps_spectrum(filter_taps[0, 0], table)
    tap_scaled = tap_spec * weights
    gain_row = norm_gain[0]
    forward_rows = fwd_in[0]
    backward_rows = bwd_in[0]

    def featurize(proj_rows):
        return (proj_rows[:, 1].astype(jnp.float32) * proj_rows[:, 2].astype(jnp.float32)).astype(
            jnp.bfloat16
        )

    def to_columns(rows):
        return lax.all_to_all(rows, "ctx", split_axis=1, concat_axis=0, tiled=True)

    def to_rows(columns):
        return lax.all_to_all(columns, "ctx", split_axis=0, concat_axis=1, tiled=True)

    def row_total(values):
        return lax.psum(jnp.sum(values, axis=1), "tp")

    partner_kv = from_partner(backward_rows[:, 1:3], "pipe", 0)
    forward_cols = to_columns(featurize(forward_rows))
    backward_cols = to_columns(featurize(backward_rows))
    forward_spec = dense_spectrum_exact(forward_cols, table)
    forward_conv = dense_signal(dense_multiply(forward_spec, tap_scaled, False), table)
    forward_conv = forward_conv.astype(jnp.bfloat16)
    partner_kv, backward_cols = lax.optimization_barrier((partner_kv, backward_cols))
    backward_spec = dense_spectrum_exact(backward_cols, table)
    forward_conv, backward_spec = lax.optimization_barrier((forward_conv, backward_spec))
    forward_z = to_rows(forward_conv)
    backward_z = to_rows(
        dense_signal(dense_multiply(backward_spec, tap_scaled, False), table).astype(jnp.bfloat16)
    )
    forward_y = forward_rows[:, 0].astype(jnp.float32) * forward_z.astype(jnp.float32)
    forward_scale = lax.rsqrt(row_total(forward_y * forward_y) / model_width + epsilon)[:, None]
    forward_out = (forward_y * forward_scale * gain_row).astype(jnp.bfloat16)
    sent_rows = from_partner(forward_out, "pipe", 0)
    backward_q = backward_rows[:, 0].astype(jnp.float32)
    conv_value = backward_z.astype(jnp.float32)
    backward_y = backward_q * conv_value
    weighted = bwd_cot[0].astype(jnp.float32) * gain_row
    backward_scale = lax.rsqrt(row_total(backward_y * backward_y) / model_width + epsilon)[:, None]
    normed = backward_y * backward_scale
    average = (row_total(weighted * normed) / model_width)[:, None]
    grad_y = backward_scale * (weighted - normed * average)
    grad_z = (grad_y * backward_q).astype(jnp.bfloat16)
    sent_first = from_partner((grad_y * conv_value).astype(jnp.bfloat16), "pipe", 0)
    grad_cols = to_columns(grad_z)
    grad_spec = dense_spectrum_exact(grad_cols, table) * weights
    mix_prod = dense_multiply(grad_spec, tap_spec, True)
    width = mix_prod.shape[1] // 2 if mix_prod.shape[1] % 256 == 0 else mix_prod.shape[1]
    pieces = mix_prod.shape[1] // width
    first_cols = dense_signal(mix_prod[:, :width], table).astype(jnp.bfloat16)
    sent_rows, sent_first, first_cols = lax.optimization_barrier((sent_rows, sent_first, first_cols))
    sent_parts = [from_partner(to_rows(first_cols), "pipe", 0)]
    for piece in range(1, pieces):
        piece_cols = dense_signal(mix_prod[:, piece * width : (piece + 1) * width], table)
        sent_parts.append(from_partner(to_rows(piece_cols.astype(jnp.bfloat16)), "pipe", 0))
    taps_prod = dense_multiply(grad_spec, backward_spec, True)
    taps_hi, taps_lo = split_bf16(taps_prod)
    table_hi, table_lo = table
    dims = (((0,), (1,)), ((), ()))
    part = lambda a, b: lax.dot_general(a, b, dims, preferred_element_type=jnp.float32)
    filt_step = part(taps_hi, table_hi) + (part(taps_hi, table_lo) + part(taps_lo, table_hi))
    token_rows = sent_parts[0].shape[0]
    ctx_count = lax.axis_size("ctx")
    sent_mix = jnp.stack(
        [p.reshape(token_rows, ctx_count, width) for p in sent_parts], axis=2
    ).reshape(token_rows, -1).astype(jnp.float32)
    rest = jnp.stack(
        [
            sent_mix * partner_kv[:, 1].astype(jnp.float32),
            sent_mix * partner_kv[:, 0].astype(jnp.float32),
        ],
        axis=1,
    ).astype(jnp.bfloat16)
    sent_grads = jnp.concatenate([sent_first[:, None], rest], axis=1)
    return (sent_rows[None], sent_grads[None], filt_step[None, None])


def solution(mesh):
    return jax.shard_map(
        on_device,
        mesh=mesh,
        in_specs=(
            P("pipe", "ctx", None, "tp"),
            P("pipe", "ctx", None, "tp"),
            P("pipe", "ctx", "tp"),
            P("pipe", "tp", "ctx", None),
            P("pipe", "tp"),
        ),
        out_specs=(
            P("pipe", "ctx", "tp"),
            P("pipe", "ctx", None, "tp"),
            P("pipe", "tp", "ctx", None),
        ),
        check_vma=False,
    )
```

```python
import math

import jax
import ml_dtypes
import numpy as np
import jax.numpy as jnp
from jax import lax
from jax.sharding import PartitionSpec as P

epsilon = 1e-06
highest = lax.Precision.HIGHEST


def from_partner(block, axis, bit):
    count = lax.axis_size(axis)
    route = []
    for low in range(count):
        high = low | 1 << bit
        if high != low and high < count:
            route += [(low, high), (high, low)]
    return lax.ppermute(block, axis, route)


def unit_table(count_out, count_in, period):
    product = lax.broadcasted_iota(jnp.int32, (count_out, count_in), 0) * lax.broadcasted_iota(
        jnp.int32, (count_out, count_in), 1
    )
    phase_angle = (product % period).astype(jnp.float32) * (-2.0 * math.pi / period)
    return (jnp.cos(phase_angle), jnp.sin(phase_angle))


def dft_tables(padded):
    blocks = padded // 128
    cos_high, sin_high = unit_table(blocks, blocks, blocks)
    cos_low, sin_low = unit_table(128, 128, 128)
    cos_twist, sin_twist = unit_table(blocks, 128, padded)
    return (cos_high, sin_high, cos_low, sin_low, cos_twist, sin_twist)


def spectrum(signal, tables):
    cos_high, sin_high, cos_low, sin_low, cos_twist, sin_twist = tables
    channels = signal.shape[0]
    half_blocks = signal.shape[1] // 128
    folded = signal.reshape(channels, half_blocks, 128)
    first_re = jnp.einsum("can,ak->ckn", folded, cos_high[:half_blocks], precision=highest)
    first_im = jnp.einsum("can,ak->ckn", folded, sin_high[:half_blocks], precision=highest)
    turned_re = first_re * cos_twist - first_im * sin_twist
    turned_im = first_re * sin_twist + first_im * cos_twist
    spec_re = jnp.einsum("ckn,nj->ckj", turned_re, cos_low, precision=highest) - jnp.einsum(
        "ckn,nj->ckj", turned_im, sin_low, precision=highest
    )
    spec_im = jnp.einsum("ckn,nj->ckj", turned_re, sin_low, precision=highest) + jnp.einsum(
        "ckn,nj->ckj", turned_im, cos_low, precision=highest
    )
    return (spec_re, spec_im)


def signal_of(spec_re, spec_im, tables):
    cos_high, sin_high, cos_low, sin_low, cos_twist, sin_twist = tables
    channels = spec_re.shape[0]
    blocks = spec_re.shape[1]
    half_blocks = blocks // 2
    mid_re = jnp.einsum("ckj,jn->ckn", spec_re, cos_low, precision=highest) + jnp.einsum(
        "ckj,jn->ckn", spec_im, sin_low, precision=highest
    )
    mid_im = jnp.einsum("ckj,jn->ckn", spec_im, cos_low, precision=highest) - jnp.einsum(
        "ckj,jn->ckn", spec_re, sin_low, precision=highest
    )
    back_re = mid_re * cos_twist + mid_im * sin_twist
    back_im = mid_im * cos_twist - mid_re * sin_twist
    values = jnp.einsum(
        "ak,ckn->can", cos_high[:half_blocks], back_re, precision=highest
    ) + jnp.einsum("ak,ckn->can", sin_high[:half_blocks], back_im, precision=highest)
    return values.reshape(channels, half_blocks * 128) / (blocks * 128)


def spec_product(a_re, a_im, b_re, b_im):
    return (a_re * b_re - a_im * b_im, a_re * b_im + a_im * b_re)


def spec_against(a_re, a_im, b_re, b_im):
    return (a_re * b_re + a_im * b_im, a_im * b_re - a_re * b_im)


def split_bf16(values):
    high = lax.reduce_precision(values, exponent_bits=8, mantissa_bits=7)
    return (high.astype(jnp.bfloat16), (values - high).astype(jnp.bfloat16))


def unit_angles(count_rows, count_cols, stride, padded):
    rows = lax.broadcasted_iota(jnp.int32, (count_rows, count_cols), 0) * stride
    cols = lax.broadcasted_iota(jnp.int32, (count_rows, count_cols), 1)
    angle = ((rows * cols) % padded).astype(jnp.float32) * (2.0 * math.pi / padded)
    return (jnp.cos(angle), jnp.sin(angle))


def real_dft_table(length):
    padded = 2 * length
    inner = 1 << (length.bit_length() // 2)
    if length % inner:
        inner = 1
    outer = length // inner
    cos_outer, sin_outer = unit_angles(outer, length, inner, padded)
    cos_inner, sin_inner = unit_angles(inner, length, 1, padded)
    cos_full = (cos_outer[:, None] * cos_inner[None] - sin_outer[:, None] * sin_inner[None]).reshape(
        length, length
    )
    sin_full = (sin_outer[:, None] * cos_inner[None] + cos_outer[:, None] * sin_inner[None]).reshape(
        length, length
    )
    rows = lax.broadcasted_iota(jnp.int32, (length, length), 0)
    cols = lax.broadcasted_iota(jnp.int32, (length, length), 1)
    alternating = jnp.where(rows % 2 == 0, 1.0, -1.0).astype(jnp.float32)
    sin_part = jnp.where(cols == 0, alternating, -sin_full)
    table = jnp.concatenate([cos_full, sin_part], axis=1)
    return split_bf16(table)


def constant_dft_table(length):
    padded = 2 * length
    rows = np.arange(length, dtype=np.int64)[:, None]
    cols = np.arange(length, dtype=np.int64)[None, :]
    angle = ((rows * cols) % padded).astype(np.float64) * (2.0 * np.pi / padded)
    alternating = np.where(rows % 2 == 0, 1.0, -1.0)
    sin_part = np.where(cols == 0, alternating, -np.sin(angle))
    table = np.concatenate([np.cos(angle), sin_part], axis=1).astype(np.float32)
    high = table.astype(ml_dtypes.bfloat16)
    low = (table - high.astype(np.float32)).astype(ml_dtypes.bfloat16)
    return (jnp.asarray(high), jnp.asarray(low))


def dot_tf(table, signal):
    return lax.dot_general(
        table, signal, (((0,), (0,)), ((), ())), preferred_element_type=jnp.float32
    )


def dot_tt(table, spec):
    return lax.dot_general(
        table, spec, (((1,), (0,)), ((), ())), preferred_element_type=jnp.float32
    )


def dense_spectrum_exact(rows_bf16, table):
    table_hi, table_lo = table
    return dot_tf(table_hi, rows_bf16) + dot_tf(table_lo, rows_bf16)


def dense_signal(spec, table):
    table_hi, table_lo = table
    spec_hi, spec_lo = split_bf16(spec)
    return dot_tt(table_hi, spec_hi) + (dot_tt(table_lo, spec_hi) + dot_tt(table_hi, spec_lo))


def dense_taps_spectrum(taps, table):
    table_hi, table_lo = table
    taps_hi, taps_lo = split_bf16(taps)
    dims = (((0,), (1,)), ((), ()))
    part = lambda a, b: lax.dot_general(a, b, dims, preferred_element_type=jnp.float32)
    return part(table_hi, taps_hi) + (part(table_lo, taps_hi) + part(table_hi, taps_lo))


def spectral_weights(length):
    index = lax.broadcasted_iota(jnp.int32, (2 * length, 1), 0)
    edge = (index == 0) | (index == length)
    return jnp.where(edge, 1.0, 2.0).astype(jnp.float32) / (2 * length)


def dense_multiply(a, b, conjugate):
    length = a.shape[0] // 2
    a_re, a_im = a[:length], a[length:]
    b_re, b_im = b[:length], b[length:]
    first = lax.broadcasted_iota(jnp.int32, (length, 1), 0) == 0
    if conjugate:
        re = a_re * b_re + a_im * b_im
        im = a_im * b_re - a_re * b_im
    else:
        re = a_re * b_re - a_im * b_im
        im = a_re * b_im + a_im * b_re
    re = jnp.where(first, a_re * b_re, re)
    im = jnp.where(first, a_im * b_im, im)
    return jnp.concatenate([re, im], axis=0)


def dense_fits(length):
    return 4 * length * length * 2 <= 16 * 1024 * 1024


def on_device_factored(fwd_in, bwd_in, bwd_cot, filter_taps, norm_gain):
    model_width = norm_gain.shape[1] * lax.axis_size("tp")
    local_taps = filter_taps[0, 0]
    tables = dft_tables(2 * local_taps.shape[1])
    tap_re, tap_im = spectrum(local_taps, tables)
    gain_row = norm_gain[0]
    forward_rows = fwd_in[0]
    backward_rows = bwd_in[0]

    def featurize(proj_rows):
        return (proj_rows[:, 1].astype(jnp.float32) * proj_rows[:, 2].astype(jnp.float32)).astype(
            jnp.bfloat16
        )

    def convolve(columns):
        sig_re, sig_im = spectrum(columns.astype(jnp.float32), tables)
        prod_re, prod_im = spec_product(sig_re, sig_im, tap_re, tap_im)
        return (signal_of(prod_re, prod_im, tables).astype(jnp.bfloat16), (sig_re, sig_im))

    def relayout(mixed_rows):
        columns = lax.all_to_all(
            jnp.transpose(mixed_rows), "ctx", split_axis=0, concat_axis=1, tiled=True
        )
        result, kept_spec = convolve(columns)
        return (
            jnp.transpose(lax.all_to_all(result, "ctx", split_axis=1, concat_axis=0, tiled=True)),
            kept_spec,
        )

    def row_total(values):
        return lax.psum(jnp.sum(values, axis=1), "tp")

    forward_mix = featurize(forward_rows)
    backward_mix = featurize(backward_rows)
    forward_z = relayout(forward_mix)[0]
    backward_z, backward_spec = relayout(backward_mix)
    forward_y = forward_rows[:, 0].astype(jnp.float32) * forward_z.astype(jnp.float32)
    backward_q = backward_rows[:, 0].astype(jnp.float32)
    conv_value = backward_z.astype(jnp.float32)
    backward_y = backward_q * conv_value
    weighted = bwd_cot[0].astype(jnp.float32) * gain_row
    forward_scale = lax.rsqrt(row_total(forward_y * forward_y) / model_width + epsilon)[:, None]
    backward_scale = lax.rsqrt(row_total(backward_y * backward_y) / model_width + epsilon)[:, None]
    normed = backward_y * backward_scale
    average = (row_total(weighted * normed) / model_width)[:, None]
    forward_out = (forward_y * forward_scale * gain_row).astype(jnp.bfloat16)
    grad_y = backward_scale * (weighted - normed * average)
    grad_z = (grad_y * backward_q).astype(jnp.bfloat16)
    grad_cols = lax.all_to_all(
        jnp.transpose(grad_z), "ctx", split_axis=0, concat_axis=1, tiled=True
    )
    grad_re, grad_im = spectrum(grad_cols.astype(jnp.float32), tables)
    input_re, input_im = spec_against(grad_re, grad_im, tap_re, tap_im)
    grad_mix_cols = signal_of(input_re, input_im, tables).astype(jnp.bfloat16)
    taps_re, taps_im = spec_against(grad_re, grad_im, backward_spec[0], backward_spec[1])
    filt_step = signal_of(taps_re, taps_im, tables)
    grad_mix = jnp.transpose(
        lax.all_to_all(grad_mix_cols, "ctx", split_axis=1, concat_axis=0, tiled=True)
    ).astype(jnp.float32)
    section_grads = jnp.stack(
        [
            grad_y * conv_value,
            grad_mix * backward_rows[:, 2].astype(jnp.float32),
            grad_mix * backward_rows[:, 1].astype(jnp.float32),
        ],
        axis=1,
    ).astype(jnp.bfloat16)
    section_grads, filt_step = (section_grads, filt_step)
    sent_rows, sent_grads = from_partner((forward_out, section_grads), "pipe", 0)
    return (sent_rows[None], sent_grads[None], filt_step[None, None])


def on_device(fwd_in, bwd_in, bwd_cot, filter_taps, norm_gain):
    length = filter_taps.shape[3]
    if not dense_fits(length):
        return on_device_factored(fwd_in, bwd_in, bwd_cot, filter_taps, norm_gain)
    model_width = norm_gain.shape[1] * lax.axis_size("tp")
    table = constant_dft_table(length)
    weights = spectral_weights(length)
    tap_spec = dense_taps_spectrum(filter_taps[0, 0], table)
    tap_scaled = tap_spec * weights
    gain_row = norm_gain[0]
    forward_rows = fwd_in[0]
    backward_rows = bwd_in[0]

    def featurize(proj_rows):
        return (proj_rows[:, 1].astype(jnp.float32) * proj_rows[:, 2].astype(jnp.float32)).astype(
            jnp.bfloat16
        )

    def to_columns(rows):
        return lax.all_to_all(rows, "ctx", split_axis=1, concat_axis=0, tiled=True)

    def to_rows(columns):
        return lax.all_to_all(columns, "ctx", split_axis=0, concat_axis=1, tiled=True)

    def row_total(values):
        return lax.psum(jnp.sum(values, axis=1), "tp")

    partner_kv = from_partner(backward_rows[:, 1:3], "pipe", 0)
    forward_cols = to_columns(featurize(forward_rows))
    backward_cols = to_columns(featurize(backward_rows))
    forward_spec = dense_spectrum_exact(forward_cols, table)
    forward_z = to_rows(
        dense_signal(dense_multiply(forward_spec, tap_scaled, False), table).astype(jnp.bfloat16)
    )
    partner_kv, backward_cols = lax.optimization_barrier((partner_kv, backward_cols))
    backward_spec = dense_spectrum_exact(backward_cols, table)
    backward_z = to_rows(
        dense_signal(dense_multiply(backward_spec, tap_scaled, False), table).astype(jnp.bfloat16)
    )
    backward_q = backward_rows[:, 0].astype(jnp.float32)
    conv_value = backward_z.astype(jnp.float32)
    backward_y = backward_q * conv_value
    weighted = bwd_cot[0].astype(jnp.float32) * gain_row
    backward_scale = lax.rsqrt(row_total(backward_y * backward_y) / model_width + epsilon)[:, None]
    normed = backward_y * backward_scale
    average = (row_total(weighted * normed) / model_width)[:, None]
    grad_y = backward_scale * (weighted - normed * average)
    grad_z = (grad_y * backward_q).astype(jnp.bfloat16)
    sent_first = from_partner((grad_y * conv_value).astype(jnp.bfloat16), "pipe", 0)
    grad_cols = to_columns(grad_z)
    forward_z, grad_z = lax.optimization_barrier((forward_z, grad_z))
    forward_y = forward_rows[:, 0].astype(jnp.float32) * forward_z.astype(jnp.float32)
    forward_scale = lax.rsqrt(row_total(forward_y * forward_y) / model_width + epsilon)[:, None]
    forward_out = (forward_y * forward_scale * gain_row).astype(jnp.bfloat16)
    sent_rows = from_partner(forward_out, "pipe", 0)
    grad_spec = dense_spectrum_exact(grad_cols, table) * weights
    mix_prod = dense_multiply(grad_spec, tap_spec, True)
    width = mix_prod.shape[1] // 2 if mix_prod.shape[1] % 256 == 0 else mix_prod.shape[1]
    pieces = mix_prod.shape[1] // width
    first_cols = dense_signal(mix_prod[:, :width], table).astype(jnp.bfloat16)
    sent_rows, sent_first, first_cols = lax.optimization_barrier((sent_rows, sent_first, first_cols))
    sent_parts = [from_partner(to_rows(first_cols), "pipe", 0)]
    for piece in range(1, pieces):
        piece_cols = dense_signal(mix_prod[:, piece * width : (piece + 1) * width], table)
        sent_parts.append(from_partner(to_rows(piece_cols.astype(jnp.bfloat16)), "pipe", 0))
    taps_prod = dense_multiply(grad_spec, backward_spec, True)
    taps_hi, taps_lo = split_bf16(taps_prod)
    table_hi, table_lo = table
    dims = (((0,), (1,)), ((), ()))
    part = lambda a, b: lax.dot_general(a, b, dims, preferred_element_type=jnp.float32)
    filt_step = part(taps_hi, table_hi) + (part(taps_hi, table_lo) + part(taps_lo, table_hi))
    token_rows = sent_parts[0].shape[0]
    ctx_count = lax.axis_size("ctx")
    sent_mix = jnp.stack(
        [p.reshape(token_rows, ctx_count, width) for p in sent_parts], axis=2
    ).reshape(token_rows, -1).astype(jnp.float32)
    rest = jnp.stack(
        [
            sent_mix * partner_kv[:, 1].astype(jnp.float32),
            sent_mix * partner_kv[:, 0].astype(jnp.float32),
        ],
        axis=1,
    ).astype(jnp.bfloat16)
    sent_grads = jnp.concatenate([sent_first[:, None], rest], axis=1)
    return (sent_rows[None], sent_grads[None], filt_step[None, None])


def solution(mesh):
    return jax.shard_map(
        on_device,
        mesh=mesh,
        in_specs=(
            P("pipe", "ctx", None, "tp"),
            P("pipe", "ctx", None, "tp"),
            P("pipe", "ctx", "tp"),
            P("pipe", "tp", "ctx", None),
            P("pipe", "tp"),
        ),
        out_specs=(
            P("pipe", "ctx", "tp"),
            P("pipe", "ctx", None, "tp"),
            P("pipe", "tp", "ctx", None),
        ),
        check_vma=False,
    )
```

```python
import math

import jax
import ml_dtypes
import numpy as np
import jax.numpy as jnp
from jax import lax
from jax.sharding import PartitionSpec as P

epsilon = 1e-06
highest = lax.Precision.HIGHEST


def from_partner(block, axis, bit):
    count = lax.axis_size(axis)
    route = []
    for low in range(count):
        high = low | 1 << bit
        if high != low and high < count:
            route += [(low, high), (high, low)]
    return lax.ppermute(block, axis, route)


def unit_table(count_out, count_in, period):
    product = lax.broadcasted_iota(jnp.int32, (count_out, count_in), 0) * lax.broadcasted_iota(
        jnp.int32, (count_out, count_in), 1
    )
    phase_angle = (product % period).astype(jnp.float32) * (-2.0 * math.pi / period)
    return (jnp.cos(phase_angle), jnp.sin(phase_angle))


def dft_tables(padded):
    blocks = padded // 128
    cos_high, sin_high = unit_table(blocks, blocks, blocks)
    cos_low, sin_low = unit_table(128, 128, 128)
    cos_twist, sin_twist = unit_table(blocks, 128, padded)
    return (cos_high, sin_high, cos_low, sin_low, cos_twist, sin_twist)


def spectrum(signal, tables):
    cos_high, sin_high, cos_low, sin_low, cos_twist, sin_twist = tables
    channels = signal.shape[0]
    half_blocks = signal.shape[1] // 128
    folded = signal.reshape(channels, half_blocks, 128)
    first_re = jnp.einsum("can,ak->ckn", folded, cos_high[:half_blocks], precision=highest)
    first_im = jnp.einsum("can,ak->ckn", folded, sin_high[:half_blocks], precision=highest)
    turned_re = first_re * cos_twist - first_im * sin_twist
    turned_im = first_re * sin_twist + first_im * cos_twist
    spec_re = jnp.einsum("ckn,nj->ckj", turned_re, cos_low, precision=highest) - jnp.einsum(
        "ckn,nj->ckj", turned_im, sin_low, precision=highest
    )
    spec_im = jnp.einsum("ckn,nj->ckj", turned_re, sin_low, precision=highest) + jnp.einsum(
        "ckn,nj->ckj", turned_im, cos_low, precision=highest
    )
    return (spec_re, spec_im)


def signal_of(spec_re, spec_im, tables):
    cos_high, sin_high, cos_low, sin_low, cos_twist, sin_twist = tables
    channels = spec_re.shape[0]
    blocks = spec_re.shape[1]
    half_blocks = blocks // 2
    mid_re = jnp.einsum("ckj,jn->ckn", spec_re, cos_low, precision=highest) + jnp.einsum(
        "ckj,jn->ckn", spec_im, sin_low, precision=highest
    )
    mid_im = jnp.einsum("ckj,jn->ckn", spec_im, cos_low, precision=highest) - jnp.einsum(
        "ckj,jn->ckn", spec_re, sin_low, precision=highest
    )
    back_re = mid_re * cos_twist + mid_im * sin_twist
    back_im = mid_im * cos_twist - mid_re * sin_twist
    values = jnp.einsum(
        "ak,ckn->can", cos_high[:half_blocks], back_re, precision=highest
    ) + jnp.einsum("ak,ckn->can", sin_high[:half_blocks], back_im, precision=highest)
    return values.reshape(channels, half_blocks * 128) / (blocks * 128)


def spec_product(a_re, a_im, b_re, b_im):
    return (a_re * b_re - a_im * b_im, a_re * b_im + a_im * b_re)


def spec_against(a_re, a_im, b_re, b_im):
    return (a_re * b_re + a_im * b_im, a_im * b_re - a_re * b_im)


def split_bf16(values):
    high = lax.reduce_precision(values, exponent_bits=8, mantissa_bits=7)
    return (high.astype(jnp.bfloat16), (values - high).astype(jnp.bfloat16))


def unit_angles(count_rows, count_cols, stride, padded):
    rows = lax.broadcasted_iota(jnp.int32, (count_rows, count_cols), 0) * stride
    cols = lax.broadcasted_iota(jnp.int32, (count_rows, count_cols), 1)
    angle = ((rows * cols) % padded).astype(jnp.float32) * (2.0 * math.pi / padded)
    return (jnp.cos(angle), jnp.sin(angle))


def real_dft_table(length):
    padded = 2 * length
    inner = 1 << (length.bit_length() // 2)
    if length % inner:
        inner = 1
    outer = length // inner
    cos_outer, sin_outer = unit_angles(outer, length, inner, padded)
    cos_inner, sin_inner = unit_angles(inner, length, 1, padded)
    cos_full = (cos_outer[:, None] * cos_inner[None] - sin_outer[:, None] * sin_inner[None]).reshape(
        length, length
    )
    sin_full = (sin_outer[:, None] * cos_inner[None] + cos_outer[:, None] * sin_inner[None]).reshape(
        length, length
    )
    rows = lax.broadcasted_iota(jnp.int32, (length, length), 0)
    cols = lax.broadcasted_iota(jnp.int32, (length, length), 1)
    alternating = jnp.where(rows % 2 == 0, 1.0, -1.0).astype(jnp.float32)
    sin_part = jnp.where(cols == 0, alternating, -sin_full)
    table = jnp.concatenate([cos_full, sin_part], axis=1)
    return split_bf16(table)


def constant_dft_table(length):
    padded = 2 * length
    rows = np.arange(length, dtype=np.int64)[:, None]
    cols = np.arange(length, dtype=np.int64)[None, :]
    angle = ((rows * cols) % padded).astype(np.float64) * (2.0 * np.pi / padded)
    alternating = np.where(rows % 2 == 0, 1.0, -1.0)
    sin_part = np.where(cols == 0, alternating, -np.sin(angle))
    table = np.concatenate([np.cos(angle), sin_part], axis=1).astype(np.float32)
    high = table.astype(ml_dtypes.bfloat16)
    low = (table - high.astype(np.float32)).astype(ml_dtypes.bfloat16)
    return (jnp.asarray(high), jnp.asarray(low))


def dot_tf(table, signal):
    return lax.dot_general(
        table, signal, (((0,), (0,)), ((), ())), preferred_element_type=jnp.float32
    )


def dot_tt(table, spec):
    return lax.dot_general(
        table, spec, (((1,), (0,)), ((), ())), preferred_element_type=jnp.float32
    )


def dense_spectrum_exact(rows_bf16, table):
    table_hi, table_lo = table
    return dot_tf(table_hi, rows_bf16) + dot_tf(table_lo, rows_bf16)


def dense_signal(spec, table):
    table_hi, table_lo = table
    spec_hi, spec_lo = split_bf16(spec)
    return dot_tt(table_hi, spec_hi) + (dot_tt(table_lo, spec_hi) + dot_tt(table_hi, spec_lo))


def dense_taps_spectrum(taps, table):
    table_hi, table_lo = table
    taps_hi, taps_lo = split_bf16(taps)
    dims = (((0,), (1,)), ((), ()))
    part = lambda a, b: lax.dot_general(a, b, dims, preferred_element_type=jnp.float32)
    return part(table_hi, taps_hi) + (part(table_lo, taps_hi) + part(table_hi, taps_lo))


def spectral_weights(length):
    index = lax.broadcasted_iota(jnp.int32, (2 * length, 1), 0)
    edge = (index == 0) | (index == length)
    return jnp.where(edge, 1.0, 2.0).astype(jnp.float32) / (2 * length)


def dense_multiply(a, b, conjugate):
    length = a.shape[0] // 2
    a_re, a_im = a[:length], a[length:]
    b_re, b_im = b[:length], b[length:]
    first = lax.broadcasted_iota(jnp.int32, (length, 1), 0) == 0
    if conjugate:
        re = a_re * b_re + a_im * b_im
        im = a_im * b_re - a_re * b_im
    else:
        re = a_re * b_re - a_im * b_im
        im = a_re * b_im + a_im * b_re
    re = jnp.where(first, a_re * b_re, re)
    im = jnp.where(first, a_im * b_im, im)
    return jnp.concatenate([re, im], axis=0)


def dense_fits(length):
    return 4 * length * length * 2 <= 16 * 1024 * 1024


def on_device_factored(fwd_in, bwd_in, bwd_cot, filter_taps, norm_gain):
    model_width = norm_gain.shape[1] * lax.axis_size("tp")
    local_taps = filter_taps[0, 0]
    tables = dft_tables(2 * local_taps.shape[1])
    tap_re, tap_im = spectrum(local_taps, tables)
    gain_row = norm_gain[0]
    forward_rows = fwd_in[0]
    backward_rows = bwd_in[0]

    def featurize(proj_rows):
        return (proj_rows[:, 1].astype(jnp.float32) * proj_rows[:, 2].astype(jnp.float32)).astype(
            jnp.bfloat16
        )

    def convolve(columns):
        sig_re, sig_im = spectrum(columns.astype(jnp.float32), tables)
        prod_re, prod_im = spec_product(sig_re, sig_im, tap_re, tap_im)
        return (signal_of(prod_re, prod_im, tables).astype(jnp.bfloat16), (sig_re, sig_im))

    def relayout(mixed_rows):
        columns = lax.all_to_all(
            jnp.transpose(mixed_rows), "ctx", split_axis=0, concat_axis=1, tiled=True
        )
        result, kept_spec = convolve(columns)
        return (
            jnp.transpose(lax.all_to_all(result, "ctx", split_axis=1, concat_axis=0, tiled=True)),
            kept_spec,
        )

    def row_total(values):
        return lax.psum(jnp.sum(values, axis=1), "tp")

    forward_mix = featurize(forward_rows)
    backward_mix = featurize(backward_rows)
    forward_z = relayout(forward_mix)[0]
    backward_z, backward_spec = relayout(backward_mix)
    forward_y = forward_rows[:, 0].astype(jnp.float32) * forward_z.astype(jnp.float32)
    backward_q = backward_rows[:, 0].astype(jnp.float32)
    conv_value = backward_z.astype(jnp.float32)
    backward_y = backward_q * conv_value
    weighted = bwd_cot[0].astype(jnp.float32) * gain_row
    forward_scale = lax.rsqrt(row_total(forward_y * forward_y) / model_width + epsilon)[:, None]
    backward_scale = lax.rsqrt(row_total(backward_y * backward_y) / model_width + epsilon)[:, None]
    normed = backward_y * backward_scale
    average = (row_total(weighted * normed) / model_width)[:, None]
    forward_out = (forward_y * forward_scale * gain_row).astype(jnp.bfloat16)
    grad_y = backward_scale * (weighted - normed * average)
    grad_z = (grad_y * backward_q).astype(jnp.bfloat16)
    grad_cols = lax.all_to_all(
        jnp.transpose(grad_z), "ctx", split_axis=0, concat_axis=1, tiled=True
    )
    grad_re, grad_im = spectrum(grad_cols.astype(jnp.float32), tables)
    input_re, input_im = spec_against(grad_re, grad_im, tap_re, tap_im)
    grad_mix_cols = signal_of(input_re, input_im, tables).astype(jnp.bfloat16)
    taps_re, taps_im = spec_against(grad_re, grad_im, backward_spec[0], backward_spec[1])
    filt_step = signal_of(taps_re, taps_im, tables)
    grad_mix = jnp.transpose(
        lax.all_to_all(grad_mix_cols, "ctx", split_axis=1, concat_axis=0, tiled=True)
    ).astype(jnp.float32)
    section_grads = jnp.stack(
        [
            grad_y * conv_value,
            grad_mix * backward_rows[:, 2].astype(jnp.float32),
            grad_mix * backward_rows[:, 1].astype(jnp.float32),
        ],
        axis=1,
    ).astype(jnp.bfloat16)
    section_grads, filt_step = (section_grads, filt_step)
    sent_rows, sent_grads = from_partner((forward_out, section_grads), "pipe", 0)
    return (sent_rows[None], sent_grads[None], filt_step[None, None])


def on_device(fwd_in, bwd_in, bwd_cot, filter_taps, norm_gain):
    length = filter_taps.shape[3]
    if not dense_fits(length):
        return on_device_factored(fwd_in, bwd_in, bwd_cot, filter_taps, norm_gain)
    model_width = norm_gain.shape[1] * lax.axis_size("tp")
    table = constant_dft_table(length)
    weights = spectral_weights(length)
    tap_spec = dense_taps_spectrum(filter_taps[0, 0], table)
    tap_scaled = tap_spec * weights
    gain_row = norm_gain[0]
    forward_rows = fwd_in[0]
    backward_rows = bwd_in[0]

    def featurize(proj_rows):
        return (proj_rows[:, 1].astype(jnp.float32) * proj_rows[:, 2].astype(jnp.float32)).astype(
            jnp.bfloat16
        )

    def to_columns(rows):
        return lax.all_to_all(rows, "ctx", split_axis=1, concat_axis=0, tiled=True)

    def to_rows(columns):
        return lax.all_to_all(columns, "ctx", split_axis=0, concat_axis=1, tiled=True)

    def row_total(values):
        return lax.psum(jnp.sum(values, axis=1), "tp")

    partner_kv = from_partner(backward_rows[:, 1:3], "pipe", 0)
    forward_cols = to_columns(featurize(forward_rows))
    backward_cols = to_columns(featurize(backward_rows))
    forward_spec = dense_spectrum_exact(forward_cols, table)
    forward_z = to_rows(
        dense_signal(dense_multiply(forward_spec, tap_scaled, False), table).astype(jnp.bfloat16)
    )
    partner_kv, backward_cols = lax.optimization_barrier((partner_kv, backward_cols))
    backward_spec = dense_spectrum_exact(backward_cols, table)
    backward_z = to_rows(
        dense_signal(dense_multiply(backward_spec, tap_scaled, False), table).astype(jnp.bfloat16)
    )
    forward_y = forward_rows[:, 0].astype(jnp.float32) * forward_z.astype(jnp.float32)
    forward_scale = lax.rsqrt(row_total(forward_y * forward_y) / model_width + epsilon)[:, None]
    forward_out = (forward_y * forward_scale * gain_row).astype(jnp.bfloat16)
    sent_rows = from_partner(forward_out, "pipe", 0)
    backward_q = backward_rows[:, 0].astype(jnp.float32)
    conv_value = backward_z.astype(jnp.float32)
    backward_y = backward_q * conv_value
    weighted = bwd_cot[0].astype(jnp.float32) * gain_row
    backward_scale = lax.rsqrt(row_total(backward_y * backward_y) / model_width + epsilon)[:, None]
    normed = backward_y * backward_scale
    average = (row_total(weighted * normed) / model_width)[:, None]
    grad_y = backward_scale * (weighted - normed * average)
    grad_z = (grad_y * backward_q).astype(jnp.bfloat16)
    sent_first = from_partner((grad_y * conv_value).astype(jnp.bfloat16), "pipe", 0)
    grad_cols = to_columns(grad_z)
    grad_spec = dense_spectrum_exact(grad_cols, table) * weights
    mix_prod = dense_multiply(grad_spec, tap_spec, True)
    width = mix_prod.shape[1] // 2 if mix_prod.shape[1] % 256 == 0 else mix_prod.shape[1]
    pieces = mix_prod.shape[1] // width
    first_cols = dense_signal(mix_prod[:, :width], table).astype(jnp.bfloat16)
    sent_rows, sent_first, first_cols = lax.optimization_barrier((sent_rows, sent_first, first_cols))
    sent_parts = [from_partner(to_rows(first_cols), "pipe", 0)]
    for piece in range(1, pieces):
        piece_cols = dense_signal(mix_prod[:, piece * width : (piece + 1) * width], table)
        sent_parts.append(from_partner(to_rows(piece_cols.astype(jnp.bfloat16)), "pipe", 0))
    taps_prod = dense_multiply(grad_spec, backward_spec, True)
    taps_hi, taps_lo = split_bf16(taps_prod)
    table_hi, table_lo = table
    dims = (((0,), (1,)), ((), ()))
    part = lambda a, b: lax.dot_general(a, b, dims, preferred_element_type=jnp.float32)
    filt_step = part(taps_hi, table_hi) + (part(taps_hi, table_lo) + part(taps_lo, table_hi))
    token_rows = sent_parts[0].shape[0]
    ctx_count = lax.axis_size("ctx")
    kv_pieces = partner_kv.reshape(token_rows, 2, ctx_count, pieces, width)
    grad_pieces = []
    for piece, received in enumerate(sent_parts):
        received = received.reshape(token_rows, ctx_count, width).astype(jnp.float32)
        grad_pieces.append(
            jnp.stack(
                [
                    received * kv_pieces[:, 1, :, piece].astype(jnp.float32),
                    received * kv_pieces[:, 0, :, piece].astype(jnp.float32),
                ],
                axis=1,
            ).astype(jnp.bfloat16)
        )
    rest = jnp.stack(grad_pieces, axis=3).reshape(token_rows, 2, -1)
    sent_grads = jnp.concatenate([sent_first[:, None], rest], axis=1)
    return (sent_rows[None], sent_grads[None], filt_step[None, None])


def solution(mesh):
    return jax.shard_map(
        on_device,
        mesh=mesh,
        in_specs=(
            P("pipe", "ctx", None, "tp"),
            P("pipe", "ctx", None, "tp"),
            P("pipe", "ctx", "tp"),
            P("pipe", "tp", "ctx", None),
            P("pipe", "tp"),
        ),
        out_specs=(
            P("pipe", "ctx", "tp"),
            P("pipe", "ctx", None, "tp"),
            P("pipe", "tp", "ctx", None),
        ),
        check_vma=False,
    )
```

```python
import math

import jax
import ml_dtypes
import numpy as np
import jax.numpy as jnp
from jax import lax
from jax.sharding import PartitionSpec as P

epsilon = 1e-06
highest = lax.Precision.HIGHEST


def from_partner(block, axis, bit):
    count = lax.axis_size(axis)
    route = []
    for low in range(count):
        high = low | 1 << bit
        if high != low and high < count:
            route += [(low, high), (high, low)]
    return lax.ppermute(block, axis, route)


def unit_table(count_out, count_in, period):
    product = lax.broadcasted_iota(jnp.int32, (count_out, count_in), 0) * lax.broadcasted_iota(
        jnp.int32, (count_out, count_in), 1
    )
    phase_angle = (product % period).astype(jnp.float32) * (-2.0 * math.pi / period)
    return (jnp.cos(phase_angle), jnp.sin(phase_angle))


def dft_tables(padded):
    blocks = padded // 128
    cos_high, sin_high = unit_table(blocks, blocks, blocks)
    cos_low, sin_low = unit_table(128, 128, 128)
    cos_twist, sin_twist = unit_table(blocks, 128, padded)
    return (cos_high, sin_high, cos_low, sin_low, cos_twist, sin_twist)


def spectrum(signal, tables):
    cos_high, sin_high, cos_low, sin_low, cos_twist, sin_twist = tables
    channels = signal.shape[0]
    half_blocks = signal.shape[1] // 128
    folded = signal.reshape(channels, half_blocks, 128)
    first_re = jnp.einsum("can,ak->ckn", folded, cos_high[:half_blocks], precision=highest)
    first_im = jnp.einsum("can,ak->ckn", folded, sin_high[:half_blocks], precision=highest)
    turned_re = first_re * cos_twist - first_im * sin_twist
    turned_im = first_re * sin_twist + first_im * cos_twist
    spec_re = jnp.einsum("ckn,nj->ckj", turned_re, cos_low, precision=highest) - jnp.einsum(
        "ckn,nj->ckj", turned_im, sin_low, precision=highest
    )
    spec_im = jnp.einsum("ckn,nj->ckj", turned_re, sin_low, precision=highest) + jnp.einsum(
        "ckn,nj->ckj", turned_im, cos_low, precision=highest
    )
    return (spec_re, spec_im)


def signal_of(spec_re, spec_im, tables):
    cos_high, sin_high, cos_low, sin_low, cos_twist, sin_twist = tables
    channels = spec_re.shape[0]
    blocks = spec_re.shape[1]
    half_blocks = blocks // 2
    mid_re = jnp.einsum("ckj,jn->ckn", spec_re, cos_low, precision=highest) + jnp.einsum(
        "ckj,jn->ckn", spec_im, sin_low, precision=highest
    )
    mid_im = jnp.einsum("ckj,jn->ckn", spec_im, cos_low, precision=highest) - jnp.einsum(
        "ckj,jn->ckn", spec_re, sin_low, precision=highest
    )
    back_re = mid_re * cos_twist + mid_im * sin_twist
    back_im = mid_im * cos_twist - mid_re * sin_twist
    values = jnp.einsum(
        "ak,ckn->can", cos_high[:half_blocks], back_re, precision=highest
    ) + jnp.einsum("ak,ckn->can", sin_high[:half_blocks], back_im, precision=highest)
    return values.reshape(channels, half_blocks * 128) / (blocks * 128)


def spec_product(a_re, a_im, b_re, b_im):
    return (a_re * b_re - a_im * b_im, a_re * b_im + a_im * b_re)


def spec_against(a_re, a_im, b_re, b_im):
    return (a_re * b_re + a_im * b_im, a_im * b_re - a_re * b_im)


def split_bf16(values):
    high = lax.reduce_precision(values, exponent_bits=8, mantissa_bits=7)
    return (high.astype(jnp.bfloat16), (values - high).astype(jnp.bfloat16))


def unit_angles(count_rows, count_cols, stride, padded):
    rows = lax.broadcasted_iota(jnp.int32, (count_rows, count_cols), 0) * stride
    cols = lax.broadcasted_iota(jnp.int32, (count_rows, count_cols), 1)
    angle = ((rows * cols) % padded).astype(jnp.float32) * (2.0 * math.pi / padded)
    return (jnp.cos(angle), jnp.sin(angle))


def real_dft_table(length):
    padded = 2 * length
    inner = 1 << (length.bit_length() // 2)
    if length % inner:
        inner = 1
    outer = length // inner
    cos_outer, sin_outer = unit_angles(outer, length, inner, padded)
    cos_inner, sin_inner = unit_angles(inner, length, 1, padded)
    cos_full = (cos_outer[:, None] * cos_inner[None] - sin_outer[:, None] * sin_inner[None]).reshape(
        length, length
    )
    sin_full = (sin_outer[:, None] * cos_inner[None] + cos_outer[:, None] * sin_inner[None]).reshape(
        length, length
    )
    rows = lax.broadcasted_iota(jnp.int32, (length, length), 0)
    cols = lax.broadcasted_iota(jnp.int32, (length, length), 1)
    alternating = jnp.where(rows % 2 == 0, 1.0, -1.0).astype(jnp.float32)
    sin_part = jnp.where(cols == 0, alternating, -sin_full)
    table = jnp.concatenate([cos_full, sin_part], axis=1)
    return split_bf16(table)


def constant_dft_table(length):
    padded = 2 * length
    rows = np.arange(length, dtype=np.int64)[:, None]
    cols = np.arange(length, dtype=np.int64)[None, :]
    angle = ((rows * cols) % padded).astype(np.float64) * (2.0 * np.pi / padded)
    alternating = np.where(rows % 2 == 0, 1.0, -1.0)
    sin_part = np.where(cols == 0, alternating, -np.sin(angle))
    table = np.concatenate([np.cos(angle), sin_part], axis=1).astype(np.float32)
    high = table.astype(ml_dtypes.bfloat16)
    low = (table - high.astype(np.float32)).astype(ml_dtypes.bfloat16)
    return (jnp.asarray(high), jnp.asarray(low))


def dot_tf(table, signal):
    return lax.dot_general(
        table, signal, (((0,), (0,)), ((), ())), preferred_element_type=jnp.float32
    )


def dot_tt(table, spec):
    return lax.dot_general(
        table, spec, (((1,), (0,)), ((), ())), preferred_element_type=jnp.float32
    )


def dense_spectrum_exact(rows_bf16, table):
    table_hi, table_lo = table
    return dot_tf(table_hi, rows_bf16) + dot_tf(table_lo, rows_bf16)


def dense_signal(spec, table):
    table_hi, table_lo = table
    spec_hi, spec_lo = split_bf16(spec)
    return dot_tt(table_hi, spec_hi) + (dot_tt(table_lo, spec_hi) + dot_tt(table_hi, spec_lo))


def dense_taps_spectrum(taps, table):
    table_hi, table_lo = table
    taps_hi, taps_lo = split_bf16(taps)
    dims = (((0,), (1,)), ((), ()))
    part = lambda a, b: lax.dot_general(a, b, dims, preferred_element_type=jnp.float32)
    return part(table_hi, taps_hi) + (part(table_lo, taps_hi) + part(table_hi, taps_lo))


def spectral_weights(length):
    index = lax.broadcasted_iota(jnp.int32, (2 * length, 1), 0)
    edge = (index == 0) | (index == length)
    return jnp.where(edge, 1.0, 2.0).astype(jnp.float32) / (2 * length)


def dense_multiply(a, b, conjugate):
    length = a.shape[0] // 2
    a_re, a_im = a[:length], a[length:]
    b_re, b_im = b[:length], b[length:]
    first = lax.broadcasted_iota(jnp.int32, (length, 1), 0) == 0
    if conjugate:
        re = a_re * b_re + a_im * b_im
        im = a_im * b_re - a_re * b_im
    else:
        re = a_re * b_re - a_im * b_im
        im = a_re * b_im + a_im * b_re
    re = jnp.where(first, a_re * b_re, re)
    im = jnp.where(first, a_im * b_im, im)
    return jnp.concatenate([re, im], axis=0)


def dense_fits(length):
    return 4 * length * length * 2 <= 16 * 1024 * 1024


def on_device_factored(fwd_in, bwd_in, bwd_cot, filter_taps, norm_gain):
    model_width = norm_gain.shape[1] * lax.axis_size("tp")
    local_taps = filter_taps[0, 0]
    tables = dft_tables(2 * local_taps.shape[1])
    tap_re, tap_im = spectrum(local_taps, tables)
    gain_row = norm_gain[0]
    forward_rows = fwd_in[0]
    backward_rows = bwd_in[0]

    def featurize(proj_rows):
        return (proj_rows[:, 1].astype(jnp.float32) * proj_rows[:, 2].astype(jnp.float32)).astype(
            jnp.bfloat16
        )

    def convolve(columns):
        sig_re, sig_im = spectrum(columns.astype(jnp.float32), tables)
        prod_re, prod_im = spec_product(sig_re, sig_im, tap_re, tap_im)
        return (signal_of(prod_re, prod_im, tables).astype(jnp.bfloat16), (sig_re, sig_im))

    def relayout(mixed_rows):
        columns = lax.all_to_all(
            jnp.transpose(mixed_rows), "ctx", split_axis=0, concat_axis=1, tiled=True
        )
        result, kept_spec = convolve(columns)
        return (
            jnp.transpose(lax.all_to_all(result, "ctx", split_axis=1, concat_axis=0, tiled=True)),
            kept_spec,
        )

    def row_total(values):
        return lax.psum(jnp.sum(values, axis=1), "tp")

    forward_mix = featurize(forward_rows)
    backward_mix = featurize(backward_rows)
    forward_z = relayout(forward_mix)[0]
    backward_z, backward_spec = relayout(backward_mix)
    forward_y = forward_rows[:, 0].astype(jnp.float32) * forward_z.astype(jnp.float32)
    backward_q = backward_rows[:, 0].astype(jnp.float32)
    conv_value = backward_z.astype(jnp.float32)
    backward_y = backward_q * conv_value
    weighted = bwd_cot[0].astype(jnp.float32) * gain_row
    forward_scale = lax.rsqrt(row_total(forward_y * forward_y) / model_width + epsilon)[:, None]
    backward_scale = lax.rsqrt(row_total(backward_y * backward_y) / model_width + epsilon)[:, None]
    normed = backward_y * backward_scale
    average = (row_total(weighted * normed) / model_width)[:, None]
    forward_out = (forward_y * forward_scale * gain_row).astype(jnp.bfloat16)
    grad_y = backward_scale * (weighted - normed * average)
    grad_z = (grad_y * backward_q).astype(jnp.bfloat16)
    grad_cols = lax.all_to_all(
        jnp.transpose(grad_z), "ctx", split_axis=0, concat_axis=1, tiled=True
    )
    grad_re, grad_im = spectrum(grad_cols.astype(jnp.float32), tables)
    input_re, input_im = spec_against(grad_re, grad_im, tap_re, tap_im)
    grad_mix_cols = signal_of(input_re, input_im, tables).astype(jnp.bfloat16)
    taps_re, taps_im = spec_against(grad_re, grad_im, backward_spec[0], backward_spec[1])
    filt_step = signal_of(taps_re, taps_im, tables)
    grad_mix = jnp.transpose(
        lax.all_to_all(grad_mix_cols, "ctx", split_axis=1, concat_axis=0, tiled=True)
    ).astype(jnp.float32)
    section_grads = jnp.stack(
        [
            grad_y * conv_value,
            grad_mix * backward_rows[:, 2].astype(jnp.float32),
            grad_mix * backward_rows[:, 1].astype(jnp.float32),
        ],
        axis=1,
    ).astype(jnp.bfloat16)
    section_grads, filt_step = (section_grads, filt_step)
    sent_rows, sent_grads = from_partner((forward_out, section_grads), "pipe", 0)
    return (sent_rows[None], sent_grads[None], filt_step[None, None])


def on_device(fwd_in, bwd_in, bwd_cot, filter_taps, norm_gain):
    length = filter_taps.shape[3]
    if not dense_fits(length):
        return on_device_factored(fwd_in, bwd_in, bwd_cot, filter_taps, norm_gain)
    model_width = norm_gain.shape[1] * lax.axis_size("tp")
    table = constant_dft_table(length)
    weights = spectral_weights(length)
    tap_spec = dense_taps_spectrum(filter_taps[0, 0], table)
    tap_scaled = tap_spec * weights
    gain_row = norm_gain[0]
    forward_rows = fwd_in[0]
    backward_rows = bwd_in[0]

    def featurize(proj_rows):
        return (proj_rows[:, 1].astype(jnp.float32) * proj_rows[:, 2].astype(jnp.float32)).astype(
            jnp.bfloat16
        )

    def to_columns(rows):
        return lax.all_to_all(rows, "ctx", split_axis=1, concat_axis=0, tiled=True)

    def to_rows(columns):
        return lax.all_to_all(columns, "ctx", split_axis=0, concat_axis=1, tiled=True)

    def row_total(values):
        return lax.psum(jnp.sum(values, axis=1), "tp")

    partner_kv = from_partner(backward_rows[:, 1:3], "pipe", 0)
    forward_cols = to_columns(featurize(forward_rows))
    backward_cols = to_columns(featurize(backward_rows))
    forward_spec = dense_spectrum_exact(forward_cols, table)
    forward_z = to_rows(
        dense_signal(dense_multiply(forward_spec, tap_scaled, False), table).astype(jnp.bfloat16)
    )
    partner_kv, backward_cols = lax.optimization_barrier((partner_kv, backward_cols))
    backward_spec = dense_spectrum_exact(backward_cols, table)
    backward_z = to_rows(
        dense_signal(dense_multiply(backward_spec, tap_scaled, False), table).astype(jnp.bfloat16)
    )
    forward_y = forward_rows[:, 0].astype(jnp.float32) * forward_z.astype(jnp.float32)
    forward_scale = lax.rsqrt(row_total(forward_y * forward_y) / model_width + epsilon)[:, None]
    forward_out = (forward_y * forward_scale * gain_row).astype(jnp.bfloat16)
    sent_rows = from_partner(forward_out, "pipe", 0)
    backward_q = backward_rows[:, 0].astype(jnp.float32)
    conv_value = backward_z.astype(jnp.float32)
    backward_y = backward_q * conv_value
    weighted = bwd_cot[0].astype(jnp.float32) * gain_row
    backward_scale = lax.rsqrt(row_total(backward_y * backward_y) / model_width + epsilon)[:, None]
    normed = backward_y * backward_scale
    average = (row_total(weighted * normed) / model_width)[:, None]
    grad_y = backward_scale * (weighted - normed * average)
    grad_z = (grad_y * backward_q).astype(jnp.bfloat16)
    sent_first = from_partner((grad_y * conv_value).astype(jnp.bfloat16), "pipe", 0)
    grad_cols = to_columns(grad_z)
    grad_spec = dense_spectrum_exact(grad_cols, table) * weights
    mix_prod = dense_multiply(grad_spec, tap_spec, True)
    width = mix_prod.shape[1] // 2 if mix_prod.shape[1] % 256 == 0 else mix_prod.shape[1]
    pieces = mix_prod.shape[1] // width
    first_cols = dense_signal(mix_prod[:, :width], table).astype(jnp.bfloat16)
    sent_rows, sent_first, first_cols = lax.optimization_barrier((sent_rows, sent_first, first_cols))
    sent_parts = [from_partner(to_rows(first_cols), "pipe", 0)]
    for piece in range(1, pieces):
        piece_cols = dense_signal(mix_prod[:, piece * width : (piece + 1) * width], table)
        piece_rows = to_rows(piece_cols.astype(jnp.bfloat16))
        sent_parts[-1], piece_rows = lax.optimization_barrier((sent_parts[-1], piece_rows))
        sent_parts.append(from_partner(piece_rows, "pipe", 0))
    taps_prod = dense_multiply(grad_spec, backward_spec, True)
    taps_hi, taps_lo = split_bf16(taps_prod)
    table_hi, table_lo = table
    dims = (((0,), (1,)), ((), ()))
    part = lambda a, b: lax.dot_general(a, b, dims, preferred_element_type=jnp.float32)
    filt_step = part(taps_hi, table_hi) + (part(taps_hi, table_lo) + part(taps_lo, table_hi))
    token_rows = sent_parts[0].shape[0]
    ctx_count = lax.axis_size("ctx")
    sent_mix = jnp.stack(
        [p.reshape(token_rows, ctx_count, width) for p in sent_parts], axis=2
    ).reshape(token_rows, -1).astype(jnp.float32)
    rest = jnp.stack(
        [
            sent_mix * partner_kv[:, 1].astype(jnp.float32),
            sent_mix * partner_kv[:, 0].astype(jnp.float32),
        ],
        axis=1,
    ).astype(jnp.bfloat16)
    sent_grads = jnp.concatenate([sent_first[:, None], rest], axis=1)
    return (sent_rows[None], sent_grads[None], filt_step[None, None])


def solution(mesh):
    return jax.shard_map(
        on_device,
        mesh=mesh,
        in_specs=(
            P("pipe", "ctx", None, "tp"),
            P("pipe", "ctx", None, "tp"),
            P("pipe", "ctx", "tp"),
            P("pipe", "tp", "ctx", None),
            P("pipe", "tp"),
        ),
        out_specs=(
            P("pipe", "ctx", "tp"),
            P("pipe", "ctx", None, "tp"),
            P("pipe", "tp", "ctx", None),
        ),
        check_vma=False,
    )
```

```python
import math

import jax
import ml_dtypes
import numpy as np
import jax.numpy as jnp
from jax import lax
from jax.sharding import PartitionSpec as P

epsilon = 1e-06
highest = lax.Precision.HIGHEST


def from_partner(block, axis, bit):
    count = lax.axis_size(axis)
    route = []
    for low in range(count):
        high = low | 1 << bit
        if high != low and high < count:
            route += [(low, high), (high, low)]
    return lax.ppermute(block, axis, route)


def unit_table(count_out, count_in, period):
    product = lax.broadcasted_iota(jnp.int32, (count_out, count_in), 0) * lax.broadcasted_iota(
        jnp.int32, (count_out, count_in), 1
    )
    phase_angle = (product % period).astype(jnp.float32) * (-2.0 * math.pi / period)
    return (jnp.cos(phase_angle), jnp.sin(phase_angle))


def dft_tables(padded):
    blocks = padded // 128
    cos_high, sin_high = unit_table(blocks, blocks, blocks)
    cos_low, sin_low = unit_table(128, 128, 128)
    cos_twist, sin_twist = unit_table(blocks, 128, padded)
    return (cos_high, sin_high, cos_low, sin_low, cos_twist, sin_twist)


def spectrum(signal, tables):
    cos_high, sin_high, cos_low, sin_low, cos_twist, sin_twist = tables
    channels = signal.shape[0]
    half_blocks = signal.shape[1] // 128
    folded = signal.reshape(channels, half_blocks, 128)
    first_re = jnp.einsum("can,ak->ckn", folded, cos_high[:half_blocks], precision=highest)
    first_im = jnp.einsum("can,ak->ckn", folded, sin_high[:half_blocks], precision=highest)
    turned_re = first_re * cos_twist - first_im * sin_twist
    turned_im = first_re * sin_twist + first_im * cos_twist
    spec_re = jnp.einsum("ckn,nj->ckj", turned_re, cos_low, precision=highest) - jnp.einsum(
        "ckn,nj->ckj", turned_im, sin_low, precision=highest
    )
    spec_im = jnp.einsum("ckn,nj->ckj", turned_re, sin_low, precision=highest) + jnp.einsum(
        "ckn,nj->ckj", turned_im, cos_low, precision=highest
    )
    return (spec_re, spec_im)


def signal_of(spec_re, spec_im, tables):
    cos_high, sin_high, cos_low, sin_low, cos_twist, sin_twist = tables
    channels = spec_re.shape[0]
    blocks = spec_re.shape[1]
    half_blocks = blocks // 2
    mid_re = jnp.einsum("ckj,jn->ckn", spec_re, cos_low, precision=highest) + jnp.einsum(
        "ckj,jn->ckn", spec_im, sin_low, precision=highest
    )
    mid_im = jnp.einsum("ckj,jn->ckn", spec_im, cos_low, precision=highest) - jnp.einsum(
        "ckj,jn->ckn", spec_re, sin_low, precision=highest
    )
    back_re = mid_re * cos_twist + mid_im * sin_twist
    back_im = mid_im * cos_twist - mid_re * sin_twist
    values = jnp.einsum(
        "ak,ckn->can", cos_high[:half_blocks], back_re, precision=highest
    ) + jnp.einsum("ak,ckn->can", sin_high[:half_blocks], back_im, precision=highest)
    return values.reshape(channels, half_blocks * 128) / (blocks * 128)


def spec_product(a_re, a_im, b_re, b_im):
    return (a_re * b_re - a_im * b_im, a_re * b_im + a_im * b_re)


def spec_against(a_re, a_im, b_re, b_im):
    return (a_re * b_re + a_im * b_im, a_im * b_re - a_re * b_im)


def split_bf16(values):
    high = lax.reduce_precision(values, exponent_bits=8, mantissa_bits=7)
    return (high.astype(jnp.bfloat16), (values - high).astype(jnp.bfloat16))


def unit_angles(count_rows, count_cols, stride, padded):
    rows = lax.broadcasted_iota(jnp.int32, (count_rows, count_cols), 0) * stride
    cols = lax.broadcasted_iota(jnp.int32, (count_rows, count_cols), 1)
    angle = ((rows * cols) % padded).astype(jnp.float32) * (2.0 * math.pi / padded)
    return (jnp.cos(angle), jnp.sin(angle))


def real_dft_table(length):
    padded = 2 * length
    inner = 1 << (length.bit_length() // 2)
    if length % inner:
        inner = 1
    outer = length // inner
    cos_outer, sin_outer = unit_angles(outer, length, inner, padded)
    cos_inner, sin_inner = unit_angles(inner, length, 1, padded)
    cos_full = (cos_outer[:, None] * cos_inner[None] - sin_outer[:, None] * sin_inner[None]).reshape(
        length, length
    )
    sin_full = (sin_outer[:, None] * cos_inner[None] + cos_outer[:, None] * sin_inner[None]).reshape(
        length, length
    )
    rows = lax.broadcasted_iota(jnp.int32, (length, length), 0)
    cols = lax.broadcasted_iota(jnp.int32, (length, length), 1)
    alternating = jnp.where(rows % 2 == 0, 1.0, -1.0).astype(jnp.float32)
    sin_part = jnp.where(cols == 0, alternating, -sin_full)
    table = jnp.concatenate([cos_full, sin_part], axis=1)
    return split_bf16(table)


def constant_dft_table(length):
    padded = 2 * length
    rows = np.arange(length, dtype=np.int64)[:, None]
    cols = np.arange(length, dtype=np.int64)[None, :]
    angle = ((rows * cols) % padded).astype(np.float64) * (2.0 * np.pi / padded)
    alternating = np.where(rows % 2 == 0, 1.0, -1.0)
    sin_part = np.where(cols == 0, alternating, -np.sin(angle))
    table = np.concatenate([np.cos(angle), sin_part], axis=1).astype(np.float32)
    high = table.astype(ml_dtypes.bfloat16)
    low = (table - high.astype(np.float32)).astype(ml_dtypes.bfloat16)
    return (jnp.asarray(high), jnp.asarray(low))


def dot_tf(table, signal):
    return lax.dot_general(
        table, signal, (((0,), (0,)), ((), ())), preferred_element_type=jnp.float32
    )


def dot_tt(table, spec):
    return lax.dot_general(
        table, spec, (((1,), (0,)), ((), ())), preferred_element_type=jnp.float32
    )


def dense_spectrum_exact(rows_bf16, table):
    table_hi, table_lo = table
    return dot_tf(table_hi, rows_bf16) + dot_tf(table_lo, rows_bf16)


def dense_signal(spec, table):
    table_hi, table_lo = table
    spec_hi, spec_lo = split_bf16(spec)
    return dot_tt(table_hi, spec_hi) + (dot_tt(table_lo, spec_hi) + dot_tt(table_hi, spec_lo))


def dense_taps_spectrum(taps, table):
    table_hi, table_lo = table
    taps_hi, taps_lo = split_bf16(taps)
    dims = (((0,), (1,)), ((), ()))
    part = lambda a, b: lax.dot_general(a, b, dims, preferred_element_type=jnp.float32)
    return part(table_hi, taps_hi) + (part(table_lo, taps_hi) + part(table_hi, taps_lo))


def spectral_weights(length):
    index = lax.broadcasted_iota(jnp.int32, (2 * length, 1), 0)
    edge = (index == 0) | (index == length)
    return jnp.where(edge, 1.0, 2.0).astype(jnp.float32) / (2 * length)


def dense_multiply(a, b, conjugate):
    length = a.shape[0] // 2
    a_re, a_im = a[:length], a[length:]
    b_re, b_im = b[:length], b[length:]
    first = lax.broadcasted_iota(jnp.int32, (length, 1), 0) == 0
    if conjugate:
        re = a_re * b_re + a_im * b_im
        im = a_im * b_re - a_re * b_im
    else:
        re = a_re * b_re - a_im * b_im
        im = a_re * b_im + a_im * b_re
    re = jnp.where(first, a_re * b_re, re)
    im = jnp.where(first, a_im * b_im, im)
    return jnp.concatenate([re, im], axis=0)


def dense_fits(length):
    return 4 * length * length * 2 <= 16 * 1024 * 1024


def on_device_factored(fwd_in, bwd_in, bwd_cot, filter_taps, norm_gain):
    model_width = norm_gain.shape[1] * lax.axis_size("tp")
    local_taps = filter_taps[0, 0]
    tables = dft_tables(2 * local_taps.shape[1])
    tap_re, tap_im = spectrum(local_taps, tables)
    gain_row = norm_gain[0]
    forward_rows = fwd_in[0]
    backward_rows = bwd_in[0]

    def featurize(proj_rows):
        return (proj_rows[:, 1].astype(jnp.float32) * proj_rows[:, 2].astype(jnp.float32)).astype(
            jnp.bfloat16
        )

    def convolve(columns):
        sig_re, sig_im = spectrum(columns.astype(jnp.float32), tables)
        prod_re, prod_im = spec_product(sig_re, sig_im, tap_re, tap_im)
        return (signal_of(prod_re, prod_im, tables).astype(jnp.bfloat16), (sig_re, sig_im))

    def relayout(mixed_rows):
        columns = lax.all_to_all(
            jnp.transpose(mixed_rows), "ctx", split_axis=0, concat_axis=1, tiled=True
        )
        result, kept_spec = convolve(columns)
        return (
            jnp.transpose(lax.all_to_all(result, "ctx", split_axis=1, concat_axis=0, tiled=True)),
            kept_spec,
        )

    def row_total(values):
        return lax.psum(jnp.sum(values, axis=1), "tp")

    forward_mix = featurize(forward_rows)
    backward_mix = featurize(backward_rows)
    forward_z = relayout(forward_mix)[0]
    backward_z, backward_spec = relayout(backward_mix)
    forward_y = forward_rows[:, 0].astype(jnp.float32) * forward_z.astype(jnp.float32)
    backward_q = backward_rows[:, 0].astype(jnp.float32)
    conv_value = backward_z.astype(jnp.float32)
    backward_y = backward_q * conv_value
    weighted = bwd_cot[0].astype(jnp.float32) * gain_row
    forward_scale = lax.rsqrt(row_total(forward_y * forward_y) / model_width + epsilon)[:, None]
    backward_scale = lax.rsqrt(row_total(backward_y * backward_y) / model_width + epsilon)[:, None]
    normed = backward_y * backward_scale
    average = (row_total(weighted * normed) / model_width)[:, None]
    forward_out = (forward_y * forward_scale * gain_row).astype(jnp.bfloat16)
    grad_y = backward_scale * (weighted - normed * average)
    grad_z = (grad_y * backward_q).astype(jnp.bfloat16)
    grad_cols = lax.all_to_all(
        jnp.transpose(grad_z), "ctx", split_axis=0, concat_axis=1, tiled=True
    )
    grad_re, grad_im = spectrum(grad_cols.astype(jnp.float32), tables)
    input_re, input_im = spec_against(grad_re, grad_im, tap_re, tap_im)
    grad_mix_cols = signal_of(input_re, input_im, tables).astype(jnp.bfloat16)
    taps_re, taps_im = spec_against(grad_re, grad_im, backward_spec[0], backward_spec[1])
    filt_step = signal_of(taps_re, taps_im, tables)
    grad_mix = jnp.transpose(
        lax.all_to_all(grad_mix_cols, "ctx", split_axis=1, concat_axis=0, tiled=True)
    ).astype(jnp.float32)
    section_grads = jnp.stack(
        [
            grad_y * conv_value,
            grad_mix * backward_rows[:, 2].astype(jnp.float32),
            grad_mix * backward_rows[:, 1].astype(jnp.float32),
        ],
        axis=1,
    ).astype(jnp.bfloat16)
    section_grads, filt_step = (section_grads, filt_step)
    sent_rows, sent_grads = from_partner((forward_out, section_grads), "pipe", 0)
    return (sent_rows[None], sent_grads[None], filt_step[None, None])


def on_device(fwd_in, bwd_in, bwd_cot, filter_taps, norm_gain):
    length = filter_taps.shape[3]
    if not dense_fits(length):
        return on_device_factored(fwd_in, bwd_in, bwd_cot, filter_taps, norm_gain)
    model_width = norm_gain.shape[1] * lax.axis_size("tp")
    table = constant_dft_table(length)
    weights = spectral_weights(length)
    tap_spec = dense_taps_spectrum(filter_taps[0, 0], table)
    tap_scaled = tap_spec * weights
    gain_row = norm_gain[0]
    forward_rows = fwd_in[0]
    backward_rows = bwd_in[0]

    def featurize(proj_rows):
        return (proj_rows[:, 1].astype(jnp.float32) * proj_rows[:, 2].astype(jnp.float32)).astype(
            jnp.bfloat16
        )

    def to_columns(rows):
        return lax.all_to_all(rows, "ctx", split_axis=1, concat_axis=0, tiled=True)

    def to_rows(columns):
        return lax.all_to_all(columns, "ctx", split_axis=0, concat_axis=1, tiled=True)

    def row_total(values):
        return lax.psum(jnp.sum(values, axis=1), "tp")

    partner_kv = from_partner(backward_rows[:, 1:3], "pipe", 0)
    forward_cols = to_columns(featurize(forward_rows))
    backward_cols = to_columns(featurize(backward_rows))
    forward_spec = dense_spectrum_exact(forward_cols, table)
    forward_z = to_rows(
        dense_signal(dense_multiply(forward_spec, tap_scaled, False), table).astype(jnp.bfloat16)
    )
    partner_kv, backward_cols = lax.optimization_barrier((partner_kv, backward_cols))
    backward_spec = dense_spectrum_exact(backward_cols, table)
    backward_z = to_rows(
        dense_signal(dense_multiply(backward_spec, tap_scaled, False), table).astype(jnp.bfloat16)
    )
    forward_y = forward_rows[:, 0].astype(jnp.float32) * forward_z.astype(jnp.float32)
    forward_scale = lax.rsqrt(row_total(forward_y * forward_y) / model_width + epsilon)[:, None]
    forward_out = (forward_y * forward_scale * gain_row).astype(jnp.bfloat16)
    sent_rows = from_partner(forward_out, "pipe", 0)
    backward_q = backward_rows[:, 0].astype(jnp.float32)
    conv_value = backward_z.astype(jnp.float32)
    backward_y = backward_q * conv_value
    weighted = bwd_cot[0].astype(jnp.float32) * gain_row
    backward_scale = lax.rsqrt(row_total(backward_y * backward_y) / model_width + epsilon)[:, None]
    normed = backward_y * backward_scale
    average = (row_total(weighted * normed) / model_width)[:, None]
    grad_y = backward_scale * (weighted - normed * average)
    grad_z = (grad_y * backward_q).astype(jnp.bfloat16)
    sent_first = from_partner((grad_y * conv_value).astype(jnp.bfloat16), "pipe", 0)
    grad_cols = to_columns(grad_z)
    grad_spec = dense_spectrum_exact(grad_cols, table) * weights
    mix_prod = dense_multiply(grad_spec, tap_spec, True)
    width = mix_prod.shape[1] // 2 if mix_prod.shape[1] % 256 == 0 else mix_prod.shape[1]
    pieces = mix_prod.shape[1] // width
    first_cols = dense_signal(mix_prod[:, :width], table).astype(jnp.bfloat16)
    sent_rows, sent_first, first_cols = lax.optimization_barrier((sent_rows, sent_first, first_cols))
    taps_prod = dense_multiply(grad_spec, backward_spec, True)
    taps_hi, taps_lo = split_bf16(taps_prod)
    table_hi, table_lo = table
    dims = (((0,), (1,)), ((), ()))
    part = lambda a, b: lax.dot_general(a, b, dims, preferred_element_type=jnp.float32)
    first_rows, filt_lead = lax.optimization_barrier((to_rows(first_cols), part(taps_hi, table_hi)))
    sent_parts = [from_partner(first_rows, "pipe", 0)]
    for piece in range(1, pieces):
        piece_cols = dense_signal(mix_prod[:, piece * width : (piece + 1) * width], table)
        piece_rows = to_rows(piece_cols.astype(jnp.bfloat16))
        sent_parts[-1], piece_rows = lax.optimization_barrier((sent_parts[-1], piece_rows))
        sent_parts.append(from_partner(piece_rows, "pipe", 0))
    filt_step = filt_lead + (part(taps_hi, table_lo) + part(taps_lo, table_hi))
    token_rows = sent_parts[0].shape[0]
    ctx_count = lax.axis_size("ctx")
    sent_mix = jnp.stack(
        [p.reshape(token_rows, ctx_count, width) for p in sent_parts], axis=2
    ).reshape(token_rows, -1).astype(jnp.float32)
    rest = jnp.stack(
        [
            sent_mix * partner_kv[:, 1].astype(jnp.float32),
            sent_mix * partner_kv[:, 0].astype(jnp.float32),
        ],
        axis=1,
    ).astype(jnp.bfloat16)
    sent_grads = jnp.concatenate([sent_first[:, None], rest], axis=1)
    return (sent_rows[None], sent_grads[None], filt_step[None, None])


def solution(mesh):
    return jax.shard_map(
        on_device,
        mesh=mesh,
        in_specs=(
            P("pipe", "ctx", None, "tp"),
            P("pipe", "ctx", None, "tp"),
            P("pipe", "ctx", "tp"),
            P("pipe", "tp", "ctx", None),
            P("pipe", "tp"),
        ),
        out_specs=(
            P("pipe", "ctx", "tp"),
            P("pipe", "ctx", None, "tp"),
            P("pipe", "tp", "ctx", None),
        ),
        check_vma=False,
    )
```

```python
import math

import jax
import ml_dtypes
import numpy as np
import jax.numpy as jnp
from jax import lax
from jax.sharding import PartitionSpec as P

epsilon = 1e-06
highest = lax.Precision.HIGHEST


def from_partner(block, axis, bit):
    count = lax.axis_size(axis)
    route = []
    for low in range(count):
        high = low | 1 << bit
        if high != low and high < count:
            route += [(low, high), (high, low)]
    return lax.ppermute(block, axis, route)


def unit_table(count_out, count_in, period):
    product = lax.broadcasted_iota(jnp.int32, (count_out, count_in), 0) * lax.broadcasted_iota(
        jnp.int32, (count_out, count_in), 1
    )
    phase_angle = (product % period).astype(jnp.float32) * (-2.0 * math.pi / period)
    return (jnp.cos(phase_angle), jnp.sin(phase_angle))


def dft_tables(padded):
    blocks = padded // 128
    cos_high, sin_high = unit_table(blocks, blocks, blocks)
    cos_low, sin_low = unit_table(128, 128, 128)
    cos_twist, sin_twist = unit_table(blocks, 128, padded)
    return (cos_high, sin_high, cos_low, sin_low, cos_twist, sin_twist)


def spectrum(signal, tables):
    cos_high, sin_high, cos_low, sin_low, cos_twist, sin_twist = tables
    channels = signal.shape[0]
    half_blocks = signal.shape[1] // 128
    folded = signal.reshape(channels, half_blocks, 128)
    first_re = jnp.einsum("can,ak->ckn", folded, cos_high[:half_blocks], precision=highest)
    first_im = jnp.einsum("can,ak->ckn", folded, sin_high[:half_blocks], precision=highest)
    turned_re = first_re * cos_twist - first_im * sin_twist
    turned_im = first_re * sin_twist + first_im * cos_twist
    spec_re = jnp.einsum("ckn,nj->ckj", turned_re, cos_low, precision=highest) - jnp.einsum(
        "ckn,nj->ckj", turned_im, sin_low, precision=highest
    )
    spec_im = jnp.einsum("ckn,nj->ckj", turned_re, sin_low, precision=highest) + jnp.einsum(
        "ckn,nj->ckj", turned_im, cos_low, precision=highest
    )
    return (spec_re, spec_im)


def signal_of(spec_re, spec_im, tables):
    cos_high, sin_high, cos_low, sin_low, cos_twist, sin_twist = tables
    channels = spec_re.shape[0]
    blocks = spec_re.shape[1]
    half_blocks = blocks // 2
    mid_re = jnp.einsum("ckj,jn->ckn", spec_re, cos_low, precision=highest) + jnp.einsum(
        "ckj,jn->ckn", spec_im, sin_low, precision=highest
    )
    mid_im = jnp.einsum("ckj,jn->ckn", spec_im, cos_low, precision=highest) - jnp.einsum(
        "ckj,jn->ckn", spec_re, sin_low, precision=highest
    )
    back_re = mid_re * cos_twist + mid_im * sin_twist
    back_im = mid_im * cos_twist - mid_re * sin_twist
    values = jnp.einsum(
        "ak,ckn->can", cos_high[:half_blocks], back_re, precision=highest
    ) + jnp.einsum("ak,ckn->can", sin_high[:half_blocks], back_im, precision=highest)
    return values.reshape(channels, half_blocks * 128) / (blocks * 128)


def spec_product(a_re, a_im, b_re, b_im):
    return (a_re * b_re - a_im * b_im, a_re * b_im + a_im * b_re)


def spec_against(a_re, a_im, b_re, b_im):
    return (a_re * b_re + a_im * b_im, a_im * b_re - a_re * b_im)


def split_bf16(values):
    high = lax.reduce_precision(values, exponent_bits=8, mantissa_bits=7)
    return (high.astype(jnp.bfloat16), (values - high).astype(jnp.bfloat16))


def unit_angles(count_rows, count_cols, stride, padded):
    rows = lax.broadcasted_iota(jnp.int32, (count_rows, count_cols), 0) * stride
    cols = lax.broadcasted_iota(jnp.int32, (count_rows, count_cols), 1)
    angle = ((rows * cols) % padded).astype(jnp.float32) * (2.0 * math.pi / padded)
    return (jnp.cos(angle), jnp.sin(angle))


def real_dft_table(length):
    padded = 2 * length
    inner = 1 << (length.bit_length() // 2)
    if length % inner:
        inner = 1
    outer = length // inner
    cos_outer, sin_outer = unit_angles(outer, length, inner, padded)
    cos_inner, sin_inner = unit_angles(inner, length, 1, padded)
    cos_full = (cos_outer[:, None] * cos_inner[None] - sin_outer[:, None] * sin_inner[None]).reshape(
        length, length
    )
    sin_full = (sin_outer[:, None] * cos_inner[None] + cos_outer[:, None] * sin_inner[None]).reshape(
        length, length
    )
    rows = lax.broadcasted_iota(jnp.int32, (length, length), 0)
    cols = lax.broadcasted_iota(jnp.int32, (length, length), 1)
    alternating = jnp.where(rows % 2 == 0, 1.0, -1.0).astype(jnp.float32)
    sin_part = jnp.where(cols == 0, alternating, -sin_full)
    table = jnp.concatenate([cos_full, sin_part], axis=1)
    return split_bf16(table)


def constant_dft_table(length):
    padded = 2 * length
    rows = np.arange(length, dtype=np.int64)[:, None]
    cols = np.arange(length, dtype=np.int64)[None, :]
    angle = ((rows * cols) % padded).astype(np.float64) * (2.0 * np.pi / padded)
    alternating = np.where(rows % 2 == 0, 1.0, -1.0)
    sin_part = np.where(cols == 0, alternating, -np.sin(angle))
    table = np.concatenate([np.cos(angle), sin_part], axis=1).astype(np.float32)
    high = table.astype(ml_dtypes.bfloat16)
    low = (table - high.astype(np.float32)).astype(ml_dtypes.bfloat16)
    return (jnp.asarray(high), jnp.asarray(low))


def dot_tf(table, signal):
    return lax.dot_general(
        table, signal, (((0,), (0,)), ((), ())), preferred_element_type=jnp.float32
    )


def dot_tt(table, spec):
    return lax.dot_general(
        table, spec, (((1,), (0,)), ((), ())), preferred_element_type=jnp.float32
    )


def dense_spectrum_exact(rows_bf16, table):
    table_hi, table_lo = table
    return dot_tf(table_hi, rows_bf16) + dot_tf(table_lo, rows_bf16)


def dense_signal(spec, table):
    table_hi, table_lo = table
    spec_hi, spec_lo = split_bf16(spec)
    return dot_tt(table_hi, spec_hi) + (dot_tt(table_lo, spec_hi) + dot_tt(table_hi, spec_lo))


def dense_taps_spectrum(taps, table):
    table_hi, table_lo = table
    taps_hi, taps_lo = split_bf16(taps)
    dims = (((0,), (1,)), ((), ()))
    part = lambda a, b: lax.dot_general(a, b, dims, preferred_element_type=jnp.float32)
    return part(table_hi, taps_hi) + (part(table_lo, taps_hi) + part(table_hi, taps_lo))


def spectral_weights(length):
    index = lax.broadcasted_iota(jnp.int32, (2 * length, 1), 0)
    edge = (index == 0) | (index == length)
    return jnp.where(edge, 1.0, 2.0).astype(jnp.float32) / (2 * length)


def dense_multiply(a, b, conjugate):
    length = a.shape[0] // 2
    a_re, a_im = a[:length], a[length:]
    b_re, b_im = b[:length], b[length:]
    first = lax.broadcasted_iota(jnp.int32, (length, 1), 0) == 0
    if conjugate:
        re = a_re * b_re + a_im * b_im
        im = a_im * b_re - a_re * b_im
    else:
        re = a_re * b_re - a_im * b_im
        im = a_re * b_im + a_im * b_re
    re = jnp.where(first, a_re * b_re, re)
    im = jnp.where(first, a_im * b_im, im)
    return jnp.concatenate([re, im], axis=0)


def dense_fits(length):
    return 4 * length * length * 2 <= 16 * 1024 * 1024


def on_device_factored(fwd_in, bwd_in, bwd_cot, filter_taps, norm_gain):
    model_width = norm_gain.shape[1] * lax.axis_size("tp")
    local_taps = filter_taps[0, 0]
    tables = dft_tables(2 * local_taps.shape[1])
    tap_re, tap_im = spectrum(local_taps, tables)
    gain_row = norm_gain[0]
    forward_rows = fwd_in[0]
    backward_rows = bwd_in[0]

    def featurize(proj_rows):
        return (proj_rows[:, 1].astype(jnp.float32) * proj_rows[:, 2].astype(jnp.float32)).astype(
            jnp.bfloat16
        )

    def convolve(columns):
        sig_re, sig_im = spectrum(columns.astype(jnp.float32), tables)
        prod_re, prod_im = spec_product(sig_re, sig_im, tap_re, tap_im)
        return (signal_of(prod_re, prod_im, tables).astype(jnp.bfloat16), (sig_re, sig_im))

    def relayout(mixed_rows):
        columns = lax.all_to_all(
            jnp.transpose(mixed_rows), "ctx", split_axis=0, concat_axis=1, tiled=True
        )
        result, kept_spec = convolve(columns)
        return (
            jnp.transpose(lax.all_to_all(result, "ctx", split_axis=1, concat_axis=0, tiled=True)),
            kept_spec,
        )

    def row_total(values):
        return lax.psum(jnp.sum(values, axis=1), "tp")

    forward_mix = featurize(forward_rows)
    backward_mix = featurize(backward_rows)
    forward_z = relayout(forward_mix)[0]
    backward_z, backward_spec = relayout(backward_mix)
    forward_y = forward_rows[:, 0].astype(jnp.float32) * forward_z.astype(jnp.float32)
    backward_q = backward_rows[:, 0].astype(jnp.float32)
    conv_value = backward_z.astype(jnp.float32)
    backward_y = backward_q * conv_value
    weighted = bwd_cot[0].astype(jnp.float32) * gain_row
    forward_scale = lax.rsqrt(row_total(forward_y * forward_y) / model_width + epsilon)[:, None]
    backward_scale = lax.rsqrt(row_total(backward_y * backward_y) / model_width + epsilon)[:, None]
    normed = backward_y * backward_scale
    average = (row_total(weighted * normed) / model_width)[:, None]
    forward_out = (forward_y * forward_scale * gain_row).astype(jnp.bfloat16)
    grad_y = backward_scale * (weighted - normed * average)
    grad_z = (grad_y * backward_q).astype(jnp.bfloat16)
    grad_cols = lax.all_to_all(
        jnp.transpose(grad_z), "ctx", split_axis=0, concat_axis=1, tiled=True
    )
    grad_re, grad_im = spectrum(grad_cols.astype(jnp.float32), tables)
    input_re, input_im = spec_against(grad_re, grad_im, tap_re, tap_im)
    grad_mix_cols = signal_of(input_re, input_im, tables).astype(jnp.bfloat16)
    taps_re, taps_im = spec_against(grad_re, grad_im, backward_spec[0], backward_spec[1])
    filt_step = signal_of(taps_re, taps_im, tables)
    grad_mix = jnp.transpose(
        lax.all_to_all(grad_mix_cols, "ctx", split_axis=1, concat_axis=0, tiled=True)
    ).astype(jnp.float32)
    section_grads = jnp.stack(
        [
            grad_y * conv_value,
            grad_mix * backward_rows[:, 2].astype(jnp.float32),
            grad_mix * backward_rows[:, 1].astype(jnp.float32),
        ],
        axis=1,
    ).astype(jnp.bfloat16)
    section_grads, filt_step = (section_grads, filt_step)
    sent_rows, sent_grads = from_partner((forward_out, section_grads), "pipe", 0)
    return (sent_rows[None], sent_grads[None], filt_step[None, None])


def on_device(fwd_in, bwd_in, bwd_cot, filter_taps, norm_gain):
    length = filter_taps.shape[3]
    if not dense_fits(length):
        return on_device_factored(fwd_in, bwd_in, bwd_cot, filter_taps, norm_gain)
    model_width = norm_gain.shape[1] * lax.axis_size("tp")
    table = constant_dft_table(length)
    weights = spectral_weights(length)
    tap_spec = dense_taps_spectrum(filter_taps[0, 0], table)
    tap_scaled = tap_spec * weights
    gain_row = norm_gain[0]
    forward_rows = fwd_in[0]
    backward_rows = bwd_in[0]

    def featurize(proj_rows):
        return (proj_rows[:, 1].astype(jnp.float32) * proj_rows[:, 2].astype(jnp.float32)).astype(
            jnp.bfloat16
        )

    def to_columns(rows):
        return lax.all_to_all(rows, "ctx", split_axis=1, concat_axis=0, tiled=True)

    def to_rows(columns):
        return lax.all_to_all(columns, "ctx", split_axis=0, concat_axis=1, tiled=True)

    def row_total(values):
        return lax.psum(jnp.sum(values, axis=1), "tp")

    partner_kv = from_partner(backward_rows[:, 1:3], "pipe", 0)
    forward_cols = to_columns(featurize(forward_rows))
    backward_cols = to_columns(featurize(backward_rows))
    forward_spec = dense_spectrum_exact(forward_cols, table)
    forward_z = to_rows(
        dense_signal(dense_multiply(forward_spec, tap_scaled, False), table).astype(jnp.bfloat16)
    )
    partner_kv, backward_cols = lax.optimization_barrier((partner_kv, backward_cols))
    backward_spec = dense_spectrum_exact(backward_cols, table)
    backward_z = to_rows(
        dense_signal(dense_multiply(backward_spec, tap_scaled, False), table).astype(jnp.bfloat16)
    )
    forward_y = forward_rows[:, 0].astype(jnp.float32) * forward_z.astype(jnp.float32)
    forward_scale = lax.rsqrt(row_total(forward_y * forward_y) / model_width + epsilon)[:, None]
    forward_out = (forward_y * forward_scale * gain_row).astype(jnp.bfloat16)
    sent_rows = from_partner(forward_out, "pipe", 0)
    backward_q = backward_rows[:, 0].astype(jnp.float32)
    conv_value = backward_z.astype(jnp.float32)
    backward_y = backward_q * conv_value
    weighted = bwd_cot[0].astype(jnp.float32) * gain_row
    backward_scale = lax.rsqrt(row_total(backward_y * backward_y) / model_width + epsilon)[:, None]
    normed = backward_y * backward_scale
    average = (row_total(weighted * normed) / model_width)[:, None]
    grad_y = backward_scale * (weighted - normed * average)
    grad_z = (grad_y * backward_q).astype(jnp.bfloat16)
    sent_first = from_partner((grad_y * conv_value).astype(jnp.bfloat16), "pipe", 0)
    grad_cols = to_columns(grad_z)
    grad_spec = dense_spectrum_exact(grad_cols, table) * weights
    mix_prod = dense_multiply(grad_spec, tap_spec, True)
    width = mix_prod.shape[1] // 2 if mix_prod.shape[1] % 256 == 0 else mix_prod.shape[1]
    pieces = mix_prod.shape[1] // width
    first_cols = dense_signal(mix_prod[:, :width], table).astype(jnp.bfloat16)

    sent_parts = [from_partner(to_rows(first_cols), "pipe", 0)]
    for piece in range(1, pieces):
        piece_cols = dense_signal(mix_prod[:, piece * width : (piece + 1) * width], table)
        piece_rows = to_rows(piece_cols.astype(jnp.bfloat16))
        sent_parts[-1], sent_rows, sent_first, piece_rows = lax.optimization_barrier(
            (sent_parts[-1], sent_rows, sent_first, piece_rows)
        )
        sent_parts.append(from_partner(piece_rows, "pipe", 0))
    taps_prod = dense_multiply(grad_spec, backward_spec, True)
    taps_hi, taps_lo = split_bf16(taps_prod)
    table_hi, table_lo = table
    dims = (((0,), (1,)), ((), ()))
    part = lambda a, b: lax.dot_general(a, b, dims, preferred_element_type=jnp.float32)
    filt_step = part(taps_hi, table_hi) + (part(taps_hi, table_lo) + part(taps_lo, table_hi))
    token_rows = sent_parts[0].shape[0]
    ctx_count = lax.axis_size("ctx")
    sent_mix = jnp.stack(
        [p.reshape(token_rows, ctx_count, width) for p in sent_parts], axis=2
    ).reshape(token_rows, -1).astype(jnp.float32)
    rest = jnp.stack(
        [
            sent_mix * partner_kv[:, 1].astype(jnp.float32),
            sent_mix * partner_kv[:, 0].astype(jnp.float32),
        ],
        axis=1,
    ).astype(jnp.bfloat16)
    sent_grads = jnp.concatenate([sent_first[:, None], rest], axis=1)
    return (sent_rows[None], sent_grads[None], filt_step[None, None])


def solution(mesh):
    return jax.shard_map(
        on_device,
        mesh=mesh,
        in_specs=(
            P("pipe", "ctx", None, "tp"),
            P("pipe", "ctx", None, "tp"),
            P("pipe", "ctx", "tp"),
            P("pipe", "tp", "ctx", None),
            P("pipe", "tp"),
        ),
        out_specs=(
            P("pipe", "ctx", "tp"),
            P("pipe", "ctx", None, "tp"),
            P("pipe", "tp", "ctx", None),
        ),
        check_vma=False,
    )
```

```python
import math

import jax
import ml_dtypes
import numpy as np
import jax.numpy as jnp
from jax import lax
from jax.sharding import PartitionSpec as P

epsilon = 1e-06
highest = lax.Precision.HIGHEST


def from_partner(block, axis, bit):
    count = lax.axis_size(axis)
    route = []
    for low in range(count):
        high = low | 1 << bit
        if high != low and high < count:
            route += [(low, high), (high, low)]
    return lax.ppermute(block, axis, route)


def unit_table(count_out, count_in, period):
    product = lax.broadcasted_iota(jnp.int32, (count_out, count_in), 0) * lax.broadcasted_iota(
        jnp.int32, (count_out, count_in), 1
    )
    phase_angle = (product % period).astype(jnp.float32) * (-2.0 * math.pi / period)
    return (jnp.cos(phase_angle), jnp.sin(phase_angle))


def dft_tables(padded):
    blocks = padded // 128
    cos_high, sin_high = unit_table(blocks, blocks, blocks)
    cos_low, sin_low = unit_table(128, 128, 128)
    cos_twist, sin_twist = unit_table(blocks, 128, padded)
    return (cos_high, sin_high, cos_low, sin_low, cos_twist, sin_twist)


def spectrum(signal, tables):
    cos_high, sin_high, cos_low, sin_low, cos_twist, sin_twist = tables
    channels = signal.shape[0]
    half_blocks = signal.shape[1] // 128
    folded = signal.reshape(channels, half_blocks, 128)
    first_re = jnp.einsum("can,ak->ckn", folded, cos_high[:half_blocks], precision=highest)
    first_im = jnp.einsum("can,ak->ckn", folded, sin_high[:half_blocks], precision=highest)
    turned_re = first_re * cos_twist - first_im * sin_twist
    turned_im = first_re * sin_twist + first_im * cos_twist
    spec_re = jnp.einsum("ckn,nj->ckj", turned_re, cos_low, precision=highest) - jnp.einsum(
        "ckn,nj->ckj", turned_im, sin_low, precision=highest
    )
    spec_im = jnp.einsum("ckn,nj->ckj", turned_re, sin_low, precision=highest) + jnp.einsum(
        "ckn,nj->ckj", turned_im, cos_low, precision=highest
    )
    return (spec_re, spec_im)


def signal_of(spec_re, spec_im, tables):
    cos_high, sin_high, cos_low, sin_low, cos_twist, sin_twist = tables
    channels = spec_re.shape[0]
    blocks = spec_re.shape[1]
    half_blocks = blocks // 2
    mid_re = jnp.einsum("ckj,jn->ckn", spec_re, cos_low, precision=highest) + jnp.einsum(
        "ckj,jn->ckn", spec_im, sin_low, precision=highest
    )
    mid_im = jnp.einsum("ckj,jn->ckn", spec_im, cos_low, precision=highest) - jnp.einsum(
        "ckj,jn->ckn", spec_re, sin_low, precision=highest
    )
    back_re = mid_re * cos_twist + mid_im * sin_twist
    back_im = mid_im * cos_twist - mid_re * sin_twist
    values = jnp.einsum(
        "ak,ckn->can", cos_high[:half_blocks], back_re, precision=highest
    ) + jnp.einsum("ak,ckn->can", sin_high[:half_blocks], back_im, precision=highest)
    return values.reshape(channels, half_blocks * 128) / (blocks * 128)


def spec_product(a_re, a_im, b_re, b_im):
    return (a_re * b_re - a_im * b_im, a_re * b_im + a_im * b_re)


def spec_against(a_re, a_im, b_re, b_im):
    return (a_re * b_re + a_im * b_im, a_im * b_re - a_re * b_im)


def split_bf16(values):
    high = lax.reduce_precision(values, exponent_bits=8, mantissa_bits=7)
    return (high.astype(jnp.bfloat16), (values - high).astype(jnp.bfloat16))


def unit_angles(count_rows, count_cols, stride, padded):
    rows = lax.broadcasted_iota(jnp.int32, (count_rows, count_cols), 0) * stride
    cols = lax.broadcasted_iota(jnp.int32, (count_rows, count_cols), 1)
    angle = ((rows * cols) % padded).astype(jnp.float32) * (2.0 * math.pi / padded)
    return (jnp.cos(angle), jnp.sin(angle))


def real_dft_table(length):
    padded = 2 * length
    inner = 1 << (length.bit_length() // 2)
    if length % inner:
        inner = 1
    outer = length // inner
    cos_outer, sin_outer = unit_angles(outer, length, inner, padded)
    cos_inner, sin_inner = unit_angles(inner, length, 1, padded)
    cos_full = (cos_outer[:, None] * cos_inner[None] - sin_outer[:, None] * sin_inner[None]).reshape(
        length, length
    )
    sin_full = (sin_outer[:, None] * cos_inner[None] + cos_outer[:, None] * sin_inner[None]).reshape(
        length, length
    )
    rows = lax.broadcasted_iota(jnp.int32, (length, length), 0)
    cols = lax.broadcasted_iota(jnp.int32, (length, length), 1)
    alternating = jnp.where(rows % 2 == 0, 1.0, -1.0).astype(jnp.float32)
    sin_part = jnp.where(cols == 0, alternating, -sin_full)
    table = jnp.concatenate([cos_full, sin_part], axis=1)
    return split_bf16(table)


def constant_dft_table(length):
    padded = 2 * length
    rows = np.arange(length, dtype=np.int64)[:, None]
    cols = np.arange(length, dtype=np.int64)[None, :]
    angle = ((rows * cols) % padded).astype(np.float64) * (2.0 * np.pi / padded)
    alternating = np.where(rows % 2 == 0, 1.0, -1.0)
    sin_part = np.where(cols == 0, alternating, -np.sin(angle))
    table = np.concatenate([np.cos(angle), sin_part], axis=1).astype(np.float32)
    high = table.astype(ml_dtypes.bfloat16)
    low = (table - high.astype(np.float32)).astype(ml_dtypes.bfloat16)
    return (jnp.asarray(high), jnp.asarray(low))


def dot_tf(table, signal):
    return lax.dot_general(
        table, signal, (((0,), (0,)), ((), ())), preferred_element_type=jnp.float32
    )


def dot_tt(table, spec):
    return lax.dot_general(
        table, spec, (((1,), (0,)), ((), ())), preferred_element_type=jnp.float32
    )


def dense_spectrum_exact(rows_bf16, table):
    table_hi, table_lo = table
    return dot_tf(table_hi, rows_bf16) + dot_tf(table_lo, rows_bf16)


def dense_signal(spec, table):
    table_hi, table_lo = table
    spec_hi, spec_lo = split_bf16(spec)
    return dot_tt(table_hi, spec_hi) + (dot_tt(table_lo, spec_hi) + dot_tt(table_hi, spec_lo))


def dense_taps_spectrum(taps, table):
    table_hi, table_lo = table
    taps_hi, taps_lo = split_bf16(taps)
    dims = (((0,), (1,)), ((), ()))
    part = lambda a, b: lax.dot_general(a, b, dims, preferred_element_type=jnp.float32)
    return part(table_hi, taps_hi) + (part(table_lo, taps_hi) + part(table_hi, taps_lo))


def spectral_weights(length):
    index = lax.broadcasted_iota(jnp.int32, (2 * length, 1), 0)
    edge = (index == 0) | (index == length)
    return jnp.where(edge, 1.0, 2.0).astype(jnp.float32) / (2 * length)


def dense_multiply(a, b, conjugate):
    length = a.shape[0] // 2
    a_re, a_im = a[:length], a[length:]
    b_re, b_im = b[:length], b[length:]
    first = lax.broadcasted_iota(jnp.int32, (length, 1), 0) == 0
    if conjugate:
        re = a_re * b_re + a_im * b_im
        im = a_im * b_re - a_re * b_im
    else:
        re = a_re * b_re - a_im * b_im
        im = a_re * b_im + a_im * b_re
    re = jnp.where(first, a_re * b_re, re)
    im = jnp.where(first, a_im * b_im, im)
    return jnp.concatenate([re, im], axis=0)


def dense_fits(length):
    return 4 * length * length * 2 <= 16 * 1024 * 1024


def on_device_factored(fwd_in, bwd_in, bwd_cot, filter_taps, norm_gain):
    model_width = norm_gain.shape[1] * lax.axis_size("tp")
    local_taps = filter_taps[0, 0]
    tables = dft_tables(2 * local_taps.shape[1])
    tap_re, tap_im = spectrum(local_taps, tables)
    gain_row = norm_gain[0]
    forward_rows = fwd_in[0]
    backward_rows = bwd_in[0]

    def featurize(proj_rows):
        return (proj_rows[:, 1].astype(jnp.float32) * proj_rows[:, 2].astype(jnp.float32)).astype(
            jnp.bfloat16
        )

    def convolve(columns):
        sig_re, sig_im = spectrum(columns.astype(jnp.float32), tables)
        prod_re, prod_im = spec_product(sig_re, sig_im, tap_re, tap_im)
        return (signal_of(prod_re, prod_im, tables).astype(jnp.bfloat16), (sig_re, sig_im))

    def relayout(mixed_rows):
        columns = lax.all_to_all(
            jnp.transpose(mixed_rows), "ctx", split_axis=0, concat_axis=1, tiled=True
        )
        result, kept_spec = convolve(columns)
        return (
            jnp.transpose(lax.all_to_all(result, "ctx", split_axis=1, concat_axis=0, tiled=True)),
            kept_spec,
        )

    def row_total(values):
        return lax.psum(jnp.sum(values, axis=1), "tp")

    forward_mix = featurize(forward_rows)
    backward_mix = featurize(backward_rows)
    forward_z = relayout(forward_mix)[0]
    backward_z, backward_spec = relayout(backward_mix)
    forward_y = forward_rows[:, 0].astype(jnp.float32) * forward_z.astype(jnp.float32)
    backward_q = backward_rows[:, 0].astype(jnp.float32)
    conv_value = backward_z.astype(jnp.float32)
    backward_y = backward_q * conv_value
    weighted = bwd_cot[0].astype(jnp.float32) * gain_row
    forward_scale = lax.rsqrt(row_total(forward_y * forward_y) / model_width + epsilon)[:, None]
    backward_scale = lax.rsqrt(row_total(backward_y * backward_y) / model_width + epsilon)[:, None]
    normed = backward_y * backward_scale
    average = (row_total(weighted * normed) / model_width)[:, None]
    forward_out = (forward_y * forward_scale * gain_row).astype(jnp.bfloat16)
    grad_y = backward_scale * (weighted - normed * average)
    grad_z = (grad_y * backward_q).astype(jnp.bfloat16)
    grad_cols = lax.all_to_all(
        jnp.transpose(grad_z), "ctx", split_axis=0, concat_axis=1, tiled=True
    )
    grad_re, grad_im = spectrum(grad_cols.astype(jnp.float32), tables)
    input_re, input_im = spec_against(grad_re, grad_im, tap_re, tap_im)
    grad_mix_cols = signal_of(input_re, input_im, tables).astype(jnp.bfloat16)
    taps_re, taps_im = spec_against(grad_re, grad_im, backward_spec[0], backward_spec[1])
    filt_step = signal_of(taps_re, taps_im, tables)
    grad_mix = jnp.transpose(
        lax.all_to_all(grad_mix_cols, "ctx", split_axis=1, concat_axis=0, tiled=True)
    ).astype(jnp.float32)
    section_grads = jnp.stack(
        [
            grad_y * conv_value,
            grad_mix * backward_rows[:, 2].astype(jnp.float32),
            grad_mix * backward_rows[:, 1].astype(jnp.float32),
        ],
        axis=1,
    ).astype(jnp.bfloat16)
    section_grads, filt_step = (section_grads, filt_step)
    sent_rows, sent_grads = from_partner((forward_out, section_grads), "pipe", 0)
    return (sent_rows[None], sent_grads[None], filt_step[None, None])


def on_device(fwd_in, bwd_in, bwd_cot, filter_taps, norm_gain):
    length = filter_taps.shape[3]
    if not dense_fits(length):
        return on_device_factored(fwd_in, bwd_in, bwd_cot, filter_taps, norm_gain)
    model_width = norm_gain.shape[1] * lax.axis_size("tp")
    table = constant_dft_table(length)
    weights = spectral_weights(length)
    tap_spec = dense_taps_spectrum(filter_taps[0, 0], table)
    tap_scaled = tap_spec * weights
    gain_row = norm_gain[0]
    forward_rows = fwd_in[0]
    backward_rows = bwd_in[0]

    def featurize(proj_rows):
        return (proj_rows[:, 1].astype(jnp.float32) * proj_rows[:, 2].astype(jnp.float32)).astype(
            jnp.bfloat16
        )

    def to_columns(rows):
        return lax.all_to_all(rows, "ctx", split_axis=1, concat_axis=0, tiled=True)

    def to_rows(columns):
        return lax.all_to_all(columns, "ctx", split_axis=0, concat_axis=1, tiled=True)

    def row_total(values):
        return lax.psum(jnp.sum(values, axis=1), "tp")

    partner_kv = from_partner(backward_rows[:, 1:3], "pipe", 0)
    forward_cols = to_columns(featurize(forward_rows))
    backward_cols = to_columns(featurize(backward_rows))
    forward_spec = dense_spectrum_exact(forward_cols, table)
    forward_z = to_rows(
        dense_signal(dense_multiply(forward_spec, tap_scaled, False), table).astype(jnp.bfloat16)
    )
    partner_kv, backward_cols = lax.optimization_barrier((partner_kv, backward_cols))
    backward_spec = dense_spectrum_exact(backward_cols, table)
    backward_z = to_rows(
        dense_signal(dense_multiply(backward_spec, tap_scaled, False), table).astype(jnp.bfloat16)
    )
    forward_y = forward_rows[:, 0].astype(jnp.float32) * forward_z.astype(jnp.float32)
    forward_scale = lax.rsqrt(row_total(forward_y * forward_y) / model_width + epsilon)[:, None]
    forward_out = (forward_y * forward_scale * gain_row).astype(jnp.bfloat16)
    sent_rows = from_partner(forward_out, "pipe", 0)
    backward_q = backward_rows[:, 0].astype(jnp.float32)
    conv_value = backward_z.astype(jnp.float32)
    backward_y = backward_q * conv_value
    weighted = bwd_cot[0].astype(jnp.float32) * gain_row
    backward_scale = lax.rsqrt(row_total(backward_y * backward_y) / model_width + epsilon)[:, None]
    normed = backward_y * backward_scale
    average = (row_total(weighted * normed) / model_width)[:, None]
    grad_y = backward_scale * (weighted - normed * average)
    grad_z = (grad_y * backward_q).astype(jnp.bfloat16)
    sent_first = from_partner((grad_y * conv_value).astype(jnp.bfloat16), "pipe", 0)
    grad_cols = to_columns(grad_z)
    grad_spec = dense_spectrum_exact(grad_cols, table) * weights
    mix_prod = dense_multiply(grad_spec, tap_spec, True)
    width = mix_prod.shape[1] // 2 if mix_prod.shape[1] % 256 == 0 else mix_prod.shape[1]
    pieces = mix_prod.shape[1] // width
    first_cols = dense_signal(mix_prod[:, :width], table).astype(jnp.bfloat16)

    sent_rows, first_cols = lax.optimization_barrier((sent_rows, first_cols))
    sent_parts = [from_partner(to_rows(first_cols), "pipe", 0)]
    for piece in range(1, pieces):
        piece_cols = dense_signal(mix_prod[:, piece * width : (piece + 1) * width], table)
        piece_rows = to_rows(piece_cols.astype(jnp.bfloat16))
        sent_parts[-1], sent_first, piece_rows = lax.optimization_barrier(
            (sent_parts[-1], sent_first, piece_rows)
        )
        sent_parts.append(from_partner(piece_rows, "pipe", 0))
    taps_prod = dense_multiply(grad_spec, backward_spec, True)
    taps_hi, taps_lo = split_bf16(taps_prod)
    table_hi, table_lo = table
    dims = (((0,), (1,)), ((), ()))
    part = lambda a, b: lax.dot_general(a, b, dims, preferred_element_type=jnp.float32)
    filt_step = part(taps_hi, table_hi) + (part(taps_hi, table_lo) + part(taps_lo, table_hi))
    token_rows = sent_parts[0].shape[0]
    ctx_count = lax.axis_size("ctx")
    sent_mix = jnp.stack(
        [p.reshape(token_rows, ctx_count, width) for p in sent_parts], axis=2
    ).reshape(token_rows, -1).astype(jnp.float32)
    rest = jnp.stack(
        [
            sent_mix * partner_kv[:, 1].astype(jnp.float32),
            sent_mix * partner_kv[:, 0].astype(jnp.float32),
        ],
        axis=1,
    ).astype(jnp.bfloat16)
    sent_grads = jnp.concatenate([sent_first[:, None], rest], axis=1)
    return (sent_rows[None], sent_grads[None], filt_step[None, None])


def solution(mesh):
    return jax.shard_map(
        on_device,
        mesh=mesh,
        in_specs=(
            P("pipe", "ctx", None, "tp"),
            P("pipe", "ctx", None, "tp"),
            P("pipe", "ctx", "tp"),
            P("pipe", "tp", "ctx", None),
            P("pipe", "tp"),
        ),
        out_specs=(
            P("pipe", "ctx", "tp"),
            P("pipe", "ctx", None, "tp"),
            P("pipe", "tp", "ctx", None),
        ),
        check_vma=False,
    )
```
